32 devices in a mesh: gx: 8 (over z, x), gy: 4 (over y, core).
Axes of the slice: x: 2, y: 2, z: 4, core: 2. Of those that a mesh axis runs over, the one named last changes fastest.
Arguments:
- solution: float32 [4, 16, 5120], P(None, 'gx', 'gy'), may hold values from -0.12 to 0.12
- forcing: float32 [4, 16, 5120], P(None, 'gx', 'gy'), may hold values from -0.12 to 0.12
- viscosity: float32 [16, 5120], P('gx', 'gy'), may hold values from 0.3 to 1
- blocks: float32 [16, 16, 5120], P(None, 'gx', 'gy'), may hold values from -0.5 to 0.5, as said below
- layer_count: int32 [16, 64], P('gx', 'gy'), may hold values from 40 to 80
- bed_frozen: int32 [16, 64], P('gx', 'gy'), may hold values 0 or 1
- basin_map: int32 [16, 64], P('gx', 'gy'), may hold values from 0 to 15, as said below
Outputs:
- smoothed: float32 [4, 16, 5120], P(None, 'gx', 'gy')
- column_residual: float32 [4, 16, 64], P(None, 'gx', 'gy')
- basin_residual: float32 [4, 16], replicated
The draws below stay inside these ranges and needn't reach their ends.
Inputs may be any that keep to these rules, and one draw needn't show every extreme that they name: `blocks`: the first three diagonal entries of every cell's block are positive. `basin_map`: every basin number names some column.
All inputs are finite; a program needn't handle non-finite values. No bound on the sum of `bed_frozen` on one device may be relied on, other than what follows from the above.
Results may differ from the reference program's by a relative error of at most 0.00045.
Values sent between devices are 32-bit elements; how exact they have to be, the bound alone decides.
No kernel may reach another device: no remote copies, remote signals or barrier semaphores. Data moves between devices by JAX's collectives and lax.ppermute only.
A program may use at most 64 MiB of HBM per device.

```python
import math
import jax
import jax.numpy as jnp
from jax import lax

CX = 2
CY = 16
LAYERS = 80
NX = 16
NY = 64
NBASIN = 16


def viscosity_field(key):
    uniform_part = jax.random.uniform(jax.random.fold_in(key, 7), (NX, NY * LAYERS), jnp.float32)
    return jnp.exp(math.log(0.3) + (0.0 - math.log(0.3)) * uniform_part)


def draw_viscosity(key, part):
    return viscosity_field(key)


def draw_blocks(key, part):
    visc_field = viscosity_field(key)
    field_shape = (NX, NY * LAYERS)
    lane_layer = jnp.arange(NY * LAYERS, dtype=jnp.int32) % LAYERS
    key_list = jax.random.split(jax.random.fold_in(key, 9), 16)
    entries = []
    for row_idx in range(4):
        for col_idx in range(4):
            uniform_part = jax.random.uniform(key_list[row_idx * 4 + col_idx], field_shape, jnp.float32)
            if row_idx < 3 and col_idx == row_idx:
                line_key = jax.random.fold_in(key, 11 + row_idx)
                weak_pick = jax.random.randint(jax.random.fold_in(line_key, 1), (NY * LAYERS,), 0, 2)
                weak_line = jnp.logical_and(weak_pick == 1, lane_layer < LAYERS // 2)
                line_base = jnp.exp(math.log(0.0001) + math.log(10.0) * jax.random.uniform(jax.random.fold_in(line_key, 2), (NY * LAYERS,), jnp.float32))
                weak_ratio = line_base[None, :] * jnp.exp(math.log(4.0) * uniform_part)
                strong_ratio = 2.0 * jnp.exp(math.log(0.003) + math.log(4.0) * uniform_part)
                entry = visc_field * jnp.where(weak_line[None, :], weak_ratio, strong_ratio)
            elif row_idx < 3 and col_idx < 3:
                entry = visc_field * (0.1 * uniform_part - 0.05)
            elif row_idx == 3 and col_idx == 3:
                entry = -(0.05 + 0.25 * uniform_part)
            else:
                entry = uniform_part - 0.5
            entries.append(entry)
    return jnp.stack(entries)


def draw_forcing(key, part):
    rough_part = 0.02 * jax.random.normal(jax.random.fold_in(key, 5), (4, NX, NY * LAYERS), jnp.float32)
    return jnp.clip(rough_part, -0.12, 0.12)


def draw_basin_map(key, part):
    shift_x = jax.random.randint(jax.random.fold_in(key, 3), (NX, NY), 0, CX)
    shift_y = jax.random.randint(jax.random.fold_in(key, 4), (NX, NY), 0, max(CY // 2, 1))
    x_pos = jnp.arange(NX, dtype=jnp.int32)[:, None]
    y_pos = jnp.arange(NY, dtype=jnp.int32)[None, :]
    across = NY // CY
    tile_x = (x_pos + shift_x) // (2 * CX) % (NX // (2 * CX))
    tile_y = (y_pos + shift_y) // CY % across
    return (tile_x * across + tile_y).astype(jnp.int32)


def with_ends(values, stream_key, low, top_value):
    longest = values.shape.index(max(values.shape))
    spots = []
    for shift in (0, 1):
        where = [jax.random.randint(jax.random.fold_in(stream_key, axis), (), 0, length) for axis, length in enumerate(values.shape)]
        where[longest] = (where[longest] + shift) % values.shape[longest]
        spots.append(tuple(where))
    return values.at[spots[0]].set(low).at[spots[1]].set(top_value)


def steps_of(own_key, extent, cuts, low, high):
    factor_of, own = 1.0, jax.random.fold_in(own_key, 6)
    for dim, shards_of in cuts:
        steps = jnp.exp(jax.random.uniform(jax.random.fold_in(own, dim), (shards_of,), jnp.float32, low / len(cuts), high / len(cuts)))
        factor_of = factor_of * jnp.repeat(steps, extent[dim] // shards_of).reshape([-1 if axis == dim else 1 for axis in range(len(extent))])
    return factor_of


def noise(rng, shape, deviation, most, cuts=(), held_as=jnp.bfloat16):
    values = jax.random.normal(rng, shape, jnp.float32) * deviation
    if len(cuts) > 0:
        values = steps_of(rng, shape, cuts, -0.22, 0.18) * values
    return jnp.clip(values, min=-most, max=most).astype(held_as)


def setup_inputs(seed: int = 0) -> dict:
    arg_keys = jax.random.split(jax.random.key(seed), 8)
    return {
        "solution": noise(arg_keys[0], (4, NX, NY * LAYERS), 0.02, 0.12, ((1, 8), (2, 4)), jnp.float32),
        "forcing": draw_forcing(jax.random.fold_in(arg_keys[7], 71), 0),
        "viscosity": draw_viscosity(jax.random.fold_in(arg_keys[7], 71), 0),
        "blocks": draw_blocks(jax.random.fold_in(arg_keys[7], 71), 0),
        "layer_count": with_ends(jax.random.randint(arg_keys[4], (NX, NY), LAYERS // 2, LAYERS + 1), jax.random.fold_in(arg_keys[4], 1), LAYERS // 2, LAYERS).astype(jnp.int32),
        "bed_frozen": with_ends((jax.random.randint(arg_keys[5], (NX, NY), 0, 2) < 1).astype(jnp.int32), jax.random.fold_in(arg_keys[5], 1), 0, 1),
        "basin_map": draw_basin_map(jax.random.fold_in(arg_keys[7], 71), 0),
    }


coupling = 0.25


def neighbour_terms(velocity, viscosity, frozen):
    grid_view = velocity.reshape(3, NX, NY, LAYERS)
    padded = jnp.pad(grid_view, ((0, 0), (1, 1), (1, 1), (0, 0)))
    lower_cells = jnp.concatenate([grid_view[..., :1] * (1.0 - frozen)[None, :, :, None], grid_view[..., :-1]], axis=-1)
    upper_cells = jnp.concatenate([grid_view[..., 1:], jnp.zeros_like(grid_view[..., :1])], axis=-1)
    along_line = 2.0 * grid_view - padded[:, :-2, 1:-1] - padded[:, 2:, 1:-1]
    across_line = padded[:, 1:-1, :-2] + padded[:, 1:-1, 2:] + lower_cells + upper_cells
    return viscosity * along_line.reshape(velocity.shape) - coupling * viscosity * across_line.reshape(velocity.shape)


def operate(masked, matrix, viscosity, frozen):
    in_cell = jnp.sum(matrix * masked[None], axis=1)
    moving = in_cell[:3] + neighbour_terms(masked[:3], viscosity, frozen)
    return jnp.concatenate([moving, in_cell[3:]], axis=0)


def line_solve(line_lead, line_off, line_rhs):
    def sweep_down(carried, cell_cols):
        gain_prev, value_prev = carried
        lead_cell, off_cell, rhs_cell = cell_cols
        pivot = lead_cell - off_cell * gain_prev
        gain = off_cell / pivot
        value = (rhs_cell + off_cell * value_prev) / pivot
        return (gain, value), (gain, value)

    zeros_line = jnp.zeros((3, line_lead.shape[2]), jnp.float32)
    scanned = (jnp.moveaxis(line_lead, 1, 0), jnp.moveaxis(line_off, 1, 0), jnp.moveaxis(line_rhs, 1, 0))
    _, (gains, values) = lax.scan(sweep_down, (zeros_line, zeros_line), scanned)

    def sweep_up(next_value, cell_cols):
        gain, value = cell_cols
        solved = value + gain * next_value
        return solved, solved

    _, corrections = lax.scan(sweep_up, zeros_line, (gains, values), reverse=True)
    return jnp.moveaxis(corrections, 0, 1)


def reference(solution, forcing, viscosity, blocks, layer_count, bed_frozen, basin_map):
    layer_idx = jnp.arange(LAYERS, dtype=jnp.int32)
    active = (layer_idx[None, None, :] < layer_count[:, :, None]).astype(jnp.float32).reshape(NX, NY * LAYERS)
    frozen = bed_frozen.astype(jnp.float32)
    matrix = blocks.reshape(4, 4, NX, NY * LAYERS)
    masked = solution * active[None]
    residual = active[None] * (forcing - operate(masked, matrix, viscosity, frozen))
    diagonal = jnp.stack([matrix[0, 0], matrix[1, 1], matrix[2, 2]])
    line_lead = jnp.where(active[None] > 0.0, diagonal + 2.0 * viscosity[None], 1.0)
    line_off = jnp.broadcast_to((viscosity * active)[None], line_lead.shape)
    correction = line_solve(line_lead, line_off, residual[:3])
    pressure_in = residual[3] - (matrix[3, 0] * correction[0] + matrix[3, 1] * correction[1] + matrix[3, 2] * correction[2])
    pressure_step = active * pressure_in / viscosity
    smoothed = solution + jnp.concatenate([correction, pressure_step[None]], axis=0)
    post = active[None] * (forcing - operate(smoothed * active[None], matrix, viscosity, frozen))
    column_residual = jnp.sum(post.reshape(4, NX, NY, LAYERS), axis=-1)
    basin_residual = jax.ops.segment_sum(column_residual.reshape(4, NX * NY).T, basin_map.reshape(-1), num_segments=NBASIN).T
    return smoothed, column_residual, basin_residual
```

```python
import jax
import jax.numpy as jnp
from jax import lax
from jax.sharding import PartitionSpec as P

LAYERS = 80


coupling = 0.25


def neighbour_shift(block, axis, dim, width):
    count = lax.axis_size(axis)
    forward = [(i, i + 1) for i in range(count - 1)]
    backward = [(target, source) for source, target in forward]
    low = lax.ppermute(lax.slice_in_dim(block, block.shape[dim] - width, None, axis=dim), axis, forward)
    high = lax.ppermute(lax.slice_in_dim(block, 0, width, axis=dim), axis, backward)
    return low, high


def vertical_pair(grid_view, frozen):
    lower_cells = jnp.concatenate(
        [grid_view[..., :1] * (1.0 - frozen)[None, :, :, None], grid_view[..., :-1]], axis=-1
    )
    upper_cells = jnp.concatenate([grid_view[..., 1:], jnp.zeros_like(grid_view[..., :1])], axis=-1)
    return lower_cells + upper_cells


def neighbour_terms(grid_view, x_low, x_high, y_low, y_high, viscosity, frozen):
    shape = grid_view.shape
    x_pad = jnp.concatenate([x_low, grid_view, x_high], axis=1)
    y_pad = jnp.concatenate([y_low, grid_view, y_high], axis=2)
    along_line = 2.0 * grid_view - x_pad[:, :-2] - x_pad[:, 2:]
    across_line = y_pad[:, :, :-2] + y_pad[:, :, 2:] + vertical_pair(grid_view, frozen)
    flat = (3, shape[1], shape[2] * shape[3])
    return viscosity * along_line.reshape(flat) - coupling * viscosity * across_line.reshape(flat)


def in_cell_terms(masked, matrix):
    return jnp.sum(matrix * masked[None], axis=1)


def gather_rows(block, axis):
    count, mine = (lax.axis_size(axis), lax.axis_index(axis))
    if count > 8:
        return lax.all_gather(block, axis, axis=1, tiled=True)
    pieces = [block]
    for step in range(1, count):
        pairs = [((i + step) % count, i) for i in range(count)]
        pieces.append(lax.ppermute(block, axis, pairs))
    stacked = jnp.stack(pieces + pieces, axis=0)
    ordered = lax.dynamic_slice_in_dim(stacked, count - mine, count, axis=0)
    ordered = jnp.moveaxis(ordered, 0, 1)
    return ordered.reshape(block.shape[0], count * block.shape[1], *block.shape[2:])


def line_solve(line_lead, line_off, line_rhs):
    rows = line_lead.shape[1]
    gain_prev = jnp.zeros_like(line_rhs[:, 0])
    value_prev = jnp.zeros_like(line_rhs[:, 0])
    gains, values = [], []
    for cell_idx in range(rows):
        off_cell = line_off[:, cell_idx]
        pivot = line_lead[:, cell_idx] - off_cell * gain_prev
        gain_prev = off_cell / pivot
        value_prev = (line_rhs[:, cell_idx] + off_cell * value_prev) / pivot
        gains.append(gain_prev)
        values.append(value_prev)
    next_value = jnp.zeros_like(line_rhs[:, 0])
    corrections = list(values)
    for cell_idx in reversed(range(rows)):
        next_value = values[cell_idx] + gains[cell_idx] * next_value
        corrections[cell_idx] = next_value
    return jnp.stack(corrections, axis=1)


def line_solve_scan(line_lead, line_off, line_rhs):
    def sweep_down(carried, cell_cols):
        gain_prev, value_prev = carried
        lead_cell, off_cell, rhs_cell = cell_cols
        pivot = lead_cell - off_cell * gain_prev
        gain = off_cell / pivot
        value = (rhs_cell + off_cell * value_prev) / pivot
        return (gain, value), (gain, value)

    zeros_line = jnp.zeros_like(line_rhs[:, 0])
    scanned = (jnp.moveaxis(line_lead, 1, 0), jnp.moveaxis(line_off, 1, 0), jnp.moveaxis(line_rhs, 1, 0))
    _, (gains, values) = lax.scan(sweep_down, (zeros_line, zeros_line), scanned)

    def sweep_up(next_value, cell_cols):
        gain, value = cell_cols
        solved = value + gain * next_value
        return solved, solved

    _, corrections = lax.scan(sweep_up, zeros_line, (gains, values), reverse=True)
    return jnp.moveaxis(corrections, 0, 1)


def tree_sum(value, axis):
    count = lax.axis_size(axis)
    if count & (count - 1):
        return lax.psum(value, axis)
    step = 1
    while step < count:
        value = value + lax.ppermute(value, axis, [(i, i ^ step) for i in range(count)])
        step *= 2
    return value


def local(solution, forcing, viscosity, blocks, layer_count, bed_frozen, basin_map):
    row_count = solution.shape[1]
    lane_count = solution.shape[2]
    y_cells = lane_count // LAYERS
    layer_idx = jnp.arange(LAYERS, dtype=jnp.int32)
    active = (
        (layer_idx[None, None, :] < layer_count[:, :, None])
        .astype(jnp.float32)
        .reshape(row_count, lane_count)
    )
    frozen = bed_frozen.astype(jnp.float32)
    matrix = blocks.reshape(4, 4, row_count, lane_count)
    grid = (3, row_count, y_cells, LAYERS)

    masked = solution * active[None]
    masked_grid = masked[:3].reshape(grid)
    x_low, x_high = neighbour_shift(masked_grid, "gx", 1, 1)
    y_low, y_high = neighbour_shift(masked_grid, "gy", 2, 1)
    in_cell = in_cell_terms(masked, matrix)
    moving = in_cell[:3] + neighbour_terms(masked_grid, x_low, x_high, y_low, y_high, viscosity, frozen)
    residual = active[None] * (forcing - jnp.concatenate([moving, in_cell[3:]], axis=0))

    diagonal = jnp.stack([matrix[0, 0], matrix[1, 1], matrix[2, 2]])
    line_lead = jnp.where(active[None] > 0.0, diagonal + 2.0 * viscosity[None], 1.0)
    line_off = (viscosity * active)[None]
    packed = jnp.concatenate([line_lead, line_off, residual[:3]], axis=0)
    whole = gather_rows(packed, "gx")
    all_rows = whole.shape[1]
    solver = line_solve if all_rows <= 32 else line_solve_scan
    whole_corr = solver(whole[0:3], jnp.broadcast_to(whole[3:4], (3,) + whole.shape[1:]), whole[4:7])

    first = lax.axis_index("gx") * row_count
    padded_corr = jnp.pad(whole_corr, ((0, 0), (1, 1), (0, 0)))
    near_corr = lax.dynamic_slice_in_dim(padded_corr, first, row_count + 2, axis=1)
    correction = near_corr[:, 1:-1]

    pressure_in = residual[3] - (
        matrix[3, 0] * correction[0] + matrix[3, 1] * correction[1] + matrix[3, 2] * correction[2]
    )
    pressure_step = active * pressure_in / viscosity
    full_step = jnp.concatenate([correction, pressure_step[None]], axis=0)
    smoothed = solution + full_step

    smoothed_masked = smoothed * active[None]
    sm_grid = smoothed_masked[:3].reshape(grid)
    edge = (3, 1, y_cells, LAYERS)
    x_low2 = x_low + near_corr[:, :1].reshape(edge)
    x_high2 = x_high + near_corr[:, -1:].reshape(edge)
    y_low2, y_high2 = neighbour_shift(sm_grid, "gy", 2, 1)
    in_cell2 = in_cell_terms(smoothed_masked, matrix)
    moving2 = in_cell2[:3] + neighbour_terms(sm_grid, x_low2, x_high2, y_low2, y_high2, viscosity, frozen)
    post = active[None] * (forcing - jnp.concatenate([moving2, in_cell2[3:]], axis=0))

    column_residual = jnp.sum(post.reshape(4, row_count, y_cells, LAYERS), axis=-1)
    basin_count = lax.axis_size("gx") // 2 * lax.axis_size("gy")
    member = basin_map.reshape(-1)[:, None] == jnp.arange(basin_count, dtype=jnp.int32)[None, :]
    partial_sums = jnp.sum(
        jnp.where(member[None], column_residual.reshape(4, -1)[:, :, None], 0.0), axis=1
    )
    basin_residual = tree_sum(tree_sum(partial_sums, "gx"), "gy")
    return (smoothed, column_residual, basin_residual)


def solution(mesh):
    return jax.shard_map(
        local,
        mesh=mesh,
        in_specs=(
            P(None, "gx", "gy"),
            P(None, "gx", "gy"),
            P("gx", "gy"),
            P(None, "gx", "gy"),
            P("gx", "gy"),
            P("gx", "gy"),
            P("gx", "gy"),
        ),
        out_specs=(P(None, "gx", "gy"), P(None, "gx", "gy"), P()),
        check_vma=False,
    )
```

```python
import jax
import jax.numpy as jnp
from jax import lax
from jax.sharding import PartitionSpec as P

LAYERS = 80


coupling = 0.25


def neighbour_shift(block, axis, dim, width):
    count = lax.axis_size(axis)
    forward = [(i, i + 1) for i in range(count - 1)]
    backward = [(target, source) for source, target in forward]
    low = lax.ppermute(lax.slice_in_dim(block, block.shape[dim] - width, None, axis=dim), axis, forward)
    high = lax.ppermute(lax.slice_in_dim(block, 0, width, axis=dim), axis, backward)
    return low, high


def vertical_pair(grid_view, frozen):
    lower_cells = jnp.concatenate(
        [grid_view[..., :1] * (1.0 - frozen)[None, :, :, None], grid_view[..., :-1]], axis=-1
    )
    upper_cells = jnp.concatenate([grid_view[..., 1:], jnp.zeros_like(grid_view[..., :1])], axis=-1)
    return lower_cells + upper_cells


def neighbour_terms(grid_view, x_low, x_high, y_low, y_high, viscosity, frozen):
    shape = grid_view.shape
    x_pad = jnp.concatenate([x_low, grid_view, x_high], axis=1)
    y_pad = jnp.concatenate([y_low, grid_view, y_high], axis=2)
    along_line = 2.0 * grid_view - x_pad[:, :-2] - x_pad[:, 2:]
    across_line = y_pad[:, :, :-2] + y_pad[:, :, 2:] + vertical_pair(grid_view, frozen)
    flat = (3, shape[1], shape[2] * shape[3])
    return viscosity * along_line.reshape(flat) - coupling * viscosity * across_line.reshape(flat)


def in_cell_terms(masked, matrix):
    return jnp.sum(matrix * masked[None], axis=1)


def gather_rows(block, axis):
    count, mine = (lax.axis_size(axis), lax.axis_index(axis))
    if count > 8:
        return lax.all_gather(block, axis, axis=1, tiled=True)
    pieces = [block]
    for step in range(1, count):
        pairs = [((i + step) % count, i) for i in range(count)]
        pieces.append(lax.ppermute(block, axis, pairs))
    stacked = jnp.stack(pieces + pieces, axis=0)
    ordered = lax.dynamic_slice_in_dim(stacked, count - mine, count, axis=0)
    ordered = jnp.moveaxis(ordered, 0, 1)
    return ordered.reshape(block.shape[0], count * block.shape[1], *block.shape[2:])


def line_solve(line_lead, line_off, line_rhs):
    rows = line_lead.shape[1]
    gain_prev = jnp.zeros_like(line_rhs[:, 0])
    value_prev = jnp.zeros_like(line_rhs[:, 0])
    gains, values = [], []
    for cell_idx in range(rows):
        off_cell = line_off[:, cell_idx]
        pivot = line_lead[:, cell_idx] - off_cell * gain_prev
        gain_prev = off_cell / pivot
        value_prev = (line_rhs[:, cell_idx] + off_cell * value_prev) / pivot
        gains.append(gain_prev)
        values.append(value_prev)
    next_value = jnp.zeros_like(line_rhs[:, 0])
    corrections = list(values)
    for cell_idx in reversed(range(rows)):
        next_value = values[cell_idx] + gains[cell_idx] * next_value
        corrections[cell_idx] = next_value
    return jnp.stack(corrections, axis=1)


def line_solve_scan(line_lead, line_off, line_rhs):
    def sweep_down(carried, cell_cols):
        gain_prev, value_prev = carried
        lead_cell, off_cell, rhs_cell = cell_cols
        pivot = lead_cell - off_cell * gain_prev
        gain = off_cell / pivot
        value = (rhs_cell + off_cell * value_prev) / pivot
        return (gain, value), (gain, value)

    zeros_line = jnp.zeros_like(line_rhs[:, 0])
    scanned = (jnp.moveaxis(line_lead, 1, 0), jnp.moveaxis(line_off, 1, 0), jnp.moveaxis(line_rhs, 1, 0))
    _, (gains, values) = lax.scan(sweep_down, (zeros_line, zeros_line), scanned)

    def sweep_up(next_value, cell_cols):
        gain, value = cell_cols
        solved = value + gain * next_value
        return solved, solved

    _, corrections = lax.scan(sweep_up, zeros_line, (gains, values), reverse=True)
    return jnp.moveaxis(corrections, 0, 1)


def tree_sum(value, axis):
    count = lax.axis_size(axis)
    if count & (count - 1):
        return lax.psum(value, axis)
    step = 1
    while step < count:
        value = value + lax.ppermute(value, axis, [(i, i ^ step) for i in range(count)])
        step *= 2
    return value


def local(solution, forcing, viscosity, blocks, layer_count, bed_frozen, basin_map):
    row_count = solution.shape[1]
    lane_count = solution.shape[2]
    y_cells = lane_count // LAYERS
    layer_idx = jnp.arange(LAYERS, dtype=jnp.int32)
    active = (
        (layer_idx[None, None, :] < layer_count[:, :, None])
        .astype(jnp.float32)
        .reshape(row_count, lane_count)
    )
    frozen = bed_frozen.astype(jnp.float32)
    matrix = blocks.reshape(4, 4, row_count, lane_count)
    grid = (3, row_count, y_cells, LAYERS)

    diagonal = jnp.stack([matrix[0, 0], matrix[1, 1], matrix[2, 2]])
    line_lead = jnp.where(active[None] > 0.0, diagonal + 2.0 * viscosity[None], 1.0)
    line_off = (viscosity * active)[None]
    masked = solution * active[None]
    masked_grid = masked[:3].reshape(grid)
    x_low, x_high = neighbour_shift(masked_grid, "gx", 1, 1)
    y_low, y_high = neighbour_shift(masked_grid, "gy", 2, 1)
    in_cell = in_cell_terms(masked, matrix)
    moving = in_cell[:3] + neighbour_terms(masked_grid, x_low, x_high, y_low, y_high, viscosity, frozen)
    residual = active[None] * (forcing - jnp.concatenate([moving, in_cell[3:]], axis=0))

    whole_coef = gather_rows(jnp.concatenate([line_lead, line_off], axis=0), "gx")
    whole_rhs = gather_rows(residual[:3], "gx")
    all_rows = whole_rhs.shape[1]
    solver = line_solve if all_rows <= 32 else line_solve_scan
    whole_off = jnp.broadcast_to(whole_coef[3:4], (3,) + whole_rhs.shape[1:])
    whole_corr = solver(whole_coef[0:3], whole_off, whole_rhs)

    first = lax.axis_index("gx") * row_count
    padded_corr = jnp.pad(whole_corr, ((0, 0), (1, 1), (0, 0)))
    near_corr = lax.dynamic_slice_in_dim(padded_corr, first, row_count + 2, axis=1)
    correction = near_corr[:, 1:-1]

    pressure_in = residual[3] - (
        matrix[3, 0] * correction[0] + matrix[3, 1] * correction[1] + matrix[3, 2] * correction[2]
    )
    pressure_step = active * pressure_in / viscosity
    full_step = jnp.concatenate([correction, pressure_step[None]], axis=0)
    smoothed = solution + full_step

    smoothed_masked = smoothed * active[None]
    sm_grid = smoothed_masked[:3].reshape(grid)
    edge = (3, 1, y_cells, LAYERS)
    x_low2 = x_low + near_corr[:, :1].reshape(edge)
    x_high2 = x_high + near_corr[:, -1:].reshape(edge)
    y_low2, y_high2 = neighbour_shift(sm_grid, "gy", 2, 1)
    in_cell2 = in_cell_terms(smoothed_masked, matrix)
    moving2 = in_cell2[:3] + neighbour_terms(sm_grid, x_low2, x_high2, y_low2, y_high2, viscosity, frozen)
    post = active[None] * (forcing - jnp.concatenate([moving2, in_cell2[3:]], axis=0))

    column_residual = jnp.sum(post.reshape(4, row_count, y_cells, LAYERS), axis=-1)
    basin_count = lax.axis_size("gx") // 2 * lax.axis_size("gy")
    member = basin_map.reshape(-1)[:, None] == jnp.arange(basin_count, dtype=jnp.int32)[None, :]
    partial_sums = jnp.sum(
        jnp.where(member[None], column_residual.reshape(4, -1)[:, :, None], 0.0), axis=1
    )
    basin_residual = tree_sum(tree_sum(partial_sums, "gx"), "gy")
    return (smoothed, column_residual, basin_residual)


def solution(mesh):
    return jax.shard_map(
        local,
        mesh=mesh,
        in_specs=(
            P(None, "gx", "gy"),
            P(None, "gx", "gy"),
            P("gx", "gy"),
            P(None, "gx", "gy"),
            P("gx", "gy"),
            P("gx", "gy"),
            P("gx", "gy"),
        ),
        out_specs=(P(None, "gx", "gy"), P(None, "gx", "gy"), P()),
        check_vma=False,
    )
```

```python
import jax
import jax.numpy as jnp
from jax import lax
from jax.sharding import PartitionSpec as P

LAYERS = 80


coupling = 0.25


def neighbour_shift(block, axis, dim, width):
    count = lax.axis_size(axis)
    forward = [(i, i + 1) for i in range(count - 1)]
    backward = [(target, source) for source, target in forward]
    low = lax.ppermute(lax.slice_in_dim(block, block.shape[dim] - width, None, axis=dim), axis, forward)
    high = lax.ppermute(lax.slice_in_dim(block, 0, width, axis=dim), axis, backward)
    return low, high


def vertical_pair(grid_view, frozen):
    lower_cells = jnp.concatenate(
        [grid_view[..., :1] * (1.0 - frozen)[None, :, :, None], grid_view[..., :-1]], axis=-1
    )
    upper_cells = jnp.concatenate([grid_view[..., 1:], jnp.zeros_like(grid_view[..., :1])], axis=-1)
    return lower_cells + upper_cells


def neighbour_terms(grid_view, x_low, x_high, y_low, y_high, viscosity, frozen):
    shape = grid_view.shape
    y_pad = jnp.concatenate([y_low, grid_view, y_high], axis=2)
    if x_low is None:
        along_line = 2.0 * grid_view
    else:
        x_pad = jnp.concatenate([x_low, grid_view, x_high], axis=1)
        along_line = 2.0 * grid_view - x_pad[:, :-2] - x_pad[:, 2:]
    across_line = y_pad[:, :, :-2] + y_pad[:, :, 2:] + vertical_pair(grid_view, frozen)
    flat = (3, shape[1], shape[2] * shape[3])
    return viscosity * along_line.reshape(flat) - coupling * viscosity * across_line.reshape(flat)


def in_cell_terms(masked, matrix):
    return jnp.sum(matrix * masked[None], axis=1)


def gather_rows(block, axis):
    count, mine = (lax.axis_size(axis), lax.axis_index(axis))
    if count > 8:
        return lax.all_gather(block, axis, axis=1, tiled=True)
    pieces = [block]
    for step in range(1, count):
        pairs = [((i + step) % count, i) for i in range(count)]
        pieces.append(lax.ppermute(block, axis, pairs))
    stacked = jnp.stack(pieces + pieces, axis=0)
    ordered = lax.dynamic_slice_in_dim(stacked, count - mine, count, axis=0)
    ordered = jnp.moveaxis(ordered, 0, 1)
    return ordered.reshape(block.shape[0], count * block.shape[1], *block.shape[2:])


def line_solve(line_lead, line_off, line_rhs):
    rows = line_lead.shape[1]
    gain_prev = jnp.zeros_like(line_rhs[:, 0])
    value_prev = jnp.zeros_like(line_rhs[:, 0])
    gains, values = [], []
    for cell_idx in range(rows):
        off_cell = line_off[:, cell_idx]
        pivot = line_lead[:, cell_idx] - off_cell * gain_prev
        gain_prev = off_cell / pivot
        value_prev = (line_rhs[:, cell_idx] + off_cell * value_prev) / pivot
        gains.append(gain_prev)
        values.append(value_prev)
    next_value = jnp.zeros_like(line_rhs[:, 0])
    corrections = list(values)
    for cell_idx in reversed(range(rows)):
        next_value = values[cell_idx] + gains[cell_idx] * next_value
        corrections[cell_idx] = next_value
    return jnp.stack(corrections, axis=1)


def line_solve_scan(line_lead, line_off, line_rhs):
    def sweep_down(carried, cell_cols):
        gain_prev, value_prev = carried
        lead_cell, off_cell, rhs_cell = cell_cols
        pivot = lead_cell - off_cell * gain_prev
        gain = off_cell / pivot
        value = (rhs_cell + off_cell * value_prev) / pivot
        return (gain, value), (gain, value)

    zeros_line = jnp.zeros_like(line_rhs[:, 0])
    scanned = (jnp.moveaxis(line_lead, 1, 0), jnp.moveaxis(line_off, 1, 0), jnp.moveaxis(line_rhs, 1, 0))
    _, (gains, values) = lax.scan(sweep_down, (zeros_line, zeros_line), scanned)

    def sweep_up(next_value, cell_cols):
        gain, value = cell_cols
        solved = value + gain * next_value
        return solved, solved

    _, corrections = lax.scan(sweep_up, zeros_line, (gains, values), reverse=True)
    return jnp.moveaxis(corrections, 0, 1)


def tree_sum(value, axis):
    count = lax.axis_size(axis)
    if count & (count - 1):
        return lax.psum(value, axis)
    step = 1
    while step < count:
        value = value + lax.ppermute(value, axis, [(i, i ^ step) for i in range(count)])
        step *= 2
    return value


def local(solution, forcing, viscosity, blocks, layer_count, bed_frozen, basin_map):
    row_count = solution.shape[1]
    lane_count = solution.shape[2]
    y_cells = lane_count // LAYERS
    layer_idx = jnp.arange(LAYERS, dtype=jnp.int32)
    active = (
        (layer_idx[None, None, :] < layer_count[:, :, None])
        .astype(jnp.float32)
        .reshape(row_count, lane_count)
    )
    frozen = bed_frozen.astype(jnp.float32)
    matrix = blocks.reshape(4, 4, row_count, lane_count)
    grid = (3, row_count, y_cells, LAYERS)

    masked = solution * active[None]
    masked_grid = masked[:3].reshape(grid)
    y_low, y_high = neighbour_shift(masked_grid, "gy", 2, 1)
    in_cell = in_cell_terms(masked, matrix)
    moving = in_cell[:3] + neighbour_terms(masked_grid, None, None, y_low, y_high, viscosity, frozen)
    residual = active[None] * (forcing - jnp.concatenate([moving, in_cell[3:]], axis=0))

    diagonal = jnp.stack([matrix[0, 0], matrix[1, 1], matrix[2, 2]])
    line_lead = jnp.where(active[None] > 0.0, diagonal + 2.0 * viscosity[None], 1.0)
    line_off = (viscosity * active)[None]
    packed = jnp.concatenate([line_lead, line_off, residual[:3], masked[:3]], axis=0)
    whole = gather_rows(packed, "gx")
    all_rows = whole.shape[1]
    whole_off = whole[3:4]
    padded_masked = jnp.pad(whole[7:10], ((0, 0), (1, 1), (0, 0)))
    whole_rhs = whole[4:7] + whole_off * (padded_masked[:, :-2] + padded_masked[:, 2:])
    solver = line_solve if all_rows <= 32 else line_solve_scan
    whole_corr = solver(whole[0:3], jnp.broadcast_to(whole_off, whole_rhs.shape), whole_rhs)

    first = lax.axis_index("gx") * row_count
    padded_corr = jnp.pad(whole_corr, ((0, 0), (1, 1), (0, 0)))
    near_corr = lax.dynamic_slice_in_dim(padded_corr, first, row_count + 2, axis=1)
    near_masked = lax.dynamic_slice_in_dim(padded_masked, first, row_count + 2, axis=1)
    correction = near_corr[:, 1:-1]

    pressure_in = residual[3] - (
        matrix[3, 0] * correction[0] + matrix[3, 1] * correction[1] + matrix[3, 2] * correction[2]
    )
    pressure_step = active * pressure_in / viscosity
    full_step = jnp.concatenate([correction, pressure_step[None]], axis=0)
    smoothed = solution + full_step

    smoothed_masked = smoothed * active[None]
    sm_grid = smoothed_masked[:3].reshape(grid)
    edge = (3, 1, y_cells, LAYERS)
    x_low2 = (near_masked[:, :1] + near_corr[:, :1]).reshape(edge)
    x_high2 = (near_masked[:, -1:] + near_corr[:, -1:]).reshape(edge)
    y_low2, y_high2 = neighbour_shift(sm_grid, "gy", 2, 1)
    in_cell2 = in_cell_terms(smoothed_masked, matrix)
    moving2 = in_cell2[:3] + neighbour_terms(sm_grid, x_low2, x_high2, y_low2, y_high2, viscosity, frozen)
    post = active[None] * (forcing - jnp.concatenate([moving2, in_cell2[3:]], axis=0))

    column_residual = jnp.sum(post.reshape(4, row_count, y_cells, LAYERS), axis=-1)
    basin_count = lax.axis_size("gx") // 2 * lax.axis_size("gy")
    member = basin_map.reshape(-1)[:, None] == jnp.arange(basin_count, dtype=jnp.int32)[None, :]
    partial_sums = jnp.sum(
        jnp.where(member[None], column_residual.reshape(4, -1)[:, :, None], 0.0), axis=1
    )
    basin_residual = tree_sum(tree_sum(partial_sums, "gx"), "gy")
    return (smoothed, column_residual, basin_residual)


def solution(mesh):
    return jax.shard_map(
        local,
        mesh=mesh,
        in_specs=(
            P(None, "gx", "gy"),
            P(None, "gx", "gy"),
            P("gx", "gy"),
            P(None, "gx", "gy"),
            P("gx", "gy"),
            P("gx", "gy"),
            P("gx", "gy"),
        ),
        out_specs=(P(None, "gx", "gy"), P(None, "gx", "gy"), P()),
        check_vma=False,
    )
```

```python
import jax
import jax.numpy as jnp
from jax import lax
from jax.sharding import PartitionSpec as P

LAYERS = 80


coupling = 0.25


def neighbour_shift(block, axis, dim, width):
    count = lax.axis_size(axis)
    forward = [(i, i + 1) for i in range(count - 1)]
    backward = [(target, source) for source, target in forward]
    low = lax.ppermute(lax.slice_in_dim(block, block.shape[dim] - width, None, axis=dim), axis, forward)
    high = lax.ppermute(lax.slice_in_dim(block, 0, width, axis=dim), axis, backward)
    return low, high


def vertical_pair(grid_view, frozen):
    lower_cells = jnp.concatenate(
        [grid_view[..., :1] * (1.0 - frozen)[None, :, :, None], grid_view[..., :-1]], axis=-1
    )
    upper_cells = jnp.concatenate([grid_view[..., 1:], jnp.zeros_like(grid_view[..., :1])], axis=-1)
    return lower_cells + upper_cells


def neighbour_terms(grid_view, x_low, x_high, y_low, y_high, viscosity, frozen):
    shape = grid_view.shape
    y_pad = jnp.concatenate([y_low, grid_view, y_high], axis=2)
    if x_low is None:
        along_line = 2.0 * grid_view
    else:
        x_pad = jnp.concatenate([x_low, grid_view, x_high], axis=1)
        along_line = 2.0 * grid_view - x_pad[:, :-2] - x_pad[:, 2:]
    across_line = y_pad[:, :, :-2] + y_pad[:, :, 2:] + vertical_pair(grid_view, frozen)
    flat = (3, shape[1], shape[2] * shape[3])
    return viscosity * along_line.reshape(flat) - coupling * viscosity * across_line.reshape(flat)


def in_cell_terms(masked, matrix):
    return jnp.sum(matrix * masked[None], axis=1)


def gather_rows(block, axis):
    count, mine = (lax.axis_size(axis), lax.axis_index(axis))
    if count > 8:
        return lax.all_gather(block, axis, axis=1, tiled=True)
    pieces = [block]
    for step in range(1, count):
        pairs = [((i + step) % count, i) for i in range(count)]
        pieces.append(lax.ppermute(block, axis, pairs))
    stacked = jnp.stack(pieces + pieces, axis=0)
    ordered = lax.dynamic_slice_in_dim(stacked, count - mine, count, axis=0)
    ordered = jnp.moveaxis(ordered, 0, 1)
    return ordered.reshape(block.shape[0], count * block.shape[1], *block.shape[2:])


def line_solve(line_lead, line_off, line_rhs):
    rows = line_lead.shape[1]
    gain_prev = jnp.zeros_like(line_rhs[:, 0])
    value_prev = jnp.zeros_like(line_rhs[:, 0])
    gains, values = [], []
    for cell_idx in range(rows):
        off_cell = line_off[:, cell_idx]
        pivot = line_lead[:, cell_idx] - off_cell * gain_prev
        gain_prev = off_cell / pivot
        value_prev = (line_rhs[:, cell_idx] + off_cell * value_prev) / pivot
        gains.append(gain_prev)
        values.append(value_prev)
    next_value = jnp.zeros_like(line_rhs[:, 0])
    corrections = list(values)
    for cell_idx in reversed(range(rows)):
        next_value = values[cell_idx] + gains[cell_idx] * next_value
        corrections[cell_idx] = next_value
    return jnp.stack(corrections, axis=1)


def line_solve_scan(line_lead, line_off, line_rhs):
    def sweep_down(carried, cell_cols):
        gain_prev, value_prev = carried
        lead_cell, off_cell, rhs_cell = cell_cols
        pivot = lead_cell - off_cell * gain_prev
        gain = off_cell / pivot
        value = (rhs_cell + off_cell * value_prev) / pivot
        return (gain, value), (gain, value)

    zeros_line = jnp.zeros_like(line_rhs[:, 0])
    scanned = (jnp.moveaxis(line_lead, 1, 0), jnp.moveaxis(line_off, 1, 0), jnp.moveaxis(line_rhs, 1, 0))
    _, (gains, values) = lax.scan(sweep_down, (zeros_line, zeros_line), scanned)

    def sweep_up(next_value, cell_cols):
        gain, value = cell_cols
        solved = value + gain * next_value
        return solved, solved

    _, corrections = lax.scan(sweep_up, zeros_line, (gains, values), reverse=True)
    return jnp.moveaxis(corrections, 0, 1)


def tree_sum(value, axis):
    count = lax.axis_size(axis)
    if count & (count - 1):
        return lax.psum(value, axis)
    step = 1
    while step < count:
        value = value + lax.ppermute(value, axis, [(i, i ^ step) for i in range(count)])
        step *= 2
    return value


def local(solution, forcing, viscosity, blocks, layer_count, bed_frozen, basin_map):
    row_count = solution.shape[1]
    lane_count = solution.shape[2]
    y_cells = lane_count // LAYERS
    layer_idx = jnp.arange(LAYERS, dtype=jnp.int32)
    active = (
        (layer_idx[None, None, :] < layer_count[:, :, None])
        .astype(jnp.float32)
        .reshape(row_count, lane_count)
    )
    frozen = bed_frozen.astype(jnp.float32)
    matrix = blocks.reshape(4, 4, row_count, lane_count)
    grid = (3, row_count, y_cells, LAYERS)

    masked = solution * active[None]
    masked_grid = masked[:3].reshape(grid)
    weight_grid = (coupling * viscosity * active).reshape(1, row_count, y_cells, LAYERS)
    basin_grid = jnp.broadcast_to(
        basin_map.astype(jnp.float32)[None, :, :, None], (1, row_count, y_cells, LAYERS)
    )
    halo_source = jnp.concatenate([masked_grid, weight_grid, basin_grid], axis=0)
    from_low, from_high = neighbour_shift(halo_source, "gy", 2, 1)
    y_low, y_high = from_low[:3], from_high[:3]
    in_cell = in_cell_terms(masked, matrix)
    moving = in_cell[:3] + neighbour_terms(masked_grid, None, None, y_low, y_high, viscosity, frozen)
    residual = active[None] * (forcing - jnp.concatenate([moving, in_cell[3:]], axis=0))

    diagonal = jnp.stack([matrix[0, 0], matrix[1, 1], matrix[2, 2]])
    line_lead = jnp.where(active[None] > 0.0, diagonal + 2.0 * viscosity[None], 1.0)
    line_off = (viscosity * active)[None]
    packed = jnp.concatenate([line_lead, line_off, residual[:3], masked[:3]], axis=0)
    whole = gather_rows(packed, "gx")
    all_rows = whole.shape[1]
    whole_off = whole[3:4]
    padded_masked = jnp.pad(whole[7:10], ((0, 0), (1, 1), (0, 0)))
    whole_rhs = whole[4:7] + whole_off * (padded_masked[:, :-2] + padded_masked[:, 2:])
    solver = line_solve if all_rows <= 32 else line_solve_scan
    whole_corr = solver(whole[0:3], jnp.broadcast_to(whole_off, whole_rhs.shape), whole_rhs)

    first = lax.axis_index("gx") * row_count
    padded_corr = jnp.pad(whole_corr, ((0, 0), (1, 1), (0, 0)))
    near_corr = lax.dynamic_slice_in_dim(padded_corr, first, row_count + 2, axis=1)
    near_masked = lax.dynamic_slice_in_dim(padded_masked, first, row_count + 2, axis=1)
    correction = near_corr[:, 1:-1]

    pressure_in = residual[3] - (
        matrix[3, 0] * correction[0] + matrix[3, 1] * correction[1] + matrix[3, 2] * correction[2]
    )
    pressure_step = active * pressure_in / viscosity
    full_step = jnp.concatenate([correction, pressure_step[None]], axis=0)
    smoothed = solution + full_step

    smoothed_masked = smoothed * active[None]
    sm_grid = smoothed_masked[:3].reshape(grid)
    edge = (3, 1, y_cells, LAYERS)
    x_low2 = (near_masked[:, :1] + near_corr[:, :1]).reshape(edge)
    x_high2 = (near_masked[:, -1:] + near_corr[:, -1:]).reshape(edge)
    no_cols = jnp.zeros((3, row_count, 1, LAYERS), jnp.float32)
    in_cell2 = in_cell_terms(smoothed_masked, matrix)
    moving2 = in_cell2[:3] + neighbour_terms(sm_grid, x_low2, x_high2, no_cols, no_cols, viscosity, frozen)
    post = active[None] * (forcing - jnp.concatenate([moving2, in_cell2[3:]], axis=0))
    column_local = jnp.sum(post.reshape(4, row_count, y_cells, LAYERS), axis=-1)

    to_low = jnp.sum(from_low[3:4, :, 0] * sm_grid[:, :, 0], axis=-1)
    to_high = jnp.sum(from_high[3:4, :, 0] * sm_grid[:, :, -1], axis=-1)
    count = lax.axis_size("gy")
    forward = [(i, i + 1) for i in range(count - 1)]
    backward = [(target, source) for source, target in forward]
    for_last = lax.ppermute(to_low, "gy", backward)
    for_first = lax.ppermute(to_high, "gy", forward)
    edge_terms = jnp.zeros((3, row_count, y_cells), jnp.float32)
    edge_terms = edge_terms.at[:, :, 0].set(for_first).at[:, :, -1].set(for_last)
    column_residual = column_local + jnp.pad(edge_terms, ((0, 1), (0, 0), (0, 0)))

    basin_count = lax.axis_size("gx") // 2 * lax.axis_size("gy")
    basin_ids = jnp.arange(basin_count, dtype=jnp.int32)
    member = basin_map.reshape(-1)[:, None] == basin_ids[None, :]
    partial_sums = jnp.sum(jnp.where(member[None], column_local.reshape(4, -1)[:, :, None], 0.0), axis=1)
    beside_ids = jnp.concatenate([from_low[4, :, 0, 0], from_high[4, :, 0, 0]]).astype(jnp.int32)
    beside_member = beside_ids[:, None] == basin_ids[None, :]
    beside_terms = jnp.concatenate([to_low, to_high], axis=1)
    beside_sums = jnp.sum(jnp.where(beside_member[None], beside_terms[:, :, None], 0.0), axis=1)
    partial_sums = partial_sums + jnp.pad(beside_sums, ((0, 1), (0, 0)))
    basin_residual = tree_sum(tree_sum(partial_sums, "gx"), "gy")
    return (smoothed, column_residual, basin_residual)


def solution(mesh):
    return jax.shard_map(
        local,
        mesh=mesh,
        in_specs=(
            P(None, "gx", "gy"),
            P(None, "gx", "gy"),
            P("gx", "gy"),
            P(None, "gx", "gy"),
            P("gx", "gy"),
            P("gx", "gy"),
            P("gx", "gy"),
        ),
        out_specs=(P(None, "gx", "gy"), P(None, "gx", "gy"), P()),
        check_vma=False,
    )
```

```python
import jax
import jax.numpy as jnp
from jax import lax
from jax.sharding import PartitionSpec as P

LAYERS = 80


coupling = 0.25


def neighbour_shift(block, axis, dim, width):
    count = lax.axis_size(axis)
    forward = [(i, i + 1) for i in range(count - 1)]
    backward = [(target, source) for source, target in forward]
    low = lax.ppermute(lax.slice_in_dim(block, block.shape[dim] - width, None, axis=dim), axis, forward)
    high = lax.ppermute(lax.slice_in_dim(block, 0, width, axis=dim), axis, backward)
    return low, high


def vertical_pair(grid_view, frozen):
    lower_cells = jnp.concatenate(
        [grid_view[..., :1] * (1.0 - frozen)[None, :, :, None], grid_view[..., :-1]], axis=-1
    )
    upper_cells = jnp.concatenate([grid_view[..., 1:], jnp.zeros_like(grid_view[..., :1])], axis=-1)
    return lower_cells + upper_cells


def neighbour_terms(grid_view, x_low, x_high, y_low, y_high, viscosity, frozen):
    shape = grid_view.shape
    y_pad = jnp.concatenate([y_low, grid_view, y_high], axis=2)
    if x_low is None:
        along_line = 2.0 * grid_view
    else:
        x_pad = jnp.concatenate([x_low, grid_view, x_high], axis=1)
        along_line = 2.0 * grid_view - x_pad[:, :-2] - x_pad[:, 2:]
    across_line = y_pad[:, :, :-2] + y_pad[:, :, 2:] + vertical_pair(grid_view, frozen)
    flat = (3, shape[1], shape[2] * shape[3])
    return viscosity * along_line.reshape(flat) - coupling * viscosity * across_line.reshape(flat)


def in_cell_terms(masked, matrix):
    return jnp.sum(matrix * masked[None], axis=1)


def gather_rows(block, axis):
    count, mine = (lax.axis_size(axis), lax.axis_index(axis))
    if count > 8:
        return lax.all_gather(block, axis, axis=1, tiled=True)
    pieces = [block]
    for step in range(1, count):
        pairs = [((i + step) % count, i) for i in range(count)]
        pieces.append(lax.ppermute(block, axis, pairs))
    stacked = jnp.stack(pieces + pieces, axis=0)
    ordered = lax.dynamic_slice_in_dim(stacked, count - mine, count, axis=0)
    ordered = jnp.moveaxis(ordered, 0, 1)
    return ordered.reshape(block.shape[0], count * block.shape[1], *block.shape[2:])


def line_solve(line_lead, line_off, line_rhs):
    rows = line_lead.shape[1]
    gain_prev = jnp.zeros_like(line_rhs[:, 0])
    value_prev = jnp.zeros_like(line_rhs[:, 0])
    gains, values = [], []
    for cell_idx in range(rows):
        off_cell = line_off[:, cell_idx]
        pivot = line_lead[:, cell_idx] - off_cell * gain_prev
        gain_prev = off_cell / pivot
        value_prev = (line_rhs[:, cell_idx] + off_cell * value_prev) / pivot
        gains.append(gain_prev)
        values.append(value_prev)
    next_value = jnp.zeros_like(line_rhs[:, 0])
    corrections = list(values)
    for cell_idx in reversed(range(rows)):
        next_value = values[cell_idx] + gains[cell_idx] * next_value
        corrections[cell_idx] = next_value
    return jnp.stack(corrections, axis=1)


def line_solve_scan(line_lead, line_off, line_rhs):
    def sweep_down(carried, cell_cols):
        gain_prev, value_prev = carried
        lead_cell, off_cell, rhs_cell = cell_cols
        pivot = lead_cell - off_cell * gain_prev
        gain = off_cell / pivot
        value = (rhs_cell + off_cell * value_prev) / pivot
        return (gain, value), (gain, value)

    zeros_line = jnp.zeros_like(line_rhs[:, 0])
    scanned = (jnp.moveaxis(line_lead, 1, 0), jnp.moveaxis(line_off, 1, 0), jnp.moveaxis(line_rhs, 1, 0))
    _, (gains, values) = lax.scan(sweep_down, (zeros_line, zeros_line), scanned)

    def sweep_up(next_value, cell_cols):
        gain, value = cell_cols
        solved = value + gain * next_value
        return solved, solved

    _, corrections = lax.scan(sweep_up, zeros_line, (gains, values), reverse=True)
    return jnp.moveaxis(corrections, 0, 1)


def tree_sum(value, axis):
    count = lax.axis_size(axis)
    if count & (count - 1):
        return lax.psum(value, axis)
    step = 1
    while step < count:
        value = value + lax.ppermute(value, axis, [(i, i ^ step) for i in range(count)])
        step *= 2
    return value


def local(solution, forcing, viscosity, blocks, layer_count, bed_frozen, basin_map):
    row_count = solution.shape[1]
    lane_count = solution.shape[2]
    y_cells = lane_count // LAYERS
    layer_idx = jnp.arange(LAYERS, dtype=jnp.int32)
    active = (
        (layer_idx[None, None, :] < layer_count[:, :, None])
        .astype(jnp.float32)
        .reshape(row_count, lane_count)
    )
    frozen = bed_frozen.astype(jnp.float32)
    matrix = blocks.reshape(4, 4, row_count, lane_count)
    grid = (3, row_count, y_cells, LAYERS)

    masked = solution * active[None]
    masked_grid = masked[:3].reshape(grid)
    weight_grid = (coupling * viscosity * active).reshape(1, row_count, y_cells, LAYERS)
    halo_source = jnp.concatenate([masked_grid, weight_grid], axis=0)
    from_low, from_high = neighbour_shift(halo_source, "gy", 2, 1)
    y_low, y_high = from_low[:3], from_high[:3]
    in_cell = in_cell_terms(masked, matrix)
    moving = in_cell[:3] + neighbour_terms(masked_grid, None, None, y_low, y_high, viscosity, frozen)
    residual = active[None] * (forcing - jnp.concatenate([moving, in_cell[3:]], axis=0))

    diagonal = jnp.stack([matrix[0, 0], matrix[1, 1], matrix[2, 2]])
    line_lead = jnp.where(active[None] > 0.0, diagonal + 2.0 * viscosity[None], 1.0)
    line_off = (viscosity * active)[None]
    packed = jnp.concatenate([line_lead, line_off, residual[:3], masked[:3]], axis=0)
    whole = gather_rows(packed, "gx")
    all_rows = whole.shape[1]
    whole_off = whole[3:4]
    padded_masked = jnp.pad(whole[7:10], ((0, 0), (1, 1), (0, 0)))
    whole_rhs = whole[4:7] + whole_off * (padded_masked[:, :-2] + padded_masked[:, 2:])
    solver = line_solve if all_rows <= 32 else line_solve_scan
    whole_corr = solver(whole[0:3], jnp.broadcast_to(whole_off, whole_rhs.shape), whole_rhs)

    first = lax.axis_index("gx") * row_count
    padded_corr = jnp.pad(whole_corr, ((0, 0), (1, 1), (0, 0)))
    near_corr = lax.dynamic_slice_in_dim(padded_corr, first, row_count + 2, axis=1)
    near_masked = lax.dynamic_slice_in_dim(padded_masked, first, row_count + 2, axis=1)
    correction = near_corr[:, 1:-1]

    pressure_in = residual[3] - (
        matrix[3, 0] * correction[0] + matrix[3, 1] * correction[1] + matrix[3, 2] * correction[2]
    )
    pressure_step = active * pressure_in / viscosity
    full_step = jnp.concatenate([correction, pressure_step[None]], axis=0)
    smoothed = solution + full_step

    smoothed_masked = smoothed * active[None]
    sm_grid = smoothed_masked[:3].reshape(grid)
    edge = (3, 1, y_cells, LAYERS)
    x_low2 = (near_masked[:, :1] + near_corr[:, :1]).reshape(edge)
    x_high2 = (near_masked[:, -1:] + near_corr[:, -1:]).reshape(edge)
    no_cols = jnp.zeros((3, row_count, 1, LAYERS), jnp.float32)
    in_cell2 = in_cell_terms(smoothed_masked, matrix)
    moving2 = in_cell2[:3] + neighbour_terms(sm_grid, x_low2, x_high2, no_cols, no_cols, viscosity, frozen)
    post = active[None] * (forcing - jnp.concatenate([moving2, in_cell2[3:]], axis=0))
    column_local = jnp.sum(post.reshape(4, row_count, y_cells, LAYERS), axis=-1)

    to_low = jnp.sum(from_low[3:4, :, 0] * sm_grid[:, :, 0], axis=-1)
    to_high = jnp.sum(from_high[3:4, :, 0] * sm_grid[:, :, -1], axis=-1)
    count = lax.axis_size("gy")
    forward = [(i, i + 1) for i in range(count - 1)]
    backward = [(target, source) for source, target in forward]
    for_last = lax.ppermute(to_low, "gy", backward)
    for_first = lax.ppermute(to_high, "gy", forward)
    edge_terms = jnp.zeros((3, row_count, y_cells), jnp.float32)
    edge_terms = edge_terms.at[:, :, 0].set(for_first).at[:, :, -1].set(for_last)
    column_residual = column_local + jnp.pad(edge_terms, ((0, 1), (0, 0), (0, 0)))

    basin_count = lax.axis_size("gx") // 2 * lax.axis_size("gy")
    member = basin_map.reshape(-1)[:, None] == jnp.arange(basin_count, dtype=jnp.int32)[None, :]
    partial_sums = jnp.sum(
        jnp.where(member[None], column_residual.reshape(4, -1)[:, :, None], 0.0), axis=1
    )
    basin_residual = tree_sum(tree_sum(partial_sums, "gx"), "gy")
    return (smoothed, column_residual, basin_residual)


def solution(mesh):
    return jax.shard_map(
        local,
        mesh=mesh,
        in_specs=(
            P(None, "gx", "gy"),
            P(None, "gx", "gy"),
            P("gx", "gy"),
            P(None, "gx", "gy"),
            P("gx", "gy"),
            P("gx", "gy"),
            P("gx", "gy"),
        ),
        out_specs=(P(None, "gx", "gy"), P(None, "gx", "gy"), P()),
        check_vma=False,
    )
```

```python
import jax
import jax.numpy as jnp
from jax import lax
from jax.sharding import PartitionSpec as P

LAYERS = 80


coupling = 0.25


def neighbour_shift(block, axis, dim, width):
    count = lax.axis_size(axis)
    forward = [(i, i + 1) for i in range(count - 1)]
    backward = [(target, source) for source, target in forward]
    low = lax.ppermute(lax.slice_in_dim(block, block.shape[dim] - width, None, axis=dim), axis, forward)
    high = lax.ppermute(lax.slice_in_dim(block, 0, width, axis=dim), axis, backward)
    return low, high


def vertical_pair(grid_view, frozen):
    lower_cells = jnp.concatenate(
        [grid_view[..., :1] * (1.0 - frozen)[None, :, :, None], grid_view[..., :-1]], axis=-1
    )
    upper_cells = jnp.concatenate([grid_view[..., 1:], jnp.zeros_like(grid_view[..., :1])], axis=-1)
    return lower_cells + upper_cells


def neighbour_terms(grid_view, x_low, x_high, y_low, y_high, viscosity, frozen):
    shape = grid_view.shape
    y_pad = jnp.concatenate([y_low, grid_view, y_high], axis=2)
    if x_low is None:
        along_line = 2.0 * grid_view
    else:
        x_pad = jnp.concatenate([x_low, grid_view, x_high], axis=1)
        along_line = 2.0 * grid_view - x_pad[:, :-2] - x_pad[:, 2:]
    across_line = y_pad[:, :, :-2] + y_pad[:, :, 2:] + vertical_pair(grid_view, frozen)
    flat = (3, shape[1], shape[2] * shape[3])
    return viscosity * along_line.reshape(flat) - coupling * viscosity * across_line.reshape(flat)


def in_cell_terms(masked, matrix):
    return jnp.sum(matrix * masked[None], axis=1)


def gather_rows(block, axis):
    count, mine = (lax.axis_size(axis), lax.axis_index(axis))
    if count > 8:
        return lax.all_gather(block, axis, axis=1, tiled=True)
    pieces = [block]
    for step in range(1, count):
        pairs = [((i + step) % count, i) for i in range(count)]
        pieces.append(lax.ppermute(block, axis, pairs))
    stacked = jnp.stack(pieces + pieces, axis=0)
    ordered = lax.dynamic_slice_in_dim(stacked, count - mine, count, axis=0)
    ordered = jnp.moveaxis(ordered, 0, 1)
    return ordered.reshape(block.shape[0], count * block.shape[1], *block.shape[2:])


def line_solve(line_lead, line_off, line_rhs):
    rows = line_lead.shape[1]
    gain_prev = jnp.zeros_like(line_rhs[:, 0])
    value_prev = jnp.zeros_like(line_rhs[:, 0])
    gains, values = [], []
    for cell_idx in range(rows):
        off_cell = line_off[:, cell_idx]
        pivot = line_lead[:, cell_idx] - off_cell * gain_prev
        gain_prev = off_cell / pivot
        value_prev = (line_rhs[:, cell_idx] + off_cell * value_prev) / pivot
        gains.append(gain_prev)
        values.append(value_prev)
    next_value = jnp.zeros_like(line_rhs[:, 0])
    corrections = list(values)
    for cell_idx in reversed(range(rows)):
        next_value = values[cell_idx] + gains[cell_idx] * next_value
        corrections[cell_idx] = next_value
    return jnp.stack(corrections, axis=1)


def line_solve_scan(line_lead, line_off, line_rhs):
    def sweep_down(carried, cell_cols):
        gain_prev, value_prev = carried
        lead_cell, off_cell, rhs_cell = cell_cols
        pivot = lead_cell - off_cell * gain_prev
        gain = off_cell / pivot
        value = (rhs_cell + off_cell * value_prev) / pivot
        return (gain, value), (gain, value)

    zeros_line = jnp.zeros_like(line_rhs[:, 0])
    scanned = (jnp.moveaxis(line_lead, 1, 0), jnp.moveaxis(line_off, 1, 0), jnp.moveaxis(line_rhs, 1, 0))
    _, (gains, values) = lax.scan(sweep_down, (zeros_line, zeros_line), scanned)

    def sweep_up(next_value, cell_cols):
        gain, value = cell_cols
        solved = value + gain * next_value
        return solved, solved

    _, corrections = lax.scan(sweep_up, zeros_line, (gains, values), reverse=True)
    return jnp.moveaxis(corrections, 0, 1)


def tree_sum(value, axis):
    count = lax.axis_size(axis)
    if count & (count - 1):
        return lax.psum(value, axis)
    step = 1
    while step < count:
        value = value + lax.ppermute(value, axis, [(i, i ^ step) for i in range(count)])
        step *= 2
    return value


def local(solution, forcing, viscosity, blocks, layer_count, bed_frozen, basin_map):
    row_count = solution.shape[1]
    lane_count = solution.shape[2]
    y_cells = lane_count // LAYERS
    layer_idx = jnp.arange(LAYERS, dtype=jnp.int32)
    active = (
        (layer_idx[None, None, :] < layer_count[:, :, None])
        .astype(jnp.float32)
        .reshape(row_count, lane_count)
    )
    frozen = bed_frozen.astype(jnp.float32)
    matrix = blocks.reshape(4, 4, row_count, lane_count)
    grid = (3, row_count, y_cells, LAYERS)

    masked = solution * active[None]
    masked_grid = masked[:3].reshape(grid)
    weight_grid = (coupling * viscosity * active).reshape(1, row_count, y_cells, LAYERS)
    basin_grid = jnp.broadcast_to(
        basin_map.astype(jnp.float32)[None, :, :, None], (1, row_count, y_cells, LAYERS)
    )
    halo_source = jnp.concatenate([masked_grid, weight_grid, basin_grid], axis=0)
    from_low, from_high = neighbour_shift(halo_source, "gy", 2, 1)
    y_low, y_high = from_low[:3], from_high[:3]
    in_cell = in_cell_terms(masked, matrix)
    moving = in_cell[:3] + neighbour_terms(masked_grid, None, None, y_low, y_high, viscosity, frozen)
    residual = active[None] * (forcing - jnp.concatenate([moving, in_cell[3:]], axis=0))

    diagonal = jnp.stack([matrix[0, 0], matrix[1, 1], matrix[2, 2]])
    line_lead = jnp.where(active[None] > 0.0, diagonal + 2.0 * viscosity[None], 1.0)
    line_off = (viscosity * active)[None]
    packed = jnp.concatenate([line_lead, line_off, residual[:3], masked[:3]], axis=0)
    whole = gather_rows(packed, "gx")
    all_rows = whole.shape[1]
    whole_off = whole[3:4]
    padded_masked = jnp.pad(whole[7:10], ((0, 0), (1, 1), (0, 0)))
    whole_rhs = whole[4:7] + whole_off * (padded_masked[:, :-2] + padded_masked[:, 2:])
    solver = line_solve if all_rows <= 32 else line_solve_scan
    whole_corr = solver(whole[0:3], jnp.broadcast_to(whole_off, whole_rhs.shape), whole_rhs)

    first = lax.axis_index("gx") * row_count
    padded_corr = jnp.pad(whole_corr, ((0, 0), (1, 1), (0, 0)))
    near_corr = lax.dynamic_slice_in_dim(padded_corr, first, row_count + 2, axis=1)
    near_masked = lax.dynamic_slice_in_dim(padded_masked, first, row_count + 2, axis=1)
    correction = near_corr[:, 1:-1]

    pressure_in = residual[3] - (
        matrix[3, 0] * correction[0] + matrix[3, 1] * correction[1] + matrix[3, 2] * correction[2]
    )
    pressure_step = active * pressure_in / viscosity
    full_step = jnp.concatenate([correction, pressure_step[None]], axis=0)
    smoothed = solution + full_step

    smoothed_masked = smoothed * active[None]
    sm_grid = smoothed_masked[:3].reshape(grid)
    edge = (3, 1, y_cells, LAYERS)
    x_low2 = (near_masked[:, :1] + near_corr[:, :1]).reshape(edge)
    x_high2 = (near_masked[:, -1:] + near_corr[:, -1:]).reshape(edge)
    no_cols = jnp.zeros((3, row_count, 1, LAYERS), jnp.float32)
    in_cell2 = in_cell_terms(smoothed_masked, matrix)
    moving2 = in_cell2[:3] + neighbour_terms(sm_grid, x_low2, x_high2, no_cols, no_cols, viscosity, frozen)
    post = active[None] * (forcing - jnp.concatenate([moving2, in_cell2[3:]], axis=0))
    column_local = jnp.sum(post.reshape(4, row_count, y_cells, LAYERS), axis=-1)

    to_low = jnp.sum(from_low[3:4, :, 0] * sm_grid[:, :, 0], axis=-1)
    to_high = jnp.sum(from_high[3:4, :, 0] * sm_grid[:, :, -1], axis=-1)
    edge_terms = jnp.zeros((3, row_count, y_cells), jnp.float32)
    count = lax.axis_size("gy")
    if count != 4:
        forward = [(i, i + 1) for i in range(count - 1)]
        backward = [(target, source) for source, target in forward]
        for_last = lax.ppermute(to_low, "gy", backward)
        for_first = lax.ppermute(to_high, "gy", forward)
        edge_terms = edge_terms.at[:, :, 0].set(for_first).at[:, :, -1].set(for_last)
        column_residual = column_local + jnp.pad(edge_terms, ((0, 1), (0, 0), (0, 0)))
    basin_count = lax.axis_size("gx") // 2 * lax.axis_size("gy")
    basin_ids = jnp.arange(basin_count, dtype=jnp.int32)
    member = basin_map.reshape(-1)[:, None] == basin_ids[None, :]
    partial_sums = jnp.sum(jnp.where(member[None], column_local.reshape(4, -1)[:, :, None], 0.0), axis=1)
    beside_ids = jnp.concatenate([from_low[4, :, 0, 0], from_high[4, :, 0, 0]]).astype(jnp.int32)
    beside_member = beside_ids[:, None] == basin_ids[None, :]
    beside_terms = jnp.concatenate([to_low, to_high], axis=1)
    beside_sums = jnp.sum(jnp.where(beside_member[None], beside_terms[:, :, None], 0.0), axis=1)
    partial_sums = partial_sums + jnp.pad(beside_sums, ((0, 1), (0, 0)))
    basin_sums = tree_sum(partial_sums, "gx")
    if count != 4:
        basin_residual = tree_sum(basin_sums, "gy")
    else:
        mine = lax.axis_index("gy")
        for pairs in ([(0, 1), (1, 0), (2, 3), (3, 2)], [(1, 2), (2, 1), (3, 0), (0, 3)]):
            sends_high = jnp.array([b == (a + 1) % 4 for a, b in sorted(pairs)])[mine]
            edge_out = jnp.where(sends_high, to_high, to_low)
            message = jnp.concatenate([basin_sums, jnp.pad(edge_out.reshape(3, -1), ((0, 1), (0, 0)))], axis=1)
            got = lax.ppermute(message, "gy", pairs)
            basin_sums = basin_sums + got[:, :basin_count]
            edge_in = got[:3, basin_count:].reshape(3, row_count)
            edge_terms = jnp.where(
                sends_high,
                edge_terms.at[:, :, -1].set(edge_in),
                edge_terms.at[:, :, 0].set(edge_in),
            )
        basin_residual = basin_sums
        column_residual = column_local + jnp.pad(edge_terms, ((0, 1), (0, 0), (0, 0)))
    return (smoothed, column_residual, basin_residual)


def solution(mesh):
    return jax.shard_map(
        local,
        mesh=mesh,
        in_specs=(
            P(None, "gx", "gy"),
            P(None, "gx", "gy"),
            P("gx", "gy"),
            P(None, "gx", "gy"),
            P("gx", "gy"),
            P("gx", "gy"),
            P("gx", "gy"),
        ),
        out_specs=(P(None, "gx", "gy"), P(None, "gx", "gy"), P()),
        check_vma=False,
    )
```

```python
import jax
import jax.numpy as jnp
from jax import lax
from jax.sharding import PartitionSpec as P

LAYERS = 80


coupling = 0.25


def neighbour_shift(block, axis, dim, width):
    count = lax.axis_size(axis)
    forward = [(i, i + 1) for i in range(count - 1)]
    backward = [(target, source) for source, target in forward]
    low = lax.ppermute(lax.slice_in_dim(block, block.shape[dim] - width, None, axis=dim), axis, forward)
    high = lax.ppermute(lax.slice_in_dim(block, 0, width, axis=dim), axis, backward)
    return low, high


def vertical_pair(grid_view, frozen):
    lower_cells = jnp.concatenate(
        [grid_view[..., :1] * (1.0 - frozen)[None, :, :, None], grid_view[..., :-1]], axis=-1
    )
    upper_cells = jnp.concatenate([grid_view[..., 1:], jnp.zeros_like(grid_view[..., :1])], axis=-1)
    return lower_cells + upper_cells


def neighbour_terms(grid_view, x_low, x_high, y_low, y_high, viscosity, frozen):
    shape = grid_view.shape
    y_pad = jnp.concatenate([y_low, grid_view, y_high], axis=2)
    if x_low is None:
        along_line = 2.0 * grid_view
    else:
        x_pad = jnp.concatenate([x_low, grid_view, x_high], axis=1)
        along_line = 2.0 * grid_view - x_pad[:, :-2] - x_pad[:, 2:]
    across_line = y_pad[:, :, :-2] + y_pad[:, :, 2:] + vertical_pair(grid_view, frozen)
    flat = (3, shape[1], shape[2] * shape[3])
    return viscosity * along_line.reshape(flat) - coupling * viscosity * across_line.reshape(flat)


def in_cell_terms(masked, matrix):
    return jnp.sum(matrix * masked[None], axis=1)


def gather_rows(block, axis):
    count, mine = (lax.axis_size(axis), lax.axis_index(axis))
    if count > 8:
        return lax.all_gather(block, axis, axis=1, tiled=True)
    pieces = [block]
    for step in range(1, count):
        pairs = [((i + step) % count, i) for i in range(count)]
        pieces.append(lax.ppermute(block, axis, pairs))
    stacked = jnp.stack(pieces + pieces, axis=0)
    ordered = lax.dynamic_slice_in_dim(stacked, count - mine, count, axis=0)
    ordered = jnp.moveaxis(ordered, 0, 1)
    return ordered.reshape(block.shape[0], count * block.shape[1], *block.shape[2:])


def line_solve(line_lead, line_off, line_rhs):
    rows = line_lead.shape[1]
    gain_prev = jnp.zeros_like(line_rhs[:, 0])
    value_prev = jnp.zeros_like(line_rhs[:, 0])
    gains, values = [], []
    for cell_idx in range(rows):
        off_cell = line_off[:, cell_idx]
        pivot = line_lead[:, cell_idx] - off_cell * gain_prev
        gain_prev = off_cell / pivot
        value_prev = (line_rhs[:, cell_idx] + off_cell * value_prev) / pivot
        gains.append(gain_prev)
        values.append(value_prev)
    next_value = jnp.zeros_like(line_rhs[:, 0])
    corrections = list(values)
    for cell_idx in reversed(range(rows)):
        next_value = values[cell_idx] + gains[cell_idx] * next_value
        corrections[cell_idx] = next_value
    return jnp.stack(corrections, axis=1)


def line_solve_scan(line_lead, line_off, line_rhs):
    def sweep_down(carried, cell_cols):
        gain_prev, value_prev = carried
        lead_cell, off_cell, rhs_cell = cell_cols
        pivot = lead_cell - off_cell * gain_prev
        gain = off_cell / pivot
        value = (rhs_cell + off_cell * value_prev) / pivot
        return (gain, value), (gain, value)

    zeros_line = jnp.zeros_like(line_rhs[:, 0])
    scanned = (jnp.moveaxis(line_lead, 1, 0), jnp.moveaxis(line_off, 1, 0), jnp.moveaxis(line_rhs, 1, 0))
    _, (gains, values) = lax.scan(sweep_down, (zeros_line, zeros_line), scanned)

    def sweep_up(next_value, cell_cols):
        gain, value = cell_cols
        solved = value + gain * next_value
        return solved, solved

    _, corrections = lax.scan(sweep_up, zeros_line, (gains, values), reverse=True)
    return jnp.moveaxis(corrections, 0, 1)


def tree_sum(value, axis):
    count = lax.axis_size(axis)
    if count & (count - 1):
        return lax.psum(value, axis)
    step = 1
    while step < count:
        value = value + lax.ppermute(value, axis, [(i, i ^ step) for i in range(count)])
        step *= 2
    return value


def local(solution, forcing, viscosity, blocks, layer_count, bed_frozen, basin_map):
    row_count = solution.shape[1]
    lane_count = solution.shape[2]
    y_cells = lane_count // LAYERS
    layer_idx = jnp.arange(LAYERS, dtype=jnp.int32)
    active = (
        (layer_idx[None, None, :] < layer_count[:, :, None])
        .astype(jnp.float32)
        .reshape(row_count, lane_count)
    )
    frozen = bed_frozen.astype(jnp.float32)
    matrix = blocks.reshape(4, 4, row_count, lane_count)
    grid = (3, row_count, y_cells, LAYERS)

    masked = solution * active[None]
    masked_grid = masked[:3].reshape(grid)
    weight_grid = (coupling * viscosity * active).reshape(1, row_count, y_cells, LAYERS)
    basin_grid = jnp.broadcast_to(
        basin_map.astype(jnp.float32)[None, :, :, None], (1, row_count, y_cells, LAYERS)
    )
    halo_source = jnp.concatenate([masked_grid, weight_grid, basin_grid], axis=0)
    from_low, from_high = neighbour_shift(halo_source, "gy", 2, 1)
    y_low, y_high = from_low[:3], from_high[:3]
    in_cell = in_cell_terms(masked, matrix)
    moving = in_cell[:3] + neighbour_terms(masked_grid, None, None, y_low, y_high, viscosity, frozen)
    residual = active[None] * (forcing - jnp.concatenate([moving, in_cell[3:]], axis=0))

    diagonal = jnp.stack([matrix[0, 0], matrix[1, 1], matrix[2, 2]])
    line_lead = jnp.where(active[None] > 0.0, diagonal + 2.0 * viscosity[None], 1.0)
    line_off = (viscosity * active)[None]
    packed = jnp.concatenate([line_lead, line_off, residual[:3], masked[:3]], axis=0)
    whole = gather_rows(packed, "gx")
    all_rows = whole.shape[1]
    whole_off = whole[3:4]
    padded_masked = jnp.pad(whole[7:10], ((0, 0), (1, 1), (0, 0)))
    whole_rhs = whole[4:7] + whole_off * (padded_masked[:, :-2] + padded_masked[:, 2:])
    solver = line_solve if all_rows <= 32 else line_solve_scan
    whole_corr = solver(whole[0:3], jnp.broadcast_to(whole_off, whole_rhs.shape), whole_rhs)

    first = lax.axis_index("gx") * row_count
    padded_corr = jnp.pad(whole_corr, ((0, 0), (1, 1), (0, 0)))
    near_corr = lax.dynamic_slice_in_dim(padded_corr, first, row_count + 2, axis=1)
    near_masked = lax.dynamic_slice_in_dim(padded_masked, first, row_count + 2, axis=1)
    correction = near_corr[:, 1:-1]

    pressure_in = residual[3] - (
        matrix[3, 0] * correction[0] + matrix[3, 1] * correction[1] + matrix[3, 2] * correction[2]
    )
    pressure_step = active * pressure_in / viscosity
    full_step = jnp.concatenate([correction, pressure_step[None]], axis=0)
    smoothed = solution + full_step

    smoothed_masked = smoothed * active[None]
    sm_grid = smoothed_masked[:3].reshape(grid)
    edge = (3, 1, y_cells, LAYERS)
    x_low2 = (near_masked[:, :1] + near_corr[:, :1]).reshape(edge)
    x_high2 = (near_masked[:, -1:] + near_corr[:, -1:]).reshape(edge)
    no_cols = jnp.zeros((3, row_count, 1, LAYERS), jnp.float32)
    in_cell2 = in_cell_terms(smoothed_masked, matrix)
    moving2 = in_cell2[:3] + neighbour_terms(sm_grid, x_low2, x_high2, no_cols, no_cols, viscosity, frozen)
    post = active[None] * (forcing - jnp.concatenate([moving2, in_cell2[3:]], axis=0))
    column_local = jnp.sum(post.reshape(4, row_count, y_cells, LAYERS), axis=-1)

    to_low = jnp.sum(from_low[3:4, :, 0] * sm_grid[:, :, 0], axis=-1)
    to_high = jnp.sum(from_high[3:4, :, 0] * sm_grid[:, :, -1], axis=-1)
    edge_terms = jnp.zeros((3, row_count, y_cells), jnp.float32)
    count = lax.axis_size("gy")
    if count != 4:
        forward = [(i, i + 1) for i in range(count - 1)]
        backward = [(target, source) for source, target in forward]
        for_last = lax.ppermute(to_low, "gy", backward)
        for_first = lax.ppermute(to_high, "gy", forward)
        edge_terms = edge_terms.at[:, :, 0].set(for_first).at[:, :, -1].set(for_last)
        column_residual = column_local + jnp.pad(edge_terms, ((0, 1), (0, 0), (0, 0)))
    basin_count = lax.axis_size("gx") // 2 * lax.axis_size("gy")
    basin_ids = jnp.arange(basin_count, dtype=jnp.int32)
    member = basin_map.reshape(-1)[:, None] == basin_ids[None, :]
    partial_sums = jnp.sum(jnp.where(member[None], column_local.reshape(4, -1)[:, :, None], 0.0), axis=1)
    beside_ids = jnp.concatenate([from_low[4, :, 0, 0], from_high[4, :, 0, 0]]).astype(jnp.int32)
    beside_member = beside_ids[:, None] == basin_ids[None, :]
    beside_terms = jnp.concatenate([to_low, to_high], axis=1)
    beside_sums = jnp.sum(jnp.where(beside_member[None], beside_terms[:, :, None], 0.0), axis=1)
    partial_sums = partial_sums + jnp.pad(beside_sums, ((0, 1), (0, 0)))
    basin_sums = tree_sum(partial_sums, "gx")
    if count != 4:
        basin_residual = tree_sum(basin_sums, "gy")
    else:
        mine = lax.axis_index("gy")
        first_term = jnp.zeros_like(to_low)
        last_term = jnp.zeros_like(to_low)
        for parity, pairs in ((0, [(0, 1), (1, 0), (2, 3), (3, 2)]), (1, [(1, 2), (2, 1), (3, 0), (0, 3)])):
            sends_high = mine % 2 == parity
            edge_out = jnp.where(sends_high, to_high, to_low)
            message = jnp.concatenate([basin_sums, jnp.pad(edge_out, ((0, 1), (0, 0)))], axis=1)
            got = lax.ppermute(message, "gy", pairs)
            basin_sums = basin_sums + got[:, :basin_count]
            edge_in = got[:3, basin_count:]
            last_term = jnp.where(sends_high, edge_in, last_term)
            first_term = jnp.where(sends_high, first_term, edge_in)
        basin_residual = basin_sums
        column_residual = column_local.at[:3, :, 0].add(first_term).at[:3, :, -1].add(last_term)
    return (smoothed, column_residual, basin_residual)


def solution(mesh):
    return jax.shard_map(
        local,
        mesh=mesh,
        in_specs=(
            P(None, "gx", "gy"),
            P(None, "gx", "gy"),
            P("gx", "gy"),
            P(None, "gx", "gy"),
            P("gx", "gy"),
            P("gx", "gy"),
            P("gx", "gy"),
        ),
        out_specs=(P(None, "gx", "gy"), P(None, "gx", "gy"), P()),
        check_vma=False,
    )
```

```python
import jax
import jax.numpy as jnp
from jax import lax
from jax.sharding import PartitionSpec as P

LAYERS = 80


coupling = 0.25


def neighbour_shift(block, axis, dim, width):
    count = lax.axis_size(axis)
    forward = [(i, i + 1) for i in range(count - 1)]
    backward = [(target, source) for source, target in forward]
    low = lax.ppermute(lax.slice_in_dim(block, block.shape[dim] - width, None, axis=dim), axis, forward)
    high = lax.ppermute(lax.slice_in_dim(block, 0, width, axis=dim), axis, backward)
    return low, high


def vertical_pair(grid_view, frozen):
    lower_cells = jnp.concatenate(
        [grid_view[..., :1] * (1.0 - frozen)[None, :, :, None], grid_view[..., :-1]], axis=-1
    )
    upper_cells = jnp.concatenate([grid_view[..., 1:], jnp.zeros_like(grid_view[..., :1])], axis=-1)
    return lower_cells + upper_cells


def neighbour_terms(grid_view, x_low, x_high, y_low, y_high, viscosity, frozen):
    shape = grid_view.shape
    y_pad = jnp.concatenate([y_low, grid_view, y_high], axis=2)
    if x_low is None:
        along_line = 2.0 * grid_view
    else:
        x_pad = jnp.concatenate([x_low, grid_view, x_high], axis=1)
        along_line = 2.0 * grid_view - x_pad[:, :-2] - x_pad[:, 2:]
    across_line = y_pad[:, :, :-2] + y_pad[:, :, 2:] + vertical_pair(grid_view, frozen)
    flat = (3, shape[1], shape[2] * shape[3])
    return viscosity * along_line.reshape(flat) - coupling * viscosity * across_line.reshape(flat)


def in_cell_terms(masked, matrix):
    return jnp.sum(matrix * masked[None], axis=1)


def gather_rows(block, axis):
    count, mine = (lax.axis_size(axis), lax.axis_index(axis))
    if count > 8:
        return lax.all_gather(block, axis, axis=1, tiled=True)
    if count % 2 == 0:
        partner = lax.ppermute(block, axis, [(i, i ^ 1) for i in range(count)])
        block = jnp.where(
            mine % 2 == 0,
            jnp.concatenate([block, partner], axis=1),
            jnp.concatenate([partner, block], axis=1),
        )
        groups, mine = (count // 2, mine // 2)
    else:
        groups = count
    pieces = [block]
    for step in range(1, groups):
        if count % 2 == 0:
            pairs = [(((g + step) % groups) * 2 + x, g * 2 + x) for g in range(groups) for x in range(2)]
        else:
            pairs = [((i + step) % count, i) for i in range(count)]
        pieces.append(lax.ppermute(block, axis, pairs))
    stacked = jnp.stack(pieces + pieces, axis=0)
    ordered = lax.dynamic_slice_in_dim(stacked, groups - mine, groups, axis=0)
    ordered = jnp.moveaxis(ordered, 0, 1)
    return ordered.reshape(block.shape[0], groups * block.shape[1], *block.shape[2:])


def line_solve(line_lead, line_off, line_rhs):
    rows = line_lead.shape[1]
    gain_prev = jnp.zeros_like(line_rhs[:, 0])
    value_prev = jnp.zeros_like(line_rhs[:, 0])
    gains, values = [], []
    for cell_idx in range(rows):
        off_cell = line_off[:, cell_idx]
        pivot = line_lead[:, cell_idx] - off_cell * gain_prev
        gain_prev = off_cell / pivot
        value_prev = (line_rhs[:, cell_idx] + off_cell * value_prev) / pivot
        gains.append(gain_prev)
        values.append(value_prev)
    next_value = jnp.zeros_like(line_rhs[:, 0])
    corrections = list(values)
    for cell_idx in reversed(range(rows)):
        next_value = values[cell_idx] + gains[cell_idx] * next_value
        corrections[cell_idx] = next_value
    return jnp.stack(corrections, axis=1)


def line_solve_scan(line_lead, line_off, line_rhs):
    def sweep_down(carried, cell_cols):
        gain_prev, value_prev = carried
        lead_cell, off_cell, rhs_cell = cell_cols
        pivot = lead_cell - off_cell * gain_prev
        gain = off_cell / pivot
        value = (rhs_cell + off_cell * value_prev) / pivot
        return (gain, value), (gain, value)

    zeros_line = jnp.zeros_like(line_rhs[:, 0])
    scanned = (jnp.moveaxis(line_lead, 1, 0), jnp.moveaxis(line_off, 1, 0), jnp.moveaxis(line_rhs, 1, 0))
    _, (gains, values) = lax.scan(sweep_down, (zeros_line, zeros_line), scanned)

    def sweep_up(next_value, cell_cols):
        gain, value = cell_cols
        solved = value + gain * next_value
        return solved, solved

    _, corrections = lax.scan(sweep_up, zeros_line, (gains, values), reverse=True)
    return jnp.moveaxis(corrections, 0, 1)


def tree_sum(value, axis):
    count = lax.axis_size(axis)
    if count & (count - 1):
        return lax.psum(value, axis)
    step = 1
    while step < count:
        value = value + lax.ppermute(value, axis, [(i, i ^ step) for i in range(count)])
        step *= 2
    return value


def local(solution, forcing, viscosity, blocks, layer_count, bed_frozen, basin_map):
    row_count = solution.shape[1]
    lane_count = solution.shape[2]
    y_cells = lane_count // LAYERS
    layer_idx = jnp.arange(LAYERS, dtype=jnp.int32)
    active = (
        (layer_idx[None, None, :] < layer_count[:, :, None])
        .astype(jnp.float32)
        .reshape(row_count, lane_count)
    )
    frozen = bed_frozen.astype(jnp.float32)
    matrix = blocks.reshape(4, 4, row_count, lane_count)
    grid = (3, row_count, y_cells, LAYERS)

    masked = solution * active[None]
    masked_grid = masked[:3].reshape(grid)
    weight_grid = (coupling * viscosity * active).reshape(1, row_count, y_cells, LAYERS)
    basin_grid = jnp.broadcast_to(
        basin_map.astype(jnp.float32)[None, :, :, None], (1, row_count, y_cells, LAYERS)
    )
    halo_source = jnp.concatenate([masked_grid, weight_grid, basin_grid], axis=0)
    from_low, from_high = neighbour_shift(halo_source, "gy", 2, 1)
    y_low, y_high = from_low[:3], from_high[:3]
    in_cell = in_cell_terms(masked, matrix)
    moving = in_cell[:3] + neighbour_terms(masked_grid, None, None, y_low, y_high, viscosity, frozen)
    residual = active[None] * (forcing - jnp.concatenate([moving, in_cell[3:]], axis=0))

    diagonal = jnp.stack([matrix[0, 0], matrix[1, 1], matrix[2, 2]])
    line_lead = jnp.where(active[None] > 0.0, diagonal + 2.0 * viscosity[None], 1.0)
    line_off = (viscosity * active)[None]
    packed = jnp.concatenate([line_lead, line_off, residual[:3], masked[:3]], axis=0)
    whole = gather_rows(packed, "gx")
    all_rows = whole.shape[1]
    whole_off = whole[3:4]
    padded_masked = jnp.pad(whole[7:10], ((0, 0), (1, 1), (0, 0)))
    whole_rhs = whole[4:7] + whole_off * (padded_masked[:, :-2] + padded_masked[:, 2:])
    solver = line_solve if all_rows <= 32 else line_solve_scan
    whole_corr = solver(whole[0:3], jnp.broadcast_to(whole_off, whole_rhs.shape), whole_rhs)

    first = lax.axis_index("gx") * row_count
    padded_corr = jnp.pad(whole_corr, ((0, 0), (1, 1), (0, 0)))
    near_corr = lax.dynamic_slice_in_dim(padded_corr, first, row_count + 2, axis=1)
    near_masked = lax.dynamic_slice_in_dim(padded_masked, first, row_count + 2, axis=1)
    correction = near_corr[:, 1:-1]

    pressure_in = residual[3] - (
        matrix[3, 0] * correction[0] + matrix[3, 1] * correction[1] + matrix[3, 2] * correction[2]
    )
    pressure_step = active * pressure_in / viscosity
    full_step = jnp.concatenate([correction, pressure_step[None]], axis=0)
    smoothed = solution + full_step

    smoothed_masked = smoothed * active[None]
    sm_grid = smoothed_masked[:3].reshape(grid)
    edge = (3, 1, y_cells, LAYERS)
    x_low2 = (near_masked[:, :1] + near_corr[:, :1]).reshape(edge)
    x_high2 = (near_masked[:, -1:] + near_corr[:, -1:]).reshape(edge)
    no_cols = jnp.zeros((3, row_count, 1, LAYERS), jnp.float32)
    in_cell2 = in_cell_terms(smoothed_masked, matrix)
    moving2 = in_cell2[:3] + neighbour_terms(sm_grid, x_low2, x_high2, no_cols, no_cols, viscosity, frozen)
    post = active[None] * (forcing - jnp.concatenate([moving2, in_cell2[3:]], axis=0))
    column_local = jnp.sum(post.reshape(4, row_count, y_cells, LAYERS), axis=-1)

    to_low = jnp.sum(from_low[3:4, :, 0] * sm_grid[:, :, 0], axis=-1)
    to_high = jnp.sum(from_high[3:4, :, 0] * sm_grid[:, :, -1], axis=-1)
    edge_terms = jnp.zeros((3, row_count, y_cells), jnp.float32)
    count = lax.axis_size("gy")
    if count != 4:
        forward = [(i, i + 1) for i in range(count - 1)]
        backward = [(target, source) for source, target in forward]
        for_last = lax.ppermute(to_low, "gy", backward)
        for_first = lax.ppermute(to_high, "gy", forward)
        edge_terms = edge_terms.at[:, :, 0].set(for_first).at[:, :, -1].set(for_last)
        column_residual = column_local + jnp.pad(edge_terms, ((0, 1), (0, 0), (0, 0)))
    basin_count = lax.axis_size("gx") // 2 * lax.axis_size("gy")
    basin_ids = jnp.arange(basin_count, dtype=jnp.int32)
    member = basin_map.reshape(-1)[:, None] == basin_ids[None, :]
    partial_sums = jnp.sum(jnp.where(member[None], column_local.reshape(4, -1)[:, :, None], 0.0), axis=1)
    beside_ids = jnp.concatenate([from_low[4, :, 0, 0], from_high[4, :, 0, 0]]).astype(jnp.int32)
    beside_member = beside_ids[:, None] == basin_ids[None, :]
    beside_terms = jnp.concatenate([to_low, to_high], axis=1)
    beside_sums = jnp.sum(jnp.where(beside_member[None], beside_terms[:, :, None], 0.0), axis=1)
    partial_sums = partial_sums + jnp.pad(beside_sums, ((0, 1), (0, 0)))
    basin_sums = tree_sum(partial_sums, "gx")
    if count != 4:
        basin_residual = tree_sum(basin_sums, "gy")
    else:
        mine = lax.axis_index("gy")
        for pairs in ([(0, 1), (1, 0), (2, 3), (3, 2)], [(1, 2), (2, 1), (3, 0), (0, 3)]):
            sends_high = jnp.array([b == (a + 1) % 4 for a, b in sorted(pairs)])[mine]
            edge_out = jnp.where(sends_high, to_high, to_low)
            message = jnp.concatenate([basin_sums, jnp.pad(edge_out.reshape(3, -1), ((0, 1), (0, 0)))], axis=1)
            got = lax.ppermute(message, "gy", pairs)
            basin_sums = basin_sums + got[:, :basin_count]
            edge_in = got[:3, basin_count:].reshape(3, row_count)
            edge_terms = jnp.where(
                sends_high,
                edge_terms.at[:, :, -1].set(edge_in),
                edge_terms.at[:, :, 0].set(edge_in),
            )
        basin_residual = basin_sums
        column_residual = column_local + jnp.pad(edge_terms, ((0, 1), (0, 0), (0, 0)))
    return (smoothed, column_residual, basin_residual)


def solution(mesh):
    return jax.shard_map(
        local,
        mesh=mesh,
        in_specs=(
            P(None, "gx", "gy"),
            P(None, "gx", "gy"),
            P("gx", "gy"),
            P(None, "gx", "gy"),
            P("gx", "gy"),
            P("gx", "gy"),
            P("gx", "gy"),
        ),
        out_specs=(P(None, "gx", "gy"), P(None, "gx", "gy"), P()),
        check_vma=False,
    )
```

```python
import jax
import jax.numpy as jnp
from jax import lax
from jax.sharding import PartitionSpec as P

LAYERS = 80


coupling = 0.25


def neighbour_shift(block, axis, dim, width):
    count = lax.axis_size(axis)
    forward = [(i, i + 1) for i in range(count - 1)]
    backward = [(target, source) for source, target in forward]
    low = lax.ppermute(lax.slice_in_dim(block, block.shape[dim] - width, None, axis=dim), axis, forward)
    high = lax.ppermute(lax.slice_in_dim(block, 0, width, axis=dim), axis, backward)
    return low, high


def vertical_pair(grid_view, frozen):
    lower_cells = jnp.concatenate(
        [grid_view[..., :1] * (1.0 - frozen)[None, :, :, None], grid_view[..., :-1]], axis=-1
    )
    upper_cells = jnp.concatenate([grid_view[..., 1:], jnp.zeros_like(grid_view[..., :1])], axis=-1)
    return lower_cells + upper_cells


def neighbour_terms(grid_view, x_low, x_high, y_low, y_high, viscosity, frozen):
    shape = grid_view.shape
    y_pad = jnp.concatenate([y_low, grid_view, y_high], axis=2)
    if x_low is None:
        along_line = 2.0 * grid_view
    else:
        x_pad = jnp.concatenate([x_low, grid_view, x_high], axis=1)
        along_line = 2.0 * grid_view - x_pad[:, :-2] - x_pad[:, 2:]
    across_line = y_pad[:, :, :-2] + y_pad[:, :, 2:] + vertical_pair(grid_view, frozen)
    flat = (3, shape[1], shape[2] * shape[3])
    return viscosity * along_line.reshape(flat) - coupling * viscosity * across_line.reshape(flat)


def in_cell_terms(masked, matrix):
    return jnp.sum(matrix * masked[None], axis=1)


def gather_rows(block, axis):
    count, mine = (lax.axis_size(axis), lax.axis_index(axis))
    if count > 8:
        return lax.all_gather(block, axis, axis=1, tiled=True)
    pieces = [block]
    for step in range(1, count):
        pairs = [((i + step) % count, i) for i in range(count)]
        pieces.append(lax.ppermute(block, axis, pairs))
    stacked = jnp.stack(pieces + pieces, axis=0)
    ordered = lax.dynamic_slice_in_dim(stacked, count - mine, count, axis=0)
    ordered = jnp.moveaxis(ordered, 0, 1)
    return ordered.reshape(block.shape[0], count * block.shape[1], *block.shape[2:])


def line_solve(line_lead, line_off, line_rhs):
    rows = line_lead.shape[1]
    gain_prev = jnp.zeros_like(line_rhs[:, 0])
    value_prev = jnp.zeros_like(line_rhs[:, 0])
    gains, values = [], []
    for cell_idx in range(rows):
        off_cell = line_off[:, cell_idx]
        pivot = line_lead[:, cell_idx] - off_cell * gain_prev
        gain_prev = off_cell / pivot
        value_prev = (line_rhs[:, cell_idx] + off_cell * value_prev) / pivot
        gains.append(gain_prev)
        values.append(value_prev)
    next_value = jnp.zeros_like(line_rhs[:, 0])
    corrections = list(values)
    for cell_idx in reversed(range(rows)):
        next_value = values[cell_idx] + gains[cell_idx] * next_value
        corrections[cell_idx] = next_value
    return jnp.stack(corrections, axis=1)


def line_solve_scan(line_lead, line_off, line_rhs):
    def sweep_down(carried, cell_cols):
        gain_prev, value_prev = carried
        lead_cell, off_cell, rhs_cell = cell_cols
        pivot = lead_cell - off_cell * gain_prev
        gain = off_cell / pivot
        value = (rhs_cell + off_cell * value_prev) / pivot
        return (gain, value), (gain, value)

    zeros_line = jnp.zeros_like(line_rhs[:, 0])
    scanned = (jnp.moveaxis(line_lead, 1, 0), jnp.moveaxis(line_off, 1, 0), jnp.moveaxis(line_rhs, 1, 0))
    _, (gains, values) = lax.scan(sweep_down, (zeros_line, zeros_line), scanned)

    def sweep_up(next_value, cell_cols):
        gain, value = cell_cols
        solved = value + gain * next_value
        return solved, solved

    _, corrections = lax.scan(sweep_up, zeros_line, (gains, values), reverse=True)
    return jnp.moveaxis(corrections, 0, 1)


def tree_sum(value, axis):
    count = lax.axis_size(axis)
    if count & (count - 1):
        return lax.psum(value, axis)
    step = 1
    while step < count:
        value = value + lax.ppermute(value, axis, [(i, i ^ step) for i in range(count)])
        step *= 2
    return value


def local(solution, forcing, viscosity, blocks, layer_count, bed_frozen, basin_map):
    row_count = solution.shape[1]
    lane_count = solution.shape[2]
    y_cells = lane_count // LAYERS
    layer_idx = jnp.arange(LAYERS, dtype=jnp.int32)
    active = (
        (layer_idx[None, None, :] < layer_count[:, :, None])
        .astype(jnp.float32)
        .reshape(row_count, lane_count)
    )
    frozen = bed_frozen.astype(jnp.float32)
    matrix = blocks.reshape(4, 4, row_count, lane_count)
    grid = (3, row_count, y_cells, LAYERS)

    masked = solution * active[None]
    masked_grid = masked[:3].reshape(grid)
    weight_grid = (coupling * viscosity * active).reshape(1, row_count, y_cells, LAYERS)
    basin_grid = jnp.broadcast_to(
        basin_map.astype(jnp.float32)[None, :, :, None], (1, row_count, y_cells, LAYERS)
    )
    halo_source = jnp.concatenate([masked_grid, weight_grid, basin_grid], axis=0)
    from_low, from_high = neighbour_shift(halo_source, "gy", 2, 1)
    y_low, y_high = from_low[:3], from_high[:3]
    x_low, x_high = neighbour_shift(masked_grid, "gx", 1, 1)
    in_cell = in_cell_terms(masked, matrix)
    moving = in_cell[:3] + neighbour_terms(masked_grid, x_low, x_high, y_low, y_high, viscosity, frozen)
    residual = active[None] * (forcing - jnp.concatenate([moving, in_cell[3:]], axis=0))

    diagonal = jnp.stack([matrix[0, 0], matrix[1, 1], matrix[2, 2]])
    line_lead = jnp.where(active[None] > 0.0, diagonal + 2.0 * viscosity[None], 1.0)
    line_off = (viscosity * active)[None]
    packed = jnp.concatenate([line_lead, line_off, residual[:3]], axis=0)
    whole = gather_rows(packed, "gx")
    all_rows = whole.shape[1]
    whole_rhs = whole[4:7]
    solver = line_solve if all_rows <= 32 else line_solve_scan
    whole_corr = solver(whole[0:3], jnp.broadcast_to(whole[3:4], whole_rhs.shape), whole_rhs)

    first = lax.axis_index("gx") * row_count
    padded_corr = jnp.pad(whole_corr, ((0, 0), (1, 1), (0, 0)))
    near_corr = lax.dynamic_slice_in_dim(padded_corr, first, row_count + 2, axis=1)
    correction = near_corr[:, 1:-1]

    pressure_in = residual[3] - (
        matrix[3, 0] * correction[0] + matrix[3, 1] * correction[1] + matrix[3, 2] * correction[2]
    )
    pressure_step = active * pressure_in / viscosity
    full_step = jnp.concatenate([correction, pressure_step[None]], axis=0)
    smoothed = solution + full_step

    smoothed_masked = smoothed * active[None]
    sm_grid = smoothed_masked[:3].reshape(grid)
    edge = (3, 1, y_cells, LAYERS)
    x_low2 = x_low + near_corr[:, :1].reshape(edge)
    x_high2 = x_high + near_corr[:, -1:].reshape(edge)
    no_cols = jnp.zeros((3, row_count, 1, LAYERS), jnp.float32)
    in_cell2 = in_cell_terms(smoothed_masked, matrix)
    moving2 = in_cell2[:3] + neighbour_terms(sm_grid, x_low2, x_high2, no_cols, no_cols, viscosity, frozen)
    post = active[None] * (forcing - jnp.concatenate([moving2, in_cell2[3:]], axis=0))
    column_local = jnp.sum(post.reshape(4, row_count, y_cells, LAYERS), axis=-1)

    to_low = jnp.sum(from_low[3:4, :, 0] * sm_grid[:, :, 0], axis=-1)
    to_high = jnp.sum(from_high[3:4, :, 0] * sm_grid[:, :, -1], axis=-1)
    edge_terms = jnp.zeros((3, row_count, y_cells), jnp.float32)
    count = lax.axis_size("gy")
    if count != 4:
        forward = [(i, i + 1) for i in range(count - 1)]
        backward = [(target, source) for source, target in forward]
        for_last = lax.ppermute(to_low, "gy", backward)
        for_first = lax.ppermute(to_high, "gy", forward)
        edge_terms = edge_terms.at[:, :, 0].set(for_first).at[:, :, -1].set(for_last)
        column_residual = column_local + jnp.pad(edge_terms, ((0, 1), (0, 0), (0, 0)))
    basin_count = lax.axis_size("gx") // 2 * lax.axis_size("gy")
    basin_ids = jnp.arange(basin_count, dtype=jnp.int32)
    member = basin_map.reshape(-1)[:, None] == basin_ids[None, :]
    partial_sums = jnp.sum(jnp.where(member[None], column_local.reshape(4, -1)[:, :, None], 0.0), axis=1)
    beside_ids = jnp.concatenate([from_low[4, :, 0, 0], from_high[4, :, 0, 0]]).astype(jnp.int32)
    beside_member = beside_ids[:, None] == basin_ids[None, :]
    beside_terms = jnp.concatenate([to_low, to_high], axis=1)
    beside_sums = jnp.sum(jnp.where(beside_member[None], beside_terms[:, :, None], 0.0), axis=1)
    partial_sums = partial_sums + jnp.pad(beside_sums, ((0, 1), (0, 0)))
    basin_sums = tree_sum(partial_sums, "gx")
    if count != 4:
        basin_residual = tree_sum(basin_sums, "gy")
    else:
        mine = lax.axis_index("gy")
        for pairs in ([(0, 1), (1, 0), (2, 3), (3, 2)], [(1, 2), (2, 1), (3, 0), (0, 3)]):
            sends_high = jnp.array([b == (a + 1) % 4 for a, b in sorted(pairs)])[mine]
            edge_out = jnp.where(sends_high, to_high, to_low)
            message = jnp.concatenate([basin_sums, jnp.pad(edge_out.reshape(3, -1), ((0, 1), (0, 0)))], axis=1)
            got = lax.ppermute(message, "gy", pairs)
            basin_sums = basin_sums + got[:, :basin_count]
            edge_in = got[:3, basin_count:].reshape(3, row_count)
            edge_terms = jnp.where(
                sends_high,
                edge_terms.at[:, :, -1].set(edge_in),
                edge_terms.at[:, :, 0].set(edge_in),
            )
        basin_residual = basin_sums
        column_residual = column_local + jnp.pad(edge_terms, ((0, 1), (0, 0), (0, 0)))
    return (smoothed, column_residual, basin_residual)


def solution(mesh):
    return jax.shard_map(
        local,
        mesh=mesh,
        in_specs=(
            P(None, "gx", "gy"),
            P(None, "gx", "gy"),
            P("gx", "gy"),
            P(None, "gx", "gy"),
            P("gx", "gy"),
            P("gx", "gy"),
            P("gx", "gy"),
        ),
        out_specs=(P(None, "gx", "gy"), P(None, "gx", "gy"), P()),
        check_vma=False,
    )
```

```python
import jax
import jax.numpy as jnp
from jax import lax
from jax.sharding import PartitionSpec as P

LAYERS = 80


coupling = 0.25


def neighbour_shift(block, axis, dim, width):
    count = lax.axis_size(axis)
    forward = [(i, i + 1) for i in range(count - 1)]
    backward = [(target, source) for source, target in forward]
    low = lax.ppermute(lax.slice_in_dim(block, block.shape[dim] - width, None, axis=dim), axis, forward)
    high = lax.ppermute(lax.slice_in_dim(block, 0, width, axis=dim), axis, backward)
    return low, high


def vertical_pair(grid_view, frozen):
    lower_cells = jnp.concatenate(
        [grid_view[..., :1] * (1.0 - frozen)[None, :, :, None], grid_view[..., :-1]], axis=-1
    )
    upper_cells = jnp.concatenate([grid_view[..., 1:], jnp.zeros_like(grid_view[..., :1])], axis=-1)
    return lower_cells + upper_cells


def neighbour_terms(grid_view, x_low, x_high, y_low, y_high, viscosity, frozen):
    shape = grid_view.shape
    y_pad = jnp.concatenate([y_low, grid_view, y_high], axis=2)
    if x_low is None:
        along_line = 2.0 * grid_view
    else:
        x_pad = jnp.concatenate([x_low, grid_view, x_high], axis=1)
        along_line = 2.0 * grid_view - x_pad[:, :-2] - x_pad[:, 2:]
    across_line = y_pad[:, :, :-2] + y_pad[:, :, 2:] + vertical_pair(grid_view, frozen)
    flat = (3, shape[1], shape[2] * shape[3])
    return viscosity * along_line.reshape(flat) - coupling * viscosity * across_line.reshape(flat)


def in_cell_terms(masked, matrix):
    return jnp.sum(matrix * masked[None], axis=1)


def gather_rows(block, axis):
    count, mine = (lax.axis_size(axis), lax.axis_index(axis))
    if count > 8:
        return lax.all_gather(block, axis, axis=1, tiled=True)
    pieces = [block]
    for step in range(1, count):
        pairs = [((i + step) % count, i) for i in range(count)]
        pieces.append(lax.ppermute(block, axis, pairs))
    stacked = jnp.stack(pieces + pieces, axis=0)
    ordered = lax.dynamic_slice_in_dim(stacked, count - mine, count, axis=0)
    ordered = jnp.moveaxis(ordered, 0, 1)
    return ordered.reshape(block.shape[0], count * block.shape[1], *block.shape[2:])


def line_solve(line_lead, line_off, line_rhs):
    rows = line_lead.shape[1]
    gain_prev = jnp.zeros_like(line_rhs[:, 0])
    value_prev = jnp.zeros_like(line_rhs[:, 0])
    gains, values = [], []
    for cell_idx in range(rows):
        off_cell = line_off[:, cell_idx]
        pivot = line_lead[:, cell_idx] - off_cell * gain_prev
        gain_prev = off_cell / pivot
        value_prev = (line_rhs[:, cell_idx] + off_cell * value_prev) / pivot
        gains.append(gain_prev)
        values.append(value_prev)
    next_value = jnp.zeros_like(line_rhs[:, 0])
    corrections = list(values)
    for cell_idx in reversed(range(rows)):
        next_value = values[cell_idx] + gains[cell_idx] * next_value
        corrections[cell_idx] = next_value
    return jnp.stack(corrections, axis=1)


def line_solve_scan(line_lead, line_off, line_rhs):
    def sweep_down(carried, cell_cols):
        gain_prev, value_prev = carried
        lead_cell, off_cell, rhs_cell = cell_cols
        pivot = lead_cell - off_cell * gain_prev
        gain = off_cell / pivot
        value = (rhs_cell + off_cell * value_prev) / pivot
        return (gain, value), (gain, value)

    zeros_line = jnp.zeros_like(line_rhs[:, 0])
    scanned = (jnp.moveaxis(line_lead, 1, 0), jnp.moveaxis(line_off, 1, 0), jnp.moveaxis(line_rhs, 1, 0))
    _, (gains, values) = lax.scan(sweep_down, (zeros_line, zeros_line), scanned)

    def sweep_up(next_value, cell_cols):
        gain, value = cell_cols
        solved = value + gain * next_value
        return solved, solved

    _, corrections = lax.scan(sweep_up, zeros_line, (gains, values), reverse=True)
    return jnp.moveaxis(corrections, 0, 1)


def tree_sum(value, axis):
    count = lax.axis_size(axis)
    if count & (count - 1):
        return lax.psum(value, axis)
    step = 1
    while step < count:
        value = value + lax.ppermute(value, axis, [(i, i ^ step) for i in range(count)])
        step *= 2
    return value


def local(solution, forcing, viscosity, blocks, layer_count, bed_frozen, basin_map):
    row_count = solution.shape[1]
    lane_count = solution.shape[2]
    y_cells = lane_count // LAYERS
    layer_idx = jnp.arange(LAYERS, dtype=jnp.int32)
    active = (
        (layer_idx[None, None, :] < layer_count[:, :, None])
        .astype(jnp.float32)
        .reshape(row_count, lane_count)
    )
    frozen = bed_frozen.astype(jnp.float32)
    matrix = blocks.reshape(4, 4, row_count, lane_count)
    grid = (3, row_count, y_cells, LAYERS)

    masked = solution * active[None]
    masked_grid = masked[:3].reshape(grid)
    weight_grid = (coupling * viscosity * active).reshape(1, row_count, y_cells, LAYERS)
    basin_grid = jnp.broadcast_to(
        basin_map.astype(jnp.float32)[None, :, :, None], (1, row_count, y_cells, LAYERS)
    )
    halo_source = jnp.concatenate([masked_grid, weight_grid, basin_grid], axis=0)
    from_low, from_high = neighbour_shift(halo_source, "gy", 2, 1)
    y_low, y_high = from_low[:3], from_high[:3]
    in_cell = in_cell_terms(masked, matrix)
    moving = in_cell[:3] + neighbour_terms(masked_grid, None, None, y_low, y_high, viscosity, frozen)
    residual = active[None] * (forcing - jnp.concatenate([moving, in_cell[3:]], axis=0))

    diagonal = jnp.stack([matrix[0, 0], matrix[1, 1], matrix[2, 2]])
    line_lead = jnp.where(active[None] > 0.0, diagonal + 2.0 * viscosity[None], 1.0)
    line_off = (viscosity * active)[None]
    packed = jnp.concatenate([line_lead, line_off, residual[:3], masked[:3]], axis=0)
    whole = gather_rows(packed, "gx")
    all_rows = whole.shape[1]
    whole_off = whole[3:4]
    padded_masked = jnp.pad(whole[7:10], ((0, 0), (1, 1), (0, 0)))
    whole_rhs = whole[4:7] + whole_off * (padded_masked[:, :-2] + padded_masked[:, 2:])
    solver = line_solve if all_rows <= 32 else line_solve_scan
    whole_corr = solver(whole[0:3], jnp.broadcast_to(whole_off, whole_rhs.shape), whole_rhs)

    first = lax.axis_index("gx") * row_count
    padded_corr = jnp.pad(whole_corr, ((0, 0), (1, 1), (0, 0)))
    near_corr = lax.dynamic_slice_in_dim(padded_corr, first, row_count + 2, axis=1)
    near_masked = lax.dynamic_slice_in_dim(padded_masked, first, row_count + 2, axis=1)
    correction = near_corr[:, 1:-1]

    pressure_in = residual[3] - (
        matrix[3, 0] * correction[0] + matrix[3, 1] * correction[1] + matrix[3, 2] * correction[2]
    )
    pressure_step = active * pressure_in / viscosity
    full_step = jnp.concatenate([correction, pressure_step[None]], axis=0)
    smoothed = solution + full_step

    smoothed_masked = smoothed * active[None]
    sm_grid = smoothed_masked[:3].reshape(grid)
    edge = (3, 1, y_cells, LAYERS)
    x_low2 = (near_masked[:, :1] + near_corr[:, :1]).reshape(edge)
    x_high2 = (near_masked[:, -1:] + near_corr[:, -1:]).reshape(edge)
    no_cols = jnp.zeros((3, row_count, 1, LAYERS), jnp.float32)
    in_cell2 = in_cell_terms(smoothed_masked, matrix)
    moving2 = in_cell2[:3] + neighbour_terms(sm_grid, x_low2, x_high2, no_cols, no_cols, viscosity, frozen)
    post = active[None] * (forcing - jnp.concatenate([moving2, in_cell2[3:]], axis=0))
    column_local = jnp.sum(post.reshape(4, row_count, y_cells, LAYERS), axis=-1)

    to_low = jnp.sum(from_low[3:4, :, 0] * sm_grid[:, :, 0], axis=-1)
    to_high = jnp.sum(from_high[3:4, :, 0] * sm_grid[:, :, -1], axis=-1)
    edge_terms = jnp.zeros((3, row_count, y_cells), jnp.float32)
    count = lax.axis_size("gy")
    if count != 4:
        forward = [(i, i + 1) for i in range(count - 1)]
        backward = [(target, source) for source, target in forward]
        for_last = lax.ppermute(to_low, "gy", backward)
        for_first = lax.ppermute(to_high, "gy", forward)
        edge_terms = edge_terms.at[:, :, 0].set(for_first).at[:, :, -1].set(for_last)
        column_residual = column_local + jnp.pad(edge_terms, ((0, 1), (0, 0), (0, 0)))
    basin_count = lax.axis_size("gx") // 2 * lax.axis_size("gy")
    basin_ids = jnp.arange(basin_count, dtype=jnp.int32)
    member = basin_map.reshape(-1)[:, None] == basin_ids[None, :]
    partial_sums = jnp.sum(jnp.where(member[None], column_local.reshape(4, -1)[:, :, None], 0.0), axis=1)
    beside_ids = jnp.concatenate([from_low[4, :, 0, 0], from_high[4, :, 0, 0]]).astype(jnp.int32)
    beside_member = beside_ids[:, None] == basin_ids[None, :]
    beside_terms = jnp.concatenate([to_low, to_high], axis=1)
    beside_sums = jnp.sum(jnp.where(beside_member[None], beside_terms[:, :, None], 0.0), axis=1)
    partial_sums = partial_sums + jnp.pad(beside_sums, ((0, 1), (0, 0)))
    basin_sums = tree_sum(partial_sums, "gx")
    if count != 4:
        basin_residual = tree_sum(basin_sums, "gy")
    else:
        even = lax.axis_index("gy") % 2 == 0
        first_out = jnp.pad(jnp.where(even, to_high, to_low), ((0, 1), (0, 0)))
        second_out = jnp.pad(jnp.where(even, to_low, to_high), ((0, 1), (0, 0)))
        received = []
        for edge_out, pairs in (
            (first_out, [(0, 1), (1, 0), (2, 3), (3, 2)]),
            (second_out, [(1, 2), (2, 1), (3, 0), (0, 3)]),
        ):
            got = lax.ppermute(jnp.concatenate([basin_sums, edge_out], axis=1), "gy", pairs)
            basin_sums = basin_sums + got[:, :basin_count]
            received.append(got[:, basin_count:])
        basin_residual = basin_sums
        first_term = jnp.where(even, received[1], received[0])
        last_term = jnp.where(even, received[0], received[1])
        middle = jnp.zeros((4, row_count, y_cells - 2), jnp.float32)
        column_residual = column_local + jnp.concatenate(
            [first_term[:, :, None], middle, last_term[:, :, None]], axis=2
        )
    return (smoothed, column_residual, basin_residual)


def solution(mesh):
    return jax.shard_map(
        local,
        mesh=mesh,
        in_specs=(
            P(None, "gx", "gy"),
            P(None, "gx", "gy"),
            P("gx", "gy"),
            P(None, "gx", "gy"),
            P("gx", "gy"),
            P("gx", "gy"),
            P("gx", "gy"),
        ),
        out_specs=(P(None, "gx", "gy"), P(None, "gx", "gy"), P()),
        check_vma=False,
    )
```

```python
import jax
import jax.numpy as jnp
from jax import lax
from jax.sharding import PartitionSpec as P

LAYERS = 80


coupling = 0.25


def neighbour_shift(block, axis, dim, width):
    count = lax.axis_size(axis)
    forward = [(i, i + 1) for i in range(count - 1)]
    backward = [(target, source) for source, target in forward]
    low = lax.ppermute(lax.slice_in_dim(block, block.shape[dim] - width, None, axis=dim), axis, forward)
    high = lax.ppermute(lax.slice_in_dim(block, 0, width, axis=dim), axis, backward)
    return low, high


def vertical_pair(grid_view, frozen):
    lower_cells = jnp.concatenate(
        [grid_view[..., :1] * (1.0 - frozen)[None, :, :, None], grid_view[..., :-1]], axis=-1
    )
    upper_cells = jnp.concatenate([grid_view[..., 1:], jnp.zeros_like(grid_view[..., :1])], axis=-1)
    return lower_cells + upper_cells


def neighbour_terms(grid_view, x_low, x_high, y_low, y_high, viscosity, frozen):
    shape = grid_view.shape
    y_pad = jnp.concatenate([y_low, grid_view, y_high], axis=2)
    if x_low is None:
        along_line = 2.0 * grid_view
    else:
        x_pad = jnp.concatenate([x_low, grid_view, x_high], axis=1)
        along_line = 2.0 * grid_view - x_pad[:, :-2] - x_pad[:, 2:]
    across_line = y_pad[:, :, :-2] + y_pad[:, :, 2:] + vertical_pair(grid_view, frozen)
    flat = (3, shape[1], shape[2] * shape[3])
    return viscosity * along_line.reshape(flat) - coupling * viscosity * across_line.reshape(flat)


def in_cell_terms(masked, matrix):
    return jnp.sum(matrix * masked[None], axis=1)


def gather_rows(block, axis):
    count, mine = (lax.axis_size(axis), lax.axis_index(axis))
    if count > 8:
        return lax.all_gather(block, axis, axis=1, tiled=True)
    pieces = [block]
    for step in range(1, count):
        pairs = [((i + step) % count, i) for i in range(count)]
        pieces.append(lax.ppermute(block, axis, pairs))
    stacked = jnp.stack(pieces + pieces, axis=0)
    ordered = lax.dynamic_slice_in_dim(stacked, count - mine, count, axis=0)
    ordered = jnp.moveaxis(ordered, 0, 1)
    return ordered.reshape(block.shape[0], count * block.shape[1], *block.shape[2:])


def line_solve(line_lead, line_off, line_rhs):
    rows = line_lead.shape[1]
    gain_prev = jnp.zeros_like(line_rhs[:, 0])
    value_prev = jnp.zeros_like(line_rhs[:, 0])
    gains, values = [], []
    for cell_idx in range(rows):
        off_cell = line_off[:, cell_idx]
        pivot = line_lead[:, cell_idx] - off_cell * gain_prev
        gain_prev = off_cell / pivot
        value_prev = (line_rhs[:, cell_idx] + off_cell * value_prev) / pivot
        gains.append(gain_prev)
        values.append(value_prev)
    next_value = jnp.zeros_like(line_rhs[:, 0])
    corrections = list(values)
    for cell_idx in reversed(range(rows)):
        next_value = values[cell_idx] + gains[cell_idx] * next_value
        corrections[cell_idx] = next_value
    return jnp.stack(corrections, axis=1)


def line_solve_scan(line_lead, line_off, line_rhs):
    def sweep_down(carried, cell_cols):
        gain_prev, value_prev = carried
        lead_cell, off_cell, rhs_cell = cell_cols
        pivot = lead_cell - off_cell * gain_prev
        gain = off_cell / pivot
        value = (rhs_cell + off_cell * value_prev) / pivot
        return (gain, value), (gain, value)

    zeros_line = jnp.zeros_like(line_rhs[:, 0])
    scanned = (jnp.moveaxis(line_lead, 1, 0), jnp.moveaxis(line_off, 1, 0), jnp.moveaxis(line_rhs, 1, 0))
    _, (gains, values) = lax.scan(sweep_down, (zeros_line, zeros_line), scanned)

    def sweep_up(next_value, cell_cols):
        gain, value = cell_cols
        solved = value + gain * next_value
        return solved, solved

    _, corrections = lax.scan(sweep_up, zeros_line, (gains, values), reverse=True)
    return jnp.moveaxis(corrections, 0, 1)


def tree_sum(value, axis):
    count = lax.axis_size(axis)
    if count & (count - 1):
        return lax.psum(value, axis)
    step = 1
    while step < count:
        value = value + lax.ppermute(value, axis, [(i, i ^ step) for i in range(count)])
        step *= 2
    return value


def local(solution, forcing, viscosity, blocks, layer_count, bed_frozen, basin_map):
    row_count = solution.shape[1]
    lane_count = solution.shape[2]
    y_cells = lane_count // LAYERS
    layer_idx = jnp.arange(LAYERS, dtype=jnp.int32)
    active = (
        (layer_idx[None, None, :] < layer_count[:, :, None])
        .astype(jnp.float32)
        .reshape(row_count, lane_count)
    )
    frozen = bed_frozen.astype(jnp.float32)
    matrix = blocks.reshape(4, 4, row_count, lane_count)
    grid = (3, row_count, y_cells, LAYERS)

    masked = solution * active[None]
    masked_grid = masked[:3].reshape(grid)

    def edge_payload(column):
        count_col = lax.slice_in_dim(layer_count, column, column + 1, axis=1)
        active_col = (layer_idx[None, None, :] < count_col[:, :, None]).astype(jnp.float32)
        solution_col = lax.slice_in_dim(solution[:3].reshape(grid), column, column + 1, axis=2)
        viscosity_col = lax.slice_in_dim(viscosity.reshape(grid[1:]), column, column + 1, axis=1)
        basin_col = lax.slice_in_dim(basin_map, column, column + 1, axis=1).astype(jnp.float32)
        return jnp.concatenate(
            [
                solution_col * active_col[None],
                (coupling * viscosity_col * active_col)[None],
                jnp.broadcast_to(basin_col[None, :, :, None], (1, row_count, 1, LAYERS)),
            ],
            axis=0,
        )

    count = lax.axis_size("gy")
    forward = [(i, i + 1) for i in range(count - 1)]
    backward = [(target, source) for source, target in forward]
    from_low = lax.ppermute(edge_payload(y_cells - 1), "gy", forward)
    from_high = lax.ppermute(edge_payload(0), "gy", backward)
    y_low, y_high = from_low[:3], from_high[:3]
    in_cell = in_cell_terms(masked, matrix)
    moving = in_cell[:3] + neighbour_terms(masked_grid, None, None, y_low, y_high, viscosity, frozen)
    residual = active[None] * (forcing - jnp.concatenate([moving, in_cell[3:]], axis=0))

    diagonal = jnp.stack([matrix[0, 0], matrix[1, 1], matrix[2, 2]])
    line_lead = jnp.where(active[None] > 0.0, diagonal + 2.0 * viscosity[None], 1.0)
    line_off = (viscosity * active)[None]
    packed = jnp.concatenate([line_lead, line_off, residual[:3], masked[:3]], axis=0)
    whole = gather_rows(packed, "gx")
    all_rows = whole.shape[1]
    whole_off = whole[3:4]
    padded_masked = jnp.pad(whole[7:10], ((0, 0), (1, 1), (0, 0)))
    whole_rhs = whole[4:7] + whole_off * (padded_masked[:, :-2] + padded_masked[:, 2:])
    solver = line_solve if all_rows <= 32 else line_solve_scan
    whole_corr = solver(whole[0:3], jnp.broadcast_to(whole_off, whole_rhs.shape), whole_rhs)

    first = lax.axis_index("gx") * row_count
    padded_corr = jnp.pad(whole_corr, ((0, 0), (1, 1), (0, 0)))
    near_corr = lax.dynamic_slice_in_dim(padded_corr, first, row_count + 2, axis=1)
    near_masked = lax.dynamic_slice_in_dim(padded_masked, first, row_count + 2, axis=1)
    correction = near_corr[:, 1:-1]

    pressure_in = residual[3] - (
        matrix[3, 0] * correction[0] + matrix[3, 1] * correction[1] + matrix[3, 2] * correction[2]
    )
    pressure_step = active * pressure_in / viscosity
    full_step = jnp.concatenate([correction, pressure_step[None]], axis=0)
    smoothed = solution + full_step

    smoothed_masked = smoothed * active[None]
    sm_grid = smoothed_masked[:3].reshape(grid)
    edge = (3, 1, y_cells, LAYERS)
    x_low2 = (near_masked[:, :1] + near_corr[:, :1]).reshape(edge)
    x_high2 = (near_masked[:, -1:] + near_corr[:, -1:]).reshape(edge)
    no_cols = jnp.zeros((3, row_count, 1, LAYERS), jnp.float32)
    in_cell2 = in_cell_terms(smoothed_masked, matrix)
    moving2 = in_cell2[:3] + neighbour_terms(sm_grid, x_low2, x_high2, no_cols, no_cols, viscosity, frozen)
    post = active[None] * (forcing - jnp.concatenate([moving2, in_cell2[3:]], axis=0))
    column_local = jnp.sum(post.reshape(4, row_count, y_cells, LAYERS), axis=-1)

    to_low = jnp.sum(from_low[3:4, :, 0] * sm_grid[:, :, 0], axis=-1)
    to_high = jnp.sum(from_high[3:4, :, 0] * sm_grid[:, :, -1], axis=-1)
    edge_terms = jnp.zeros((3, row_count, y_cells), jnp.float32)
    count = lax.axis_size("gy")
    if count != 4:
        forward = [(i, i + 1) for i in range(count - 1)]
        backward = [(target, source) for source, target in forward]
        for_last = lax.ppermute(to_low, "gy", backward)
        for_first = lax.ppermute(to_high, "gy", forward)
        edge_terms = edge_terms.at[:, :, 0].set(for_first).at[:, :, -1].set(for_last)
        column_residual = column_local + jnp.pad(edge_terms, ((0, 1), (0, 0), (0, 0)))
    basin_count = lax.axis_size("gx") // 2 * lax.axis_size("gy")
    basin_ids = jnp.arange(basin_count, dtype=jnp.int32)
    member = basin_map.reshape(-1)[:, None] == basin_ids[None, :]
    partial_sums = jnp.sum(jnp.where(member[None], column_local.reshape(4, -1)[:, :, None], 0.0), axis=1)
    beside_ids = jnp.concatenate([from_low[4, :, 0, 0], from_high[4, :, 0, 0]]).astype(jnp.int32)
    beside_member = beside_ids[:, None] == basin_ids[None, :]
    beside_terms = jnp.concatenate([to_low, to_high], axis=1)
    beside_sums = jnp.sum(jnp.where(beside_member[None], beside_terms[:, :, None], 0.0), axis=1)
    partial_sums = partial_sums + jnp.pad(beside_sums, ((0, 1), (0, 0)))
    basin_sums = tree_sum(partial_sums, "gx")
    if count != 4:
        basin_residual = tree_sum(basin_sums, "gy")
    else:
        even = lax.axis_index("gy") % 2 == 0
        first_out = jnp.pad(jnp.where(even, to_high, to_low), ((0, 1), (0, 0)))
        second_out = jnp.pad(jnp.where(even, to_low, to_high), ((0, 1), (0, 0)))
        received = []
        for edge_out, pairs in (
            (first_out, [(0, 1), (1, 0), (2, 3), (3, 2)]),
            (second_out, [(1, 2), (2, 1), (3, 0), (0, 3)]),
        ):
            got = lax.ppermute(jnp.concatenate([basin_sums, edge_out], axis=1), "gy", pairs)
            basin_sums = basin_sums + got[:, :basin_count]
            received.append(got[:, basin_count:])
        basin_residual = basin_sums
        first_term = jnp.where(even, received[1], received[0])
        last_term = jnp.where(even, received[0], received[1])
        middle = jnp.zeros((4, row_count, y_cells - 2), jnp.float32)
        column_residual = column_local + jnp.concatenate(
            [first_term[:, :, None], middle, last_term[:, :, None]], axis=2
        )
    return (smoothed, column_residual, basin_residual)


def solution(mesh):
    return jax.shard_map(
        local,
        mesh=mesh,
        in_specs=(
            P(None, "gx", "gy"),
            P(None, "gx", "gy"),
            P("gx", "gy"),
            P(None, "gx", "gy"),
            P("gx", "gy"),
            P("gx", "gy"),
            P("gx", "gy"),
        ),
        out_specs=(P(None, "gx", "gy"), P(None, "gx", "gy"), P()),
        check_vma=False,
    )
```

```python
import jax
import jax.numpy as jnp
from jax import lax
from jax.sharding import PartitionSpec as P

LAYERS = 80


coupling = 0.25


def neighbour_shift(block, axis, dim, width):
    count = lax.axis_size(axis)
    forward = [(i, i + 1) for i in range(count - 1)]
    backward = [(target, source) for source, target in forward]
    low = lax.ppermute(lax.slice_in_dim(block, block.shape[dim] - width, None, axis=dim), axis, forward)
    high = lax.ppermute(lax.slice_in_dim(block, 0, width, axis=dim), axis, backward)
    return low, high


def vertical_pair(grid_view, frozen):
    lower_cells = jnp.concatenate(
        [grid_view[..., :1] * (1.0 - frozen)[None, :, :, None], grid_view[..., :-1]], axis=-1
    )
    upper_cells = jnp.concatenate([grid_view[..., 1:], jnp.zeros_like(grid_view[..., :1])], axis=-1)
    return lower_cells + upper_cells


def neighbour_terms(grid_view, x_low, x_high, y_low, y_high, viscosity, frozen):
    shape = grid_view.shape
    y_pad = jnp.concatenate([y_low, grid_view, y_high], axis=2)
    if x_low is None:
        along_line = 2.0 * grid_view
    else:
        x_pad = jnp.concatenate([x_low, grid_view, x_high], axis=1)
        along_line = 2.0 * grid_view - x_pad[:, :-2] - x_pad[:, 2:]
    across_line = y_pad[:, :, :-2] + y_pad[:, :, 2:] + vertical_pair(grid_view, frozen)
    flat = (3, shape[1], shape[2] * shape[3])
    return viscosity * along_line.reshape(flat) - coupling * viscosity * across_line.reshape(flat)


def in_cell_terms(masked, matrix):
    return jnp.sum(matrix * masked[None], axis=1)


def gather_rows(block, axis):
    count, mine = (lax.axis_size(axis), lax.axis_index(axis))
    if count > 8:
        return lax.all_gather(block, axis, axis=1, tiled=True)
    pieces = [block]
    if count & (count - 1) == 0:
        for step in range(1, count):
            pieces.append(lax.ppermute(block, axis, [(i ^ step, i) for i in range(count)]))
        order = jnp.arange(count, dtype=jnp.int32) ^ mine
        ordered = jnp.take(jnp.stack(pieces, axis=0), order, axis=0)
    else:
        for step in range(1, count):
            pairs = [((i + step) % count, i) for i in range(count)]
            pieces.append(lax.ppermute(block, axis, pairs))
        stacked = jnp.stack(pieces + pieces, axis=0)
        ordered = lax.dynamic_slice_in_dim(stacked, count - mine, count, axis=0)
    ordered = jnp.moveaxis(ordered, 0, 1)
    return ordered.reshape(block.shape[0], count * block.shape[1], *block.shape[2:])


def line_solve(line_lead, line_off, line_rhs):
    rows = line_lead.shape[1]
    gain_prev = jnp.zeros_like(line_rhs[:, 0])
    value_prev = jnp.zeros_like(line_rhs[:, 0])
    gains, values = [], []
    for cell_idx in range(rows):
        off_cell = line_off[:, cell_idx]
        pivot = line_lead[:, cell_idx] - off_cell * gain_prev
        gain_prev = off_cell / pivot
        value_prev = (line_rhs[:, cell_idx] + off_cell * value_prev) / pivot
        gains.append(gain_prev)
        values.append(value_prev)
    next_value = jnp.zeros_like(line_rhs[:, 0])
    corrections = list(values)
    for cell_idx in reversed(range(rows)):
        next_value = values[cell_idx] + gains[cell_idx] * next_value
        corrections[cell_idx] = next_value
    return jnp.stack(corrections, axis=1)


def line_solve_scan(line_lead, line_off, line_rhs):
    def sweep_down(carried, cell_cols):
        gain_prev, value_prev = carried
        lead_cell, off_cell, rhs_cell = cell_cols
        pivot = lead_cell - off_cell * gain_prev
        gain = off_cell / pivot
        value = (rhs_cell + off_cell * value_prev) / pivot
        return (gain, value), (gain, value)

    zeros_line = jnp.zeros_like(line_rhs[:, 0])
    scanned = (jnp.moveaxis(line_lead, 1, 0), jnp.moveaxis(line_off, 1, 0), jnp.moveaxis(line_rhs, 1, 0))
    _, (gains, values) = lax.scan(sweep_down, (zeros_line, zeros_line), scanned)

    def sweep_up(next_value, cell_cols):
        gain, value = cell_cols
        solved = value + gain * next_value
        return solved, solved

    _, corrections = lax.scan(sweep_up, zeros_line, (gains, values), reverse=True)
    return jnp.moveaxis(corrections, 0, 1)


def tree_sum(value, axis):
    count = lax.axis_size(axis)
    if count & (count - 1):
        return lax.psum(value, axis)
    step = 1
    while step < count:
        value = value + lax.ppermute(value, axis, [(i, i ^ step) for i in range(count)])
        step *= 2
    return value


def local(solution, forcing, viscosity, blocks, layer_count, bed_frozen, basin_map):
    row_count = solution.shape[1]
    lane_count = solution.shape[2]
    y_cells = lane_count // LAYERS
    layer_idx = jnp.arange(LAYERS, dtype=jnp.int32)
    active = (
        (layer_idx[None, None, :] < layer_count[:, :, None])
        .astype(jnp.float32)
        .reshape(row_count, lane_count)
    )
    frozen = bed_frozen.astype(jnp.float32)
    matrix = blocks.reshape(4, 4, row_count, lane_count)
    grid = (3, row_count, y_cells, LAYERS)

    masked = solution * active[None]
    masked_grid = masked[:3].reshape(grid)
    weight_grid = (coupling * viscosity * active).reshape(1, row_count, y_cells, LAYERS)
    basin_grid = jnp.broadcast_to(
        basin_map.astype(jnp.float32)[None, :, :, None], (1, row_count, y_cells, LAYERS)
    )
    halo_source = jnp.concatenate([masked_grid, weight_grid, basin_grid], axis=0)
    from_low, from_high = neighbour_shift(halo_source, "gy", 2, 1)
    y_low, y_high = from_low[:3], from_high[:3]
    in_cell = in_cell_terms(masked, matrix)
    moving = in_cell[:3] + neighbour_terms(masked_grid, None, None, y_low, y_high, viscosity, frozen)
    residual = active[None] * (forcing - jnp.concatenate([moving, in_cell[3:]], axis=0))

    diagonal = jnp.stack([matrix[0, 0], matrix[1, 1], matrix[2, 2]])
    line_lead = jnp.where(active[None] > 0.0, diagonal + 2.0 * viscosity[None], 1.0)
    line_off = (viscosity * active)[None]
    packed = jnp.concatenate([line_lead, line_off, residual[:3], masked[:3]], axis=0)
    whole = gather_rows(packed, "gx")
    all_rows = whole.shape[1]
    whole_off = whole[3:4]
    padded_masked = jnp.pad(whole[7:10], ((0, 0), (1, 1), (0, 0)))
    whole_rhs = whole[4:7] + whole_off * (padded_masked[:, :-2] + padded_masked[:, 2:])
    solver = line_solve if all_rows <= 32 else line_solve_scan
    whole_corr = solver(whole[0:3], jnp.broadcast_to(whole_off, whole_rhs.shape), whole_rhs)

    first = lax.axis_index("gx") * row_count
    padded_corr = jnp.pad(whole_corr, ((0, 0), (1, 1), (0, 0)))
    near_corr = lax.dynamic_slice_in_dim(padded_corr, first, row_count + 2, axis=1)
    near_masked = lax.dynamic_slice_in_dim(padded_masked, first, row_count + 2, axis=1)
    correction = near_corr[:, 1:-1]

    pressure_in = residual[3] - (
        matrix[3, 0] * correction[0] + matrix[3, 1] * correction[1] + matrix[3, 2] * correction[2]
    )
    pressure_step = active * pressure_in / viscosity
    full_step = jnp.concatenate([correction, pressure_step[None]], axis=0)
    smoothed = solution + full_step

    smoothed_masked = smoothed * active[None]
    sm_grid = smoothed_masked[:3].reshape(grid)
    edge = (3, 1, y_cells, LAYERS)
    x_low2 = (near_masked[:, :1] + near_corr[:, :1]).reshape(edge)
    x_high2 = (near_masked[:, -1:] + near_corr[:, -1:]).reshape(edge)
    no_cols = jnp.zeros((3, row_count, 1, LAYERS), jnp.float32)
    in_cell2 = in_cell_terms(smoothed_masked, matrix)
    moving2 = in_cell2[:3] + neighbour_terms(sm_grid, x_low2, x_high2, no_cols, no_cols, viscosity, frozen)
    post = active[None] * (forcing - jnp.concatenate([moving2, in_cell2[3:]], axis=0))
    column_local = jnp.sum(post.reshape(4, row_count, y_cells, LAYERS), axis=-1)

    to_low = jnp.sum(from_low[3:4, :, 0] * sm_grid[:, :, 0], axis=-1)
    to_high = jnp.sum(from_high[3:4, :, 0] * sm_grid[:, :, -1], axis=-1)
    edge_terms = jnp.zeros((3, row_count, y_cells), jnp.float32)
    count = lax.axis_size("gy")
    if count != 4:
        forward = [(i, i + 1) for i in range(count - 1)]
        backward = [(target, source) for source, target in forward]
        for_last = lax.ppermute(to_low, "gy", backward)
        for_first = lax.ppermute(to_high, "gy", forward)
        edge_terms = edge_terms.at[:, :, 0].set(for_first).at[:, :, -1].set(for_last)
        column_residual = column_local + jnp.pad(edge_terms, ((0, 1), (0, 0), (0, 0)))
    basin_count = lax.axis_size("gx") // 2 * lax.axis_size("gy")
    basin_ids = jnp.arange(basin_count, dtype=jnp.int32)
    member = basin_map.reshape(-1)[:, None] == basin_ids[None, :]
    partial_sums = jnp.sum(jnp.where(member[None], column_local.reshape(4, -1)[:, :, None], 0.0), axis=1)
    beside_ids = jnp.concatenate([from_low[4, :, 0, 0], from_high[4, :, 0, 0]]).astype(jnp.int32)
    beside_member = beside_ids[:, None] == basin_ids[None, :]
    beside_terms = jnp.concatenate([to_low, to_high], axis=1)
    beside_sums = jnp.sum(jnp.where(beside_member[None], beside_terms[:, :, None], 0.0), axis=1)
    partial_sums = partial_sums + jnp.pad(beside_sums, ((0, 1), (0, 0)))
    basin_sums = tree_sum(partial_sums, "gx")
    if count != 4:
        basin_residual = tree_sum(basin_sums, "gy")
    else:
        even = lax.axis_index("gy") % 2 == 0
        first_out = jnp.pad(jnp.where(even, to_high, to_low), ((0, 1), (0, 0)))
        second_out = jnp.pad(jnp.where(even, to_low, to_high), ((0, 1), (0, 0)))
        received = []
        for edge_out, pairs in (
            (first_out, [(0, 1), (1, 0), (2, 3), (3, 2)]),
            (second_out, [(1, 2), (2, 1), (3, 0), (0, 3)]),
        ):
            got = lax.ppermute(jnp.concatenate([basin_sums, edge_out], axis=1), "gy", pairs)
            basin_sums = basin_sums + got[:, :basin_count]
            received.append(got[:, basin_count:])
        basin_residual = basin_sums
        first_term = jnp.where(even, received[1], received[0])
        last_term = jnp.where(even, received[0], received[1])
        middle = jnp.zeros((4, row_count, y_cells - 2), jnp.float32)
        column_residual = column_local + jnp.concatenate(
            [first_term[:, :, None], middle, last_term[:, :, None]], axis=2
        )
    return (smoothed, column_residual, basin_residual)


def solution(mesh):
    return jax.shard_map(
        local,
        mesh=mesh,
        in_specs=(
            P(None, "gx", "gy"),
            P(None, "gx", "gy"),
            P("gx", "gy"),
            P(None, "gx", "gy"),
            P("gx", "gy"),
            P("gx", "gy"),
            P("gx", "gy"),
        ),
        out_specs=(P(None, "gx", "gy"), P(None, "gx", "gy"), P()),
        check_vma=False,
    )
```

```python
import jax
import jax.numpy as jnp
from jax import lax
from jax.sharding import PartitionSpec as P

LAYERS = 80


coupling = 0.25


def neighbour_shift(block, axis, dim, width):
    count = lax.axis_size(axis)
    forward = [(i, i + 1) for i in range(count - 1)]
    backward = [(target, source) for source, target in forward]
    low = lax.ppermute(lax.slice_in_dim(block, block.shape[dim] - width, None, axis=dim), axis, forward)
    high = lax.ppermute(lax.slice_in_dim(block, 0, width, axis=dim), axis, backward)
    return low, high


def vertical_pair(grid_view, frozen):
    lower_cells = jnp.concatenate(
        [grid_view[..., :1] * (1.0 - frozen)[None, :, :, None], grid_view[..., :-1]], axis=-1
    )
    upper_cells = jnp.concatenate([grid_view[..., 1:], jnp.zeros_like(grid_view[..., :1])], axis=-1)
    return lower_cells + upper_cells


def neighbour_terms(grid_view, x_low, x_high, y_low, y_high, viscosity, frozen):
    shape = grid_view.shape
    y_pad = jnp.concatenate([y_low, grid_view, y_high], axis=2)
    if x_low is None:
        along_line = 2.0 * grid_view
    else:
        x_pad = jnp.concatenate([x_low, grid_view, x_high], axis=1)
        along_line = 2.0 * grid_view - x_pad[:, :-2] - x_pad[:, 2:]
    across_line = y_pad[:, :, :-2] + y_pad[:, :, 2:] + vertical_pair(grid_view, frozen)
    flat = (3, shape[1], shape[2] * shape[3])
    return viscosity * along_line.reshape(flat) - coupling * viscosity * across_line.reshape(flat)


def in_cell_terms(masked, matrix):
    return jnp.sum(matrix * masked[None], axis=1)


def gather_rows(block, axis):
    count, mine = (lax.axis_size(axis), lax.axis_index(axis))
    if count > 8:
        return lax.all_gather(block, axis, axis=1, tiled=True)
    pieces = [block]
    for step in range(1, count):
        pairs = [((i + step) % count, i) for i in range(count)]
        pieces.append(lax.ppermute(block, axis, pairs))
    stacked = jnp.stack(pieces + pieces, axis=0)
    ordered = lax.dynamic_slice_in_dim(stacked, count - mine, count, axis=0)
    ordered = jnp.moveaxis(ordered, 0, 1)
    return ordered.reshape(block.shape[0], count * block.shape[1], *block.shape[2:])


def line_solve(line_lead, line_off, line_rhs):
    rows = line_lead.shape[1]
    gain_prev = jnp.zeros_like(line_rhs[:, 0])
    value_prev = jnp.zeros_like(line_rhs[:, 0])
    gains, values = [], []
    for cell_idx in range(rows):
        off_cell = line_off[:, cell_idx]
        pivot = line_lead[:, cell_idx] - off_cell * gain_prev
        gain_prev = off_cell / pivot
        value_prev = (line_rhs[:, cell_idx] + off_cell * value_prev) / pivot
        gains.append(gain_prev)
        values.append(value_prev)
    next_value = jnp.zeros_like(line_rhs[:, 0])
    corrections = list(values)
    for cell_idx in reversed(range(rows)):
        next_value = values[cell_idx] + gains[cell_idx] * next_value
        corrections[cell_idx] = next_value
    return jnp.stack(corrections, axis=1)


def line_solve_scan(line_lead, line_off, line_rhs):
    def sweep_down(carried, cell_cols):
        gain_prev, value_prev = carried
        lead_cell, off_cell, rhs_cell = cell_cols
        pivot = lead_cell - off_cell * gain_prev
        gain = off_cell / pivot
        value = (rhs_cell + off_cell * value_prev) / pivot
        return (gain, value), (gain, value)

    zeros_line = jnp.zeros_like(line_rhs[:, 0])
    scanned = (jnp.moveaxis(line_lead, 1, 0), jnp.moveaxis(line_off, 1, 0), jnp.moveaxis(line_rhs, 1, 0))
    _, (gains, values) = lax.scan(sweep_down, (zeros_line, zeros_line), scanned)

    def sweep_up(next_value, cell_cols):
        gain, value = cell_cols
        solved = value + gain * next_value
        return solved, solved

    _, corrections = lax.scan(sweep_up, zeros_line, (gains, values), reverse=True)
    return jnp.moveaxis(corrections, 0, 1)


def tree_sum(value, axis):
    count = lax.axis_size(axis)
    if count & (count - 1):
        return lax.psum(value, axis)
    step = 1
    while step < count:
        value = value + lax.ppermute(value, axis, [(i, i ^ step) for i in range(count)])
        step *= 2
    return value


def local(solution, forcing, viscosity, blocks, layer_count, bed_frozen, basin_map):
    row_count = solution.shape[1]
    lane_count = solution.shape[2]
    y_cells = lane_count // LAYERS
    layer_idx = jnp.arange(LAYERS, dtype=jnp.int32)
    active = (
        (layer_idx[None, None, :] < layer_count[:, :, None])
        .astype(jnp.float32)
        .reshape(row_count, lane_count)
    )
    frozen = bed_frozen.astype(jnp.float32)
    matrix = blocks.reshape(4, 4, row_count, lane_count)
    grid = (3, row_count, y_cells, LAYERS)

    masked = solution * active[None]
    masked_grid = masked[:3].reshape(grid)
    weight_grid = (coupling * viscosity * active).reshape(1, row_count, y_cells, LAYERS)
    basin_grid = jnp.broadcast_to(
        basin_map.astype(jnp.float32)[None, :, :, None], (1, row_count, y_cells, LAYERS)
    )
    halo_source = jnp.concatenate([masked_grid, weight_grid, basin_grid], axis=0)
    from_low, from_high = neighbour_shift(halo_source, "gy", 2, 1)
    y_low, y_high = from_low[:3], from_high[:3]
    in_cell = in_cell_terms(masked, matrix)
    moving = in_cell[:3] + neighbour_terms(masked_grid, None, None, y_low, y_high, viscosity, frozen)
    residual = active[None] * (forcing - jnp.concatenate([moving, in_cell[3:]], axis=0))

    diagonal = jnp.stack([matrix[0, 0], matrix[1, 1], matrix[2, 2]])
    line_lead = jnp.where(active[None] > 0.0, diagonal + 2.0 * viscosity[None], 1.0)
    line_off = (viscosity * active)[None]
    packed = jnp.concatenate([line_lead, line_off, residual[:3], masked[:3]], axis=0)
    whole = gather_rows(packed, "gx")
    all_rows = whole.shape[1]
    whole_off = whole[3:4]
    padded_masked = jnp.pad(whole[7:10], ((0, 0), (1, 1), (0, 0)))
    whole_rhs = whole[4:7] + whole_off * (padded_masked[:, :-2] + padded_masked[:, 2:])
    solver = line_solve if all_rows <= 32 else line_solve_scan
    whole_corr = solver(whole[0:3], jnp.broadcast_to(whole_off, whole_rhs.shape), whole_rhs)

    first = lax.axis_index("gx") * row_count
    padded_corr = jnp.pad(whole_corr, ((0, 0), (1, 1), (0, 0)))
    near_corr = lax.dynamic_slice_in_dim(padded_corr, first, row_count + 2, axis=1)
    near_masked = lax.dynamic_slice_in_dim(padded_masked, first, row_count + 2, axis=1)
    correction = near_corr[:, 1:-1]

    pressure_in = residual[3] - (
        matrix[3, 0] * correction[0] + matrix[3, 1] * correction[1] + matrix[3, 2] * correction[2]
    )
    pressure_step = active * pressure_in / viscosity
    full_step = jnp.concatenate([correction, pressure_step[None]], axis=0)
    smoothed = solution + full_step

    smoothed_masked = smoothed * active[None]
    sm_grid = smoothed_masked[:3].reshape(grid)
    edge = (3, 1, y_cells, LAYERS)
    x_low2 = (near_masked[:, :1] + near_corr[:, :1]).reshape(edge)
    x_high2 = (near_masked[:, -1:] + near_corr[:, -1:]).reshape(edge)
    no_cols = jnp.zeros((3, row_count, 1, LAYERS), jnp.float32)
    in_cell2 = in_cell_terms(smoothed_masked, matrix)
    moving2 = in_cell2[:3] + neighbour_terms(sm_grid, x_low2, x_high2, no_cols, no_cols, viscosity, frozen)
    post = active[None] * (forcing - jnp.concatenate([moving2, in_cell2[3:]], axis=0))
    column_local = jnp.sum(post.reshape(4, row_count, y_cells, LAYERS), axis=-1)

    to_low = jnp.sum(from_low[3:4, :, 0] * sm_grid[:, :, 0], axis=-1)
    to_high = jnp.sum(from_high[3:4, :, 0] * sm_grid[:, :, -1], axis=-1)
    edge_terms = jnp.zeros((3, row_count, y_cells), jnp.float32)
    count = lax.axis_size("gy")
    if count != 4:
        forward = [(i, i + 1) for i in range(count - 1)]
        backward = [(target, source) for source, target in forward]
        for_last = lax.ppermute(to_low, "gy", backward)
        for_first = lax.ppermute(to_high, "gy", forward)
        edge_terms = edge_terms.at[:, :, 0].set(for_first).at[:, :, -1].set(for_last)
        column_residual = column_local + jnp.pad(edge_terms, ((0, 1), (0, 0), (0, 0)))
    basin_count = lax.axis_size("gx") // 2 * lax.axis_size("gy")
    basin_ids = jnp.arange(basin_count, dtype=jnp.int32)
    member = basin_map.reshape(-1)[:, None] == basin_ids[None, :]
    partial_sums = jnp.sum(jnp.where(member[None], column_local.reshape(4, -1)[:, :, None], 0.0), axis=1)
    beside_ids = jnp.concatenate([from_low[4, :, 0, 0], from_high[4, :, 0, 0]]).astype(jnp.int32)
    beside_member = beside_ids[:, None] == basin_ids[None, :]
    beside_terms = jnp.concatenate([to_low, to_high], axis=1)
    beside_sums = jnp.sum(jnp.where(beside_member[None], beside_terms[:, :, None], 0.0), axis=1)
    partial_sums = partial_sums + jnp.pad(beside_sums, ((0, 1), (0, 0)))
    basin_sums = partial_sums
    if count != 4:
        basin_residual = tree_sum(tree_sum(basin_sums, "gx"), "gy")
    else:
        even = lax.axis_index("gy") % 2 == 0
        first_out = jnp.pad(jnp.where(even, to_high, to_low), ((0, 1), (0, 0)))
        second_out = jnp.pad(jnp.where(even, to_low, to_high), ((0, 1), (0, 0)))
        received = []
        for edge_out, pairs in (
            (first_out, [(0, 1), (1, 0), (2, 3), (3, 2)]),
            (second_out, [(1, 2), (2, 1), (3, 0), (0, 3)]),
        ):
            got = lax.ppermute(jnp.concatenate([basin_sums, edge_out], axis=1), "gy", pairs)
            basin_sums = basin_sums + got[:, :basin_count]
            received.append(got[:, basin_count:])
        basin_residual = tree_sum(basin_sums, "gx")
        first_term = jnp.where(even, received[1], received[0])
        last_term = jnp.where(even, received[0], received[1])
        middle = jnp.zeros((4, row_count, y_cells - 2), jnp.float32)
        column_residual = column_local + jnp.concatenate(
            [first_term[:, :, None], middle, last_term[:, :, None]], axis=2
        )
    return (smoothed, column_residual, basin_residual)


def solution(mesh):
    return jax.shard_map(
        local,
        mesh=mesh,
        in_specs=(
            P(None, "gx", "gy"),
            P(None, "gx", "gy"),
            P("gx", "gy"),
            P(None, "gx", "gy"),
            P("gx", "gy"),
            P("gx", "gy"),
            P("gx", "gy"),
        ),
        out_specs=(P(None, "gx", "gy"), P(None, "gx", "gy"), P()),
        check_vma=False,
    )
```

```python
import jax
import jax.numpy as jnp
from jax import lax
from jax.experimental import pallas as pl
from jax.sharding import PartitionSpec as P

LAYERS = 80


coupling = 0.25


def neighbour_shift(block, axis, dim, width):
    count = lax.axis_size(axis)
    forward = [(i, i + 1) for i in range(count - 1)]
    backward = [(target, source) for source, target in forward]
    low = lax.ppermute(lax.slice_in_dim(block, block.shape[dim] - width, None, axis=dim), axis, forward)
    high = lax.ppermute(lax.slice_in_dim(block, 0, width, axis=dim), axis, backward)
    return low, high


def payload_kernel(sol_ref, count_ref, visc_ref, basin_ref, low_ref, high_ref):
    rows = sol_ref.shape[1]
    lanes = sol_ref.shape[2]
    layer = lax.broadcasted_iota(jnp.int32, (rows, LAYERS), 1)
    for out_ref, column in ((low_ref, lanes // LAYERS - 1), (high_ref, 0)):
        start = column * LAYERS
        active = (layer < count_ref[:, column : column + 1]).astype(jnp.float32)
        for k in range(3):
            out_ref[k] = sol_ref[k, :, start : start + LAYERS] * active
        out_ref[3] = coupling * visc_ref[:, start : start + LAYERS] * active
        out_ref[4] = jnp.broadcast_to(basin_ref[:, column : column + 1].astype(jnp.float32), (rows, LAYERS))


def edge_payloads(solution, layer_count, viscosity, basin_map):
    rows = solution.shape[1]
    shape = jax.ShapeDtypeStruct((5, rows, LAYERS), jnp.float32)
    low, high = pl.pallas_call(payload_kernel, out_shape=(shape, shape))(
        solution, layer_count, viscosity, basin_map
    )
    return low.reshape(5, rows, 1, LAYERS), high.reshape(5, rows, 1, LAYERS)


def vertical_pair(grid_view, frozen):
    lower_cells = jnp.concatenate(
        [grid_view[..., :1] * (1.0 - frozen)[None, :, :, None], grid_view[..., :-1]], axis=-1
    )
    upper_cells = jnp.concatenate([grid_view[..., 1:], jnp.zeros_like(grid_view[..., :1])], axis=-1)
    return lower_cells + upper_cells


def neighbour_terms(grid_view, x_low, x_high, y_low, y_high, viscosity, frozen):
    shape = grid_view.shape
    y_pad = jnp.concatenate([y_low, grid_view, y_high], axis=2)
    if x_low is None:
        along_line = 2.0 * grid_view
    else:
        x_pad = jnp.concatenate([x_low, grid_view, x_high], axis=1)
        along_line = 2.0 * grid_view - x_pad[:, :-2] - x_pad[:, 2:]
    across_line = y_pad[:, :, :-2] + y_pad[:, :, 2:] + vertical_pair(grid_view, frozen)
    flat = (3, shape[1], shape[2] * shape[3])
    return viscosity * along_line.reshape(flat) - coupling * viscosity * across_line.reshape(flat)


def in_cell_terms(masked, matrix):
    return jnp.sum(matrix * masked[None], axis=1)


def gather_rows(block, axis):
    count, mine = (lax.axis_size(axis), lax.axis_index(axis))
    if count > 8:
        return lax.all_gather(block, axis, axis=1, tiled=True)
    pieces = [block]
    for step in range(1, count):
        pairs = [((i + step) % count, i) for i in range(count)]
        pieces.append(lax.ppermute(block, axis, pairs))
    stacked = jnp.stack(pieces + pieces, axis=0)
    ordered = lax.dynamic_slice_in_dim(stacked, count - mine, count, axis=0)
    ordered = jnp.moveaxis(ordered, 0, 1)
    return ordered.reshape(block.shape[0], count * block.shape[1], *block.shape[2:])


def line_solve(line_lead, line_off, line_rhs):
    rows = line_lead.shape[1]
    gain_prev = jnp.zeros_like(line_rhs[:, 0])
    value_prev = jnp.zeros_like(line_rhs[:, 0])
    gains, values = [], []
    for cell_idx in range(rows):
        off_cell = line_off[:, cell_idx]
        pivot = line_lead[:, cell_idx] - off_cell * gain_prev
        gain_prev = off_cell / pivot
        value_prev = (line_rhs[:, cell_idx] + off_cell * value_prev) / pivot
        gains.append(gain_prev)
        values.append(value_prev)
    next_value = jnp.zeros_like(line_rhs[:, 0])
    corrections = list(values)
    for cell_idx in reversed(range(rows)):
        next_value = values[cell_idx] + gains[cell_idx] * next_value
        corrections[cell_idx] = next_value
    return jnp.stack(corrections, axis=1)


def line_solve_scan(line_lead, line_off, line_rhs):
    def sweep_down(carried, cell_cols):
        gain_prev, value_prev = carried
        lead_cell, off_cell, rhs_cell = cell_cols
        pivot = lead_cell - off_cell * gain_prev
        gain = off_cell / pivot
        value = (rhs_cell + off_cell * value_prev) / pivot
        return (gain, value), (gain, value)

    zeros_line = jnp.zeros_like(line_rhs[:, 0])
    scanned = (jnp.moveaxis(line_lead, 1, 0), jnp.moveaxis(line_off, 1, 0), jnp.moveaxis(line_rhs, 1, 0))
    _, (gains, values) = lax.scan(sweep_down, (zeros_line, zeros_line), scanned)

    def sweep_up(next_value, cell_cols):
        gain, value = cell_cols
        solved = value + gain * next_value
        return solved, solved

    _, corrections = lax.scan(sweep_up, zeros_line, (gains, values), reverse=True)
    return jnp.moveaxis(corrections, 0, 1)


def tree_sum(value, axis):
    count = lax.axis_size(axis)
    if count & (count - 1):
        return lax.psum(value, axis)
    step = 1
    while step < count:
        value = value + lax.ppermute(value, axis, [(i, i ^ step) for i in range(count)])
        step *= 2
    return value


def local(solution, forcing, viscosity, blocks, layer_count, bed_frozen, basin_map):
    row_count = solution.shape[1]
    lane_count = solution.shape[2]
    y_cells = lane_count // LAYERS
    layer_idx = jnp.arange(LAYERS, dtype=jnp.int32)
    active = (
        (layer_idx[None, None, :] < layer_count[:, :, None])
        .astype(jnp.float32)
        .reshape(row_count, lane_count)
    )
    frozen = bed_frozen.astype(jnp.float32)
    matrix = blocks.reshape(4, 4, row_count, lane_count)
    grid = (3, row_count, y_cells, LAYERS)

    masked = solution * active[None]
    masked_grid = masked[:3].reshape(grid)
    low_source, high_source = edge_payloads(solution, layer_count, viscosity, basin_map)
    count = lax.axis_size("gy")
    forward = [(i, i + 1) for i in range(count - 1)]
    backward = [(target, source) for source, target in forward]
    from_low = lax.ppermute(low_source, "gy", forward)
    from_high = lax.ppermute(high_source, "gy", backward)
    y_low, y_high = from_low[:3], from_high[:3]
    in_cell = in_cell_terms(masked, matrix)
    moving = in_cell[:3] + neighbour_terms(masked_grid, None, None, y_low, y_high, viscosity, frozen)
    residual = active[None] * (forcing - jnp.concatenate([moving, in_cell[3:]], axis=0))

    diagonal = jnp.stack([matrix[0, 0], matrix[1, 1], matrix[2, 2]])
    line_lead = jnp.where(active[None] > 0.0, diagonal + 2.0 * viscosity[None], 1.0)
    line_off = (viscosity * active)[None]
    packed = jnp.concatenate([line_lead, line_off, residual[:3], masked[:3]], axis=0)
    whole = gather_rows(packed, "gx")
    all_rows = whole.shape[1]
    whole_off = whole[3:4]
    padded_masked = jnp.pad(whole[7:10], ((0, 0), (1, 1), (0, 0)))
    whole_rhs = whole[4:7] + whole_off * (padded_masked[:, :-2] + padded_masked[:, 2:])
    solver = line_solve if all_rows <= 32 else line_solve_scan
    whole_corr = solver(whole[0:3], jnp.broadcast_to(whole_off, whole_rhs.shape), whole_rhs)

    first = lax.axis_index("gx") * row_count
    padded_corr = jnp.pad(whole_corr, ((0, 0), (1, 1), (0, 0)))
    near_corr = lax.dynamic_slice_in_dim(padded_corr, first, row_count + 2, axis=1)
    near_masked = lax.dynamic_slice_in_dim(padded_masked, first, row_count + 2, axis=1)
    correction = near_corr[:, 1:-1]

    pressure_in = residual[3] - (
        matrix[3, 0] * correction[0] + matrix[3, 1] * correction[1] + matrix[3, 2] * correction[2]
    )
    pressure_step = active * pressure_in / viscosity
    full_step = jnp.concatenate([correction, pressure_step[None]], axis=0)
    smoothed = solution + full_step

    smoothed_masked = smoothed * active[None]
    sm_grid = smoothed_masked[:3].reshape(grid)
    edge = (3, 1, y_cells, LAYERS)
    x_low2 = (near_masked[:, :1] + near_corr[:, :1]).reshape(edge)
    x_high2 = (near_masked[:, -1:] + near_corr[:, -1:]).reshape(edge)
    no_cols = jnp.zeros((3, row_count, 1, LAYERS), jnp.float32)
    in_cell2 = in_cell_terms(smoothed_masked, matrix)
    moving2 = in_cell2[:3] + neighbour_terms(sm_grid, x_low2, x_high2, no_cols, no_cols, viscosity, frozen)
    post = active[None] * (forcing - jnp.concatenate([moving2, in_cell2[3:]], axis=0))
    column_local = jnp.sum(post.reshape(4, row_count, y_cells, LAYERS), axis=-1)

    to_low = jnp.sum(from_low[3:4, :, 0] * sm_grid[:, :, 0], axis=-1)
    to_high = jnp.sum(from_high[3:4, :, 0] * sm_grid[:, :, -1], axis=-1)
    edge_terms = jnp.zeros((3, row_count, y_cells), jnp.float32)
    count = lax.axis_size("gy")
    if count != 4:
        forward = [(i, i + 1) for i in range(count - 1)]
        backward = [(target, source) for source, target in forward]
        for_last = lax.ppermute(to_low, "gy", backward)
        for_first = lax.ppermute(to_high, "gy", forward)
        edge_terms = edge_terms.at[:, :, 0].set(for_first).at[:, :, -1].set(for_last)
        column_residual = column_local + jnp.pad(edge_terms, ((0, 1), (0, 0), (0, 0)))
    basin_count = lax.axis_size("gx") // 2 * lax.axis_size("gy")
    basin_ids = jnp.arange(basin_count, dtype=jnp.int32)
    member = basin_map.reshape(-1)[:, None] == basin_ids[None, :]
    partial_sums = jnp.sum(jnp.where(member[None], column_local.reshape(4, -1)[:, :, None], 0.0), axis=1)
    beside_ids = jnp.concatenate([from_low[4, :, 0, 0], from_high[4, :, 0, 0]]).astype(jnp.int32)
    beside_member = beside_ids[:, None] == basin_ids[None, :]
    beside_terms = jnp.concatenate([to_low, to_high], axis=1)
    beside_sums = jnp.sum(jnp.where(beside_member[None], beside_terms[:, :, None], 0.0), axis=1)
    partial_sums = partial_sums + jnp.pad(beside_sums, ((0, 1), (0, 0)))
    basin_sums = partial_sums
    if count != 4:
        basin_residual = tree_sum(tree_sum(basin_sums, "gx"), "gy")
    else:
        even = lax.axis_index("gy") % 2 == 0
        first_out = jnp.pad(jnp.where(even, to_high, to_low), ((0, 1), (0, 0)))
        second_out = jnp.pad(jnp.where(even, to_low, to_high), ((0, 1), (0, 0)))
        received = []
        for edge_out, pairs in (
            (first_out, [(0, 1), (1, 0), (2, 3), (3, 2)]),
            (second_out, [(1, 2), (2, 1), (3, 0), (0, 3)]),
        ):
            got = lax.ppermute(jnp.concatenate([basin_sums, edge_out], axis=1), "gy", pairs)
            basin_sums = basin_sums + got[:, :basin_count]
            received.append(got[:, basin_count:])
        basin_residual = tree_sum(basin_sums, "gx")
        first_term = jnp.where(even, received[1], received[0])
        last_term = jnp.where(even, received[0], received[1])
        middle = jnp.zeros((4, row_count, y_cells - 2), jnp.float32)
        column_residual = column_local + jnp.concatenate(
            [first_term[:, :, None], middle, last_term[:, :, None]], axis=2
        )
    return (smoothed, column_residual, basin_residual)


def solution(mesh):
    return jax.shard_map(
        local,
        mesh=mesh,
        in_specs=(
            P(None, "gx", "gy"),
            P(None, "gx", "gy"),
            P("gx", "gy"),
            P(None, "gx", "gy"),
            P("gx", "gy"),
            P("gx", "gy"),
            P("gx", "gy"),
        ),
        out_specs=(P(None, "gx", "gy"), P(None, "gx", "gy"), P()),
        check_vma=False,
    )
```

```python
import jax
import jax.numpy as jnp
from jax import lax
from jax.experimental import pallas as pl
from jax.experimental.pallas import tpu as pltpu
from jax.sharding import PartitionSpec as P

LAYERS = 80


coupling = 0.25


def neighbour_shift(block, axis, dim, width):
    count = lax.axis_size(axis)
    forward = [(i, i + 1) for i in range(count - 1)]
    backward = [(target, source) for source, target in forward]
    low = lax.ppermute(lax.slice_in_dim(block, block.shape[dim] - width, None, axis=dim), axis, forward)
    high = lax.ppermute(lax.slice_in_dim(block, 0, width, axis=dim), axis, backward)
    return low, high


def payload_kernel(sol_ref, count_ref, visc_ref, basin_ref, low_ref, high_ref):
    rows = sol_ref.shape[1]
    lanes = sol_ref.shape[2]
    layer = lax.broadcasted_iota(jnp.int32, (rows, LAYERS), 1)
    for out_ref, column in ((low_ref, lanes // LAYERS - 1), (high_ref, 0)):
        start = column * LAYERS
        active = (layer < count_ref[:, column : column + 1]).astype(jnp.float32)
        for k in range(3):
            out_ref[k] = sol_ref[k, :, start : start + LAYERS] * active
        out_ref[3] = coupling * visc_ref[:, start : start + LAYERS] * active
        out_ref[4] = jnp.broadcast_to(basin_ref[:, column : column + 1].astype(jnp.float32), (rows, LAYERS))


def edge_payloads(solution, layer_count, viscosity, basin_map):
    rows = solution.shape[1]
    shape = jax.ShapeDtypeStruct((5, rows, LAYERS), jnp.float32)
    low, high = pl.pallas_call(payload_kernel, out_shape=(shape, shape))(
        solution, layer_count, viscosity, basin_map
    )
    return low.reshape(5, rows, 1, LAYERS), high.reshape(5, rows, 1, LAYERS)


def residual_kernel(sol_ref, force_ref, visc_ref, block_ref, count_ref, frozen_ref, packed_ref, pressure_ref):
    rows, lanes = visc_ref.shape
    lane = lax.broadcasted_iota(jnp.int32, (rows, lanes), 1)
    count_lanes = jnp.broadcast_to(count_ref[:, 0:1], (rows, lanes))
    frozen_lanes = jnp.broadcast_to(frozen_ref[:, 0:1], (rows, lanes))
    base = jnp.zeros((rows, lanes), jnp.int32)
    for column in range(1, lanes // LAYERS):
        later = lane >= column * LAYERS
        count_lanes = jnp.where(later, count_ref[:, column : column + 1], count_lanes)
        frozen_lanes = jnp.where(later, frozen_ref[:, column : column + 1], frozen_lanes)
        base = jnp.where(later, column * LAYERS, base)
    layer = lane - base
    active = (layer < count_lanes).astype(jnp.float32)
    sliding = 1.0 - frozen_lanes.astype(jnp.float32)
    viscosity = visc_ref[...]
    masked = [sol_ref[j] * active for j in range(4)]
    off = viscosity * active
    for k in range(4):
        in_cell = block_ref[4 * k] * masked[0]
        for j in range(1, 4):
            in_cell = in_cell + block_ref[4 * k + j] * masked[j]
        if k == 3:
            pressure_ref[...] = active * (force_ref[3] - in_cell)
            continue
        v = masked[k]
        y_low = jnp.where(lane >= LAYERS, pltpu.roll(v, LAYERS, 1), 0.0)
        y_high = jnp.where(lane < lanes - LAYERS, pltpu.roll(v, lanes - LAYERS, 1), 0.0)
        lower = jnp.where(layer == 0, v * sliding, pltpu.roll(v, 1, 1))
        upper = jnp.where(layer == LAYERS - 1, 0.0, pltpu.roll(v, lanes - 1, 1))
        across = y_low + y_high + (lower + upper)
        moving = in_cell + (viscosity * (2.0 * v) - coupling * viscosity * across)
        packed_ref[4 + k] = active * (force_ref[k] - moving)
        packed_ref[k] = jnp.where(active > 0.0, block_ref[5 * k] + 2.0 * viscosity, 1.0)
        packed_ref[7 + k] = v
    packed_ref[3] = off


def residual_parts(solution, forcing, viscosity, blocks, layer_count, bed_frozen):
    rows, lanes = viscosity.shape
    shapes = (
        jax.ShapeDtypeStruct((10, rows, lanes), jnp.float32),
        jax.ShapeDtypeStruct((rows, lanes), jnp.float32),
    )
    return pl.pallas_call(residual_kernel, out_shape=shapes)(
        solution, forcing, viscosity, blocks, layer_count, bed_frozen
    )


def vertical_pair(grid_view, frozen):
    lower_cells = jnp.concatenate(
        [grid_view[..., :1] * (1.0 - frozen)[None, :, :, None], grid_view[..., :-1]], axis=-1
    )
    upper_cells = jnp.concatenate([grid_view[..., 1:], jnp.zeros_like(grid_view[..., :1])], axis=-1)
    return lower_cells + upper_cells


def neighbour_terms(grid_view, x_low, x_high, y_low, y_high, viscosity, frozen):
    shape = grid_view.shape
    y_pad = jnp.concatenate([y_low, grid_view, y_high], axis=2)
    if x_low is None:
        along_line = 2.0 * grid_view
    else:
        x_pad = jnp.concatenate([x_low, grid_view, x_high], axis=1)
        along_line = 2.0 * grid_view - x_pad[:, :-2] - x_pad[:, 2:]
    across_line = y_pad[:, :, :-2] + y_pad[:, :, 2:] + vertical_pair(grid_view, frozen)
    flat = (3, shape[1], shape[2] * shape[3])
    return viscosity * along_line.reshape(flat) - coupling * viscosity * across_line.reshape(flat)


def in_cell_terms(masked, matrix):
    return jnp.sum(matrix * masked[None], axis=1)


def gather_rows(block, axis):
    count, mine = (lax.axis_size(axis), lax.axis_index(axis))
    if count > 8:
        return lax.all_gather(block, axis, axis=1, tiled=True)
    pieces = [block]
    for step in range(1, count):
        pairs = [((i + step) % count, i) for i in range(count)]
        pieces.append(lax.ppermute(block, axis, pairs))
    stacked = jnp.stack(pieces + pieces, axis=0)
    ordered = lax.dynamic_slice_in_dim(stacked, count - mine, count, axis=0)
    ordered = jnp.moveaxis(ordered, 0, 1)
    return ordered.reshape(block.shape[0], count * block.shape[1], *block.shape[2:])


def line_solve(line_lead, line_off, line_rhs):
    rows = line_lead.shape[1]
    gain_prev = jnp.zeros_like(line_rhs[:, 0])
    value_prev = jnp.zeros_like(line_rhs[:, 0])
    gains, values = [], []
    for cell_idx in range(rows):
        off_cell = line_off[:, cell_idx]
        pivot = line_lead[:, cell_idx] - off_cell * gain_prev
        gain_prev = off_cell / pivot
        value_prev = (line_rhs[:, cell_idx] + off_cell * value_prev) / pivot
        gains.append(gain_prev)
        values.append(value_prev)
    next_value = jnp.zeros_like(line_rhs[:, 0])
    corrections = list(values)
    for cell_idx in reversed(range(rows)):
        next_value = values[cell_idx] + gains[cell_idx] * next_value
        corrections[cell_idx] = next_value
    return jnp.stack(corrections, axis=1)


def line_solve_scan(line_lead, line_off, line_rhs):
    def sweep_down(carried, cell_cols):
        gain_prev, value_prev = carried
        lead_cell, off_cell, rhs_cell = cell_cols
        pivot = lead_cell - off_cell * gain_prev
        gain = off_cell / pivot
        value = (rhs_cell + off_cell * value_prev) / pivot
        return (gain, value), (gain, value)

    zeros_line = jnp.zeros_like(line_rhs[:, 0])
    scanned = (jnp.moveaxis(line_lead, 1, 0), jnp.moveaxis(line_off, 1, 0), jnp.moveaxis(line_rhs, 1, 0))
    _, (gains, values) = lax.scan(sweep_down, (zeros_line, zeros_line), scanned)

    def sweep_up(next_value, cell_cols):
        gain, value = cell_cols
        solved = value + gain * next_value
        return solved, solved

    _, corrections = lax.scan(sweep_up, zeros_line, (gains, values), reverse=True)
    return jnp.moveaxis(corrections, 0, 1)


def tree_sum(value, axis):
    count = lax.axis_size(axis)
    if count & (count - 1):
        return lax.psum(value, axis)
    step = 1
    while step < count:
        value = value + lax.ppermute(value, axis, [(i, i ^ step) for i in range(count)])
        step *= 2
    return value


def local(solution, forcing, viscosity, blocks, layer_count, bed_frozen, basin_map):
    row_count = solution.shape[1]
    lane_count = solution.shape[2]
    y_cells = lane_count // LAYERS
    layer_idx = jnp.arange(LAYERS, dtype=jnp.int32)
    active = (
        (layer_idx[None, None, :] < layer_count[:, :, None])
        .astype(jnp.float32)
        .reshape(row_count, lane_count)
    )
    frozen = bed_frozen.astype(jnp.float32)
    matrix = blocks.reshape(4, 4, row_count, lane_count)
    grid = (3, row_count, y_cells, LAYERS)

    masked = solution * active[None]
    masked_grid = masked[:3].reshape(grid)
    low_source, high_source = edge_payloads(solution, layer_count, viscosity, basin_map)
    count = lax.axis_size("gy")
    forward = [(i, i + 1) for i in range(count - 1)]
    backward = [(target, source) for source, target in forward]
    from_low = lax.ppermute(low_source, "gy", forward)
    from_high = lax.ppermute(high_source, "gy", backward)
    y_low, y_high = from_low[:3], from_high[:3]
    parts, pressure_residual = residual_parts(solution, forcing, viscosity, blocks, layer_count, bed_frozen)
    middle = jnp.zeros((3, row_count, lane_count - 2 * LAYERS), jnp.float32)
    halo_terms = jnp.concatenate(
        [high_source[3:4, :, 0] * y_low[:, :, 0], middle, low_source[3:4, :, 0] * y_high[:, :, 0]], axis=2
    )
    packed = parts + jnp.pad(halo_terms, ((4, 3), (0, 0), (0, 0)))
    residual = pressure_residual[None]
    whole = gather_rows(packed, "gx")
    all_rows = whole.shape[1]
    whole_off = whole[3:4]
    padded_masked = jnp.pad(whole[7:10], ((0, 0), (1, 1), (0, 0)))
    whole_rhs = whole[4:7] + whole_off * (padded_masked[:, :-2] + padded_masked[:, 2:])
    solver = line_solve if all_rows <= 32 else line_solve_scan
    whole_corr = solver(whole[0:3], jnp.broadcast_to(whole_off, whole_rhs.shape), whole_rhs)

    first = lax.axis_index("gx") * row_count
    padded_corr = jnp.pad(whole_corr, ((0, 0), (1, 1), (0, 0)))
    near_corr = lax.dynamic_slice_in_dim(padded_corr, first, row_count + 2, axis=1)
    near_masked = lax.dynamic_slice_in_dim(padded_masked, first, row_count + 2, axis=1)
    correction = near_corr[:, 1:-1]

    pressure_in = residual[0] - (
        matrix[3, 0] * correction[0] + matrix[3, 1] * correction[1] + matrix[3, 2] * correction[2]
    )
    pressure_step = active * pressure_in / viscosity
    full_step = jnp.concatenate([correction, pressure_step[None]], axis=0)
    smoothed = solution + full_step

    smoothed_masked = smoothed * active[None]
    sm_grid = smoothed_masked[:3].reshape(grid)
    edge = (3, 1, y_cells, LAYERS)
    x_low2 = (near_masked[:, :1] + near_corr[:, :1]).reshape(edge)
    x_high2 = (near_masked[:, -1:] + near_corr[:, -1:]).reshape(edge)
    no_cols = jnp.zeros((3, row_count, 1, LAYERS), jnp.float32)
    in_cell2 = in_cell_terms(smoothed_masked, matrix)
    moving2 = in_cell2[:3] + neighbour_terms(sm_grid, x_low2, x_high2, no_cols, no_cols, viscosity, frozen)
    post = active[None] * (forcing - jnp.concatenate([moving2, in_cell2[3:]], axis=0))
    column_local = jnp.sum(post.reshape(4, row_count, y_cells, LAYERS), axis=-1)

    to_low = jnp.sum(from_low[3:4, :, 0] * sm_grid[:, :, 0], axis=-1)
    to_high = jnp.sum(from_high[3:4, :, 0] * sm_grid[:, :, -1], axis=-1)
    edge_terms = jnp.zeros((3, row_count, y_cells), jnp.float32)
    count = lax.axis_size("gy")
    if count != 4:
        forward = [(i, i + 1) for i in range(count - 1)]
        backward = [(target, source) for source, target in forward]
        for_last = lax.ppermute(to_low, "gy", backward)
        for_first = lax.ppermute(to_high, "gy", forward)
        edge_terms = edge_terms.at[:, :, 0].set(for_first).at[:, :, -1].set(for_last)
        column_residual = column_local + jnp.pad(edge_terms, ((0, 1), (0, 0), (0, 0)))
    basin_count = lax.axis_size("gx") // 2 * lax.axis_size("gy")
    basin_ids = jnp.arange(basin_count, dtype=jnp.int32)
    member = basin_map.reshape(-1)[:, None] == basin_ids[None, :]
    partial_sums = jnp.sum(jnp.where(member[None], column_local.reshape(4, -1)[:, :, None], 0.0), axis=1)
    beside_ids = jnp.concatenate([from_low[4, :, 0, 0], from_high[4, :, 0, 0]]).astype(jnp.int32)
    beside_member = beside_ids[:, None] == basin_ids[None, :]
    beside_terms = jnp.concatenate([to_low, to_high], axis=1)
    beside_sums = jnp.sum(jnp.where(beside_member[None], beside_terms[:, :, None], 0.0), axis=1)
    partial_sums = partial_sums + jnp.pad(beside_sums, ((0, 1), (0, 0)))
    basin_sums = partial_sums
    if count != 4:
        basin_residual = tree_sum(tree_sum(basin_sums, "gx"), "gy")
    else:
        even = lax.axis_index("gy") % 2 == 0
        first_out = jnp.pad(jnp.where(even, to_high, to_low), ((0, 1), (0, 0)))
        second_out = jnp.pad(jnp.where(even, to_low, to_high), ((0, 1), (0, 0)))
        received = []
        for edge_out, pairs in (
            (first_out, [(0, 1), (1, 0), (2, 3), (3, 2)]),
            (second_out, [(1, 2), (2, 1), (3, 0), (0, 3)]),
        ):
            got = lax.ppermute(jnp.concatenate([basin_sums, edge_out], axis=1), "gy", pairs)
            basin_sums = basin_sums + got[:, :basin_count]
            received.append(got[:, basin_count:])
        basin_residual = tree_sum(basin_sums, "gx")
        first_term = jnp.where(even, received[1], received[0])
        last_term = jnp.where(even, received[0], received[1])
        middle = jnp.zeros((4, row_count, y_cells - 2), jnp.float32)
        column_residual = column_local + jnp.concatenate(
            [first_term[:, :, None], middle, last_term[:, :, None]], axis=2
        )
    return (smoothed, column_residual, basin_residual)


def solution(mesh):
    return jax.shard_map(
        local,
        mesh=mesh,
        in_specs=(
            P(None, "gx", "gy"),
            P(None, "gx", "gy"),
            P("gx", "gy"),
            P(None, "gx", "gy"),
            P("gx", "gy"),
            P("gx", "gy"),
            P("gx", "gy"),
        ),
        out_specs=(P(None, "gx", "gy"), P(None, "gx", "gy"), P()),
        check_vma=False,
    )
```

```python
import jax
import jax.numpy as jnp
from jax import lax
from jax.experimental import pallas as pl
from jax.experimental.pallas import tpu as pltpu
from jax.sharding import PartitionSpec as P

LAYERS = 80


coupling = 0.25


def neighbour_shift(block, axis, dim, width):
    count = lax.axis_size(axis)
    forward = [(i, i + 1) for i in range(count - 1)]
    backward = [(target, source) for source, target in forward]
    low = lax.ppermute(lax.slice_in_dim(block, block.shape[dim] - width, None, axis=dim), axis, forward)
    high = lax.ppermute(lax.slice_in_dim(block, 0, width, axis=dim), axis, backward)
    return low, high


def payload_kernel(sol_ref, count_ref, visc_ref, basin_ref, low_ref, high_ref):
    rows = sol_ref.shape[1]
    lanes = sol_ref.shape[2]
    layer = lax.broadcasted_iota(jnp.int32, (rows, LAYERS), 1)
    for out_ref, column in ((low_ref, lanes // LAYERS - 1), (high_ref, 0)):
        start = column * LAYERS
        active = (layer < count_ref[:, column : column + 1]).astype(jnp.float32)
        for k in range(3):
            out_ref[k] = sol_ref[k, :, start : start + LAYERS] * active
        out_ref[3] = coupling * visc_ref[:, start : start + LAYERS] * active
        out_ref[4] = jnp.broadcast_to(basin_ref[:, column : column + 1].astype(jnp.float32), (rows, LAYERS))


def edge_payloads(solution, layer_count, viscosity, basin_map):
    rows = solution.shape[1]
    shape = jax.ShapeDtypeStruct((5, rows, LAYERS), jnp.float32)
    low, high = pl.pallas_call(payload_kernel, out_shape=(shape, shape))(
        solution, layer_count, viscosity, basin_map
    )
    return low.reshape(5, rows, 1, LAYERS), high.reshape(5, rows, 1, LAYERS)


def residual_kernel(
    sol_ref, force_ref, visc_ref, block_ref, count_ref, frozen_ref, packed_ref, pressure_ref, active_ref, sliding_ref
):
    rows, lanes = visc_ref.shape
    lane = lax.broadcasted_iota(jnp.int32, (rows, lanes), 1)
    count_lanes = jnp.broadcast_to(count_ref[:, 0:1], (rows, lanes))
    frozen_lanes = jnp.broadcast_to(frozen_ref[:, 0:1], (rows, lanes))
    base = jnp.zeros((rows, lanes), jnp.int32)
    for column in range(1, lanes // LAYERS):
        later = lane >= column * LAYERS
        count_lanes = jnp.where(later, count_ref[:, column : column + 1], count_lanes)
        frozen_lanes = jnp.where(later, frozen_ref[:, column : column + 1], frozen_lanes)
        base = jnp.where(later, column * LAYERS, base)
    layer = lane - base
    active = (layer < count_lanes).astype(jnp.float32)
    sliding = 1.0 - frozen_lanes.astype(jnp.float32)
    viscosity = visc_ref[...]
    masked = [sol_ref[j] * active for j in range(4)]
    off = viscosity * active
    for k in range(4):
        in_cell = block_ref[4 * k] * masked[0]
        for j in range(1, 4):
            in_cell = in_cell + block_ref[4 * k + j] * masked[j]
        if k == 3:
            pressure_ref[...] = active * (force_ref[3] - in_cell)
            continue
        v = masked[k]
        y_low = jnp.where(lane >= LAYERS, pltpu.roll(v, LAYERS, 1), 0.0)
        y_high = jnp.where(lane < lanes - LAYERS, pltpu.roll(v, lanes - LAYERS, 1), 0.0)
        lower = jnp.where(layer == 0, v * sliding, pltpu.roll(v, 1, 1))
        upper = jnp.where(layer == LAYERS - 1, 0.0, pltpu.roll(v, lanes - 1, 1))
        across = y_low + y_high + (lower + upper)
        moving = in_cell + (viscosity * (2.0 * v) - coupling * viscosity * across)
        packed_ref[4 + k] = active * (force_ref[k] - moving)
        packed_ref[k] = jnp.where(active > 0.0, block_ref[5 * k] + 2.0 * viscosity, 1.0)
        packed_ref[7 + k] = v
    packed_ref[3] = off
    active_ref[...] = active
    sliding_ref[...] = 1.0 - frozen_ref[...].astype(jnp.float32)


def residual_parts(solution, forcing, viscosity, blocks, layer_count, bed_frozen):
    rows, lanes = viscosity.shape
    shapes = (
        jax.ShapeDtypeStruct((10, rows, lanes), jnp.float32),
        jax.ShapeDtypeStruct((rows, lanes), jnp.float32),
        jax.ShapeDtypeStruct((rows, lanes), jnp.float32),
        jax.ShapeDtypeStruct(layer_count.shape, jnp.float32),
    )
    return pl.pallas_call(residual_kernel, out_shape=shapes)(
        solution, forcing, viscosity, blocks, layer_count, bed_frozen
    )


def vertical_pair(grid_view, sliding):
    lower_cells = jnp.concatenate(
        [grid_view[..., :1] * sliding[None, :, :, None], grid_view[..., :-1]], axis=-1
    )
    upper_cells = jnp.concatenate([grid_view[..., 1:], jnp.zeros_like(grid_view[..., :1])], axis=-1)
    return lower_cells + upper_cells


def neighbour_terms(grid_view, x_low, x_high, y_low, y_high, viscosity, sliding):
    shape = grid_view.shape
    y_pad = jnp.concatenate([y_low, grid_view, y_high], axis=2)
    if x_low is None:
        along_line = 2.0 * grid_view
    else:
        x_pad = jnp.concatenate([x_low, grid_view, x_high], axis=1)
        along_line = 2.0 * grid_view - x_pad[:, :-2] - x_pad[:, 2:]
    across_line = y_pad[:, :, :-2] + y_pad[:, :, 2:] + vertical_pair(grid_view, sliding)
    flat = (3, shape[1], shape[2] * shape[3])
    return viscosity * along_line.reshape(flat) - coupling * viscosity * across_line.reshape(flat)


def in_cell_terms(masked, matrix):
    return jnp.sum(matrix * masked[None], axis=1)


def gather_rows(block, axis):
    count, mine = (lax.axis_size(axis), lax.axis_index(axis))
    if count > 8:
        return lax.all_gather(block, axis, axis=1, tiled=True)
    pieces = [block]
    for step in range(1, count):
        pairs = [((i + step) % count, i) for i in range(count)]
        pieces.append(lax.ppermute(block, axis, pairs))
    stacked = jnp.stack(pieces + pieces, axis=0)
    ordered = lax.dynamic_slice_in_dim(stacked, count - mine, count, axis=0)
    ordered = jnp.moveaxis(ordered, 0, 1)
    return ordered.reshape(block.shape[0], count * block.shape[1], *block.shape[2:])


def line_solve(line_lead, line_off, line_rhs):
    rows = line_lead.shape[1]
    gain_prev = jnp.zeros_like(line_rhs[:, 0])
    value_prev = jnp.zeros_like(line_rhs[:, 0])
    gains, values = [], []
    for cell_idx in range(rows):
        off_cell = line_off[:, cell_idx]
        pivot = line_lead[:, cell_idx] - off_cell * gain_prev
        gain_prev = off_cell / pivot
        value_prev = (line_rhs[:, cell_idx] + off_cell * value_prev) / pivot
        gains.append(gain_prev)
        values.append(value_prev)
    next_value = jnp.zeros_like(line_rhs[:, 0])
    corrections = list(values)
    for cell_idx in reversed(range(rows)):
        next_value = values[cell_idx] + gains[cell_idx] * next_value
        corrections[cell_idx] = next_value
    return jnp.stack(corrections, axis=1)


def line_solve_scan(line_lead, line_off, line_rhs):
    def sweep_down(carried, cell_cols):
        gain_prev, value_prev = carried
        lead_cell, off_cell, rhs_cell = cell_cols
        pivot = lead_cell - off_cell * gain_prev
        gain = off_cell / pivot
        value = (rhs_cell + off_cell * value_prev) / pivot
        return (gain, value), (gain, value)

    zeros_line = jnp.zeros_like(line_rhs[:, 0])
    scanned = (jnp.moveaxis(line_lead, 1, 0), jnp.moveaxis(line_off, 1, 0), jnp.moveaxis(line_rhs, 1, 0))
    _, (gains, values) = lax.scan(sweep_down, (zeros_line, zeros_line), scanned)

    def sweep_up(next_value, cell_cols):
        gain, value = cell_cols
        solved = value + gain * next_value
        return solved, solved

    _, corrections = lax.scan(sweep_up, zeros_line, (gains, values), reverse=True)
    return jnp.moveaxis(corrections, 0, 1)


def tree_sum(value, axis):
    count = lax.axis_size(axis)
    if count & (count - 1):
        return lax.psum(value, axis)
    step = 1
    while step < count:
        value = value + lax.ppermute(value, axis, [(i, i ^ step) for i in range(count)])
        step *= 2
    return value


def local(solution, forcing, viscosity, blocks, layer_count, bed_frozen, basin_map):
    row_count = solution.shape[1]
    lane_count = solution.shape[2]
    y_cells = lane_count // LAYERS
    matrix = blocks.reshape(4, 4, row_count, lane_count)
    grid = (3, row_count, y_cells, LAYERS)

    low_source, high_source = edge_payloads(solution, layer_count, viscosity, basin_map)
    count = lax.axis_size("gy")
    forward = [(i, i + 1) for i in range(count - 1)]
    backward = [(target, source) for source, target in forward]
    from_low = lax.ppermute(low_source, "gy", forward)
    from_high = lax.ppermute(high_source, "gy", backward)
    y_low, y_high = from_low[:3], from_high[:3]
    parts, pressure_residual, active, sliding = residual_parts(solution, forcing, viscosity, blocks, layer_count, bed_frozen)
    middle = jnp.zeros((3, row_count, lane_count - 2 * LAYERS), jnp.float32)
    halo_terms = jnp.concatenate(
        [high_source[3:4, :, 0] * y_low[:, :, 0], middle, low_source[3:4, :, 0] * y_high[:, :, 0]], axis=2
    )
    packed = parts + jnp.pad(halo_terms, ((4, 3), (0, 0), (0, 0)))
    residual = pressure_residual[None]
    whole = gather_rows(packed, "gx")
    all_rows = whole.shape[1]
    whole_off = whole[3:4]
    padded_masked = jnp.pad(whole[7:10], ((0, 0), (1, 1), (0, 0)))
    whole_rhs = whole[4:7] + whole_off * (padded_masked[:, :-2] + padded_masked[:, 2:])
    solver = line_solve if all_rows <= 32 else line_solve_scan
    whole_corr = solver(whole[0:3], jnp.broadcast_to(whole_off, whole_rhs.shape), whole_rhs)

    first = lax.axis_index("gx") * row_count
    padded_corr = jnp.pad(whole_corr, ((0, 0), (1, 1), (0, 0)))
    near_corr = lax.dynamic_slice_in_dim(padded_corr, first, row_count + 2, axis=1)
    near_masked = lax.dynamic_slice_in_dim(padded_masked, first, row_count + 2, axis=1)
    correction = near_corr[:, 1:-1]

    pressure_in = residual[0] - (
        matrix[3, 0] * correction[0] + matrix[3, 1] * correction[1] + matrix[3, 2] * correction[2]
    )
    pressure_step = active * pressure_in / viscosity
    full_step = jnp.concatenate([correction, pressure_step[None]], axis=0)
    smoothed = solution + full_step

    smoothed_masked = smoothed * active[None]
    sm_grid = smoothed_masked[:3].reshape(grid)
    edge = (3, 1, y_cells, LAYERS)
    x_low2 = (near_masked[:, :1] + near_corr[:, :1]).reshape(edge)
    x_high2 = (near_masked[:, -1:] + near_corr[:, -1:]).reshape(edge)
    no_cols = jnp.zeros((3, row_count, 1, LAYERS), jnp.float32)
    in_cell2 = in_cell_terms(smoothed_masked, matrix)
    moving2 = in_cell2[:3] + neighbour_terms(sm_grid, x_low2, x_high2, no_cols, no_cols, viscosity, sliding)
    post = active[None] * (forcing - jnp.concatenate([moving2, in_cell2[3:]], axis=0))
    column_local = jnp.sum(post.reshape(4, row_count, y_cells, LAYERS), axis=-1)

    to_low = jnp.sum(from_low[3:4, :, 0] * sm_grid[:, :, 0], axis=-1)
    to_high = jnp.sum(from_high[3:4, :, 0] * sm_grid[:, :, -1], axis=-1)
    edge_terms = jnp.zeros((3, row_count, y_cells), jnp.float32)
    count = lax.axis_size("gy")
    if count != 4:
        forward = [(i, i + 1) for i in range(count - 1)]
        backward = [(target, source) for source, target in forward]
        for_last = lax.ppermute(to_low, "gy", backward)
        for_first = lax.ppermute(to_high, "gy", forward)
        edge_terms = edge_terms.at[:, :, 0].set(for_first).at[:, :, -1].set(for_last)
        column_residual = column_local + jnp.pad(edge_terms, ((0, 1), (0, 0), (0, 0)))
    basin_count = lax.axis_size("gx") // 2 * lax.axis_size("gy")
    basin_ids = jnp.arange(basin_count, dtype=jnp.int32)
    member = basin_map.reshape(-1)[:, None] == basin_ids[None, :]
    partial_sums = jnp.sum(jnp.where(member[None], column_local.reshape(4, -1)[:, :, None], 0.0), axis=1)
    beside_ids = jnp.concatenate([from_low[4, :, 0, 0], from_high[4, :, 0, 0]]).astype(jnp.int32)
    beside_member = beside_ids[:, None] == basin_ids[None, :]
    beside_terms = jnp.concatenate([to_low, to_high], axis=1)
    beside_sums = jnp.sum(jnp.where(beside_member[None], beside_terms[:, :, None], 0.0), axis=1)
    partial_sums = partial_sums + jnp.pad(beside_sums, ((0, 1), (0, 0)))
    basin_sums = partial_sums
    if count != 4:
        basin_residual = tree_sum(tree_sum(basin_sums, "gx"), "gy")
    else:
        even = lax.axis_index("gy") % 2 == 0
        first_out = jnp.pad(jnp.where(even, to_high, to_low), ((0, 1), (0, 0)))
        second_out = jnp.pad(jnp.where(even, to_low, to_high), ((0, 1), (0, 0)))
        received = []
        for edge_out, pairs in (
            (first_out, [(0, 1), (1, 0), (2, 3), (3, 2)]),
            (second_out, [(1, 2), (2, 1), (3, 0), (0, 3)]),
        ):
            got = lax.ppermute(jnp.concatenate([basin_sums, edge_out], axis=1), "gy", pairs)
            basin_sums = basin_sums + got[:, :basin_count]
            received.append(got[:, basin_count:])
        basin_residual = tree_sum(basin_sums, "gx")
        first_term = jnp.where(even, received[1], received[0])
        last_term = jnp.where(even, received[0], received[1])
        middle = jnp.zeros((4, row_count, y_cells - 2), jnp.float32)
        column_residual = column_local + jnp.concatenate(
            [first_term[:, :, None], middle, last_term[:, :, None]], axis=2
        )
    return (smoothed, column_residual, basin_residual)


def solution(mesh):
    return jax.shard_map(
        local,
        mesh=mesh,
        in_specs=(
            P(None, "gx", "gy"),
            P(None, "gx", "gy"),
            P("gx", "gy"),
            P(None, "gx", "gy"),
            P("gx", "gy"),
            P("gx", "gy"),
            P("gx", "gy"),
        ),
        out_specs=(P(None, "gx", "gy"), P(None, "gx", "gy"), P()),
        check_vma=False,
    )
```

```python
import jax
import jax.numpy as jnp
from jax import lax
from jax.experimental import pallas as pl
from jax.experimental.pallas import tpu as pltpu
from jax.sharding import PartitionSpec as P

LAYERS = 80


coupling = 0.25


def neighbour_shift(block, axis, dim, width):
    count = lax.axis_size(axis)
    forward = [(i, i + 1) for i in range(count - 1)]
    backward = [(target, source) for source, target in forward]
    low = lax.ppermute(lax.slice_in_dim(block, block.shape[dim] - width, None, axis=dim), axis, forward)
    high = lax.ppermute(lax.slice_in_dim(block, 0, width, axis=dim), axis, backward)
    return low, high


def payload_kernel(sol_ref, count_ref, visc_ref, basin_ref, low_ref, high_ref):
    rows = sol_ref.shape[1]
    lanes = sol_ref.shape[2]
    layer = lax.broadcasted_iota(jnp.int32, (rows, LAYERS), 1)
    for out_ref, column in ((low_ref, lanes // LAYERS - 1), (high_ref, 0)):
        start = column * LAYERS
        active = (layer < count_ref[:, column : column + 1]).astype(jnp.float32)
        for k in range(3):
            out_ref[k] = sol_ref[k, :, start : start + LAYERS] * active
        out_ref[3] = coupling * visc_ref[:, start : start + LAYERS] * active
        out_ref[4] = jnp.broadcast_to(basin_ref[:, column : column + 1].astype(jnp.float32), (rows, LAYERS))


def edge_payloads(solution, layer_count, viscosity, basin_map):
    rows = solution.shape[1]
    shape = jax.ShapeDtypeStruct((5, rows, LAYERS), jnp.float32)
    low, high = pl.pallas_call(payload_kernel, out_shape=(shape, shape))(
        solution, layer_count, viscosity, basin_map
    )
    return low.reshape(5, rows, 1, LAYERS), high.reshape(5, rows, 1, LAYERS)


def residual_kernel(
    sol_ref, force_ref, visc_ref, block_ref, count_ref, frozen_ref, low_ref, high_ref,
    packed_ref, pressure_ref, active_ref, sliding_ref,
):
    rows, lanes = visc_ref.shape
    lane = lax.broadcasted_iota(jnp.int32, (rows, lanes), 1)
    count_lanes = jnp.broadcast_to(count_ref[:, 0:1], (rows, lanes))
    frozen_lanes = jnp.broadcast_to(frozen_ref[:, 0:1], (rows, lanes))
    base = jnp.zeros((rows, lanes), jnp.int32)
    for column in range(1, lanes // LAYERS):
        later = lane >= column * LAYERS
        count_lanes = jnp.where(later, count_ref[:, column : column + 1], count_lanes)
        frozen_lanes = jnp.where(later, frozen_ref[:, column : column + 1], frozen_lanes)
        base = jnp.where(later, column * LAYERS, base)
    layer = lane - base
    active = (layer < count_lanes).astype(jnp.float32)
    sliding = 1.0 - frozen_lanes.astype(jnp.float32)
    viscosity = visc_ref[...]
    masked = [sol_ref[j] * active for j in range(4)]
    off = viscosity * active
    for k in range(4):
        in_cell = block_ref[4 * k] * masked[0]
        for j in range(1, 4):
            in_cell = in_cell + block_ref[4 * k + j] * masked[j]
        if k == 3:
            pressure_ref[...] = active * (force_ref[3] - in_cell)
            continue
        v = masked[k]
        y_low = jnp.where(lane >= LAYERS, pltpu.roll(v, LAYERS, 1), low_ref[k])
        y_high = jnp.where(lane < lanes - LAYERS, pltpu.roll(v, lanes - LAYERS, 1), high_ref[k])
        lower = jnp.where(layer == 0, v * sliding, pltpu.roll(v, 1, 1))
        upper = jnp.where(layer == LAYERS - 1, 0.0, pltpu.roll(v, lanes - 1, 1))
        across = y_low + y_high + (lower + upper)
        moving = in_cell + (viscosity * (2.0 * v) - coupling * viscosity * across)
        packed_ref[4 + k] = active * (force_ref[k] - moving)
        packed_ref[k] = jnp.where(active > 0.0, block_ref[5 * k] + 2.0 * viscosity, 1.0)
        packed_ref[7 + k] = v
    packed_ref[3] = off
    active_ref[...] = active
    sliding_ref[...] = 1.0 - frozen_ref[...].astype(jnp.float32)


def residual_parts(solution, forcing, viscosity, blocks, layer_count, bed_frozen, y_low, y_high):
    rows, lanes = viscosity.shape
    shapes = (
        jax.ShapeDtypeStruct((10, rows, lanes), jnp.float32),
        jax.ShapeDtypeStruct((rows, lanes), jnp.float32),
        jax.ShapeDtypeStruct((rows, lanes), jnp.float32),
        jax.ShapeDtypeStruct(layer_count.shape, jnp.float32),
    )
    return pl.pallas_call(residual_kernel, out_shape=shapes)(
        solution, forcing, viscosity, blocks, layer_count, bed_frozen, y_low, y_high
    )


def vertical_pair(grid_view, sliding):
    lower_cells = jnp.concatenate(
        [grid_view[..., :1] * sliding[None, :, :, None], grid_view[..., :-1]], axis=-1
    )
    upper_cells = jnp.concatenate([grid_view[..., 1:], jnp.zeros_like(grid_view[..., :1])], axis=-1)
    return lower_cells + upper_cells


def neighbour_terms(grid_view, x_low, x_high, y_low, y_high, viscosity, sliding):
    shape = grid_view.shape
    y_pad = jnp.concatenate([y_low, grid_view, y_high], axis=2)
    if x_low is None:
        along_line = 2.0 * grid_view
    else:
        x_pad = jnp.concatenate([x_low, grid_view, x_high], axis=1)
        along_line = 2.0 * grid_view - x_pad[:, :-2] - x_pad[:, 2:]
    across_line = y_pad[:, :, :-2] + y_pad[:, :, 2:] + vertical_pair(grid_view, sliding)
    flat = (3, shape[1], shape[2] * shape[3])
    return viscosity * along_line.reshape(flat) - coupling * viscosity * across_line.reshape(flat)


def in_cell_terms(masked, matrix):
    return jnp.sum(matrix * masked[None], axis=1)


def gather_rows(block, axis):
    count, mine = (lax.axis_size(axis), lax.axis_index(axis))
    if count > 8:
        return lax.all_gather(block, axis, axis=1, tiled=True)
    pieces = [block]
    for step in range(1, count):
        pairs = [((i + step) % count, i) for i in range(count)]
        pieces.append(lax.ppermute(block, axis, pairs))
    stacked = jnp.stack(pieces + pieces, axis=0)
    ordered = lax.dynamic_slice_in_dim(stacked, count - mine, count, axis=0)
    ordered = jnp.moveaxis(ordered, 0, 1)
    return ordered.reshape(block.shape[0], count * block.shape[1], *block.shape[2:])


def line_solve(line_lead, line_off, line_rhs):
    rows = line_lead.shape[1]
    gain_prev = jnp.zeros_like(line_rhs[:, 0])
    value_prev = jnp.zeros_like(line_rhs[:, 0])
    gains, values = [], []
    for cell_idx in range(rows):
        off_cell = line_off[:, cell_idx]
        pivot = line_lead[:, cell_idx] - off_cell * gain_prev
        gain_prev = off_cell / pivot
        value_prev = (line_rhs[:, cell_idx] + off_cell * value_prev) / pivot
        gains.append(gain_prev)
        values.append(value_prev)
    next_value = jnp.zeros_like(line_rhs[:, 0])
    corrections = list(values)
    for cell_idx in reversed(range(rows)):
        next_value = values[cell_idx] + gains[cell_idx] * next_value
        corrections[cell_idx] = next_value
    return jnp.stack(corrections, axis=1)


def line_solve_scan(line_lead, line_off, line_rhs):
    def sweep_down(carried, cell_cols):
        gain_prev, value_prev = carried
        lead_cell, off_cell, rhs_cell = cell_cols
        pivot = lead_cell - off_cell * gain_prev
        gain = off_cell / pivot
        value = (rhs_cell + off_cell * value_prev) / pivot
        return (gain, value), (gain, value)

    zeros_line = jnp.zeros_like(line_rhs[:, 0])
    scanned = (jnp.moveaxis(line_lead, 1, 0), jnp.moveaxis(line_off, 1, 0), jnp.moveaxis(line_rhs, 1, 0))
    _, (gains, values) = lax.scan(sweep_down, (zeros_line, zeros_line), scanned)

    def sweep_up(next_value, cell_cols):
        gain, value = cell_cols
        solved = value + gain * next_value
        return solved, solved

    _, corrections = lax.scan(sweep_up, zeros_line, (gains, values), reverse=True)
    return jnp.moveaxis(corrections, 0, 1)


def tree_sum(value, axis):
    count = lax.axis_size(axis)
    if count & (count - 1):
        return lax.psum(value, axis)
    step = 1
    while step < count:
        value = value + lax.ppermute(value, axis, [(i, i ^ step) for i in range(count)])
        step *= 2
    return value


def local(solution, forcing, viscosity, blocks, layer_count, bed_frozen, basin_map):
    row_count = solution.shape[1]
    lane_count = solution.shape[2]
    y_cells = lane_count // LAYERS
    matrix = blocks.reshape(4, 4, row_count, lane_count)
    grid = (3, row_count, y_cells, LAYERS)

    low_source, high_source = edge_payloads(solution, layer_count, viscosity, basin_map)
    count = lax.axis_size("gy")
    forward = [(i, i + 1) for i in range(count - 1)]
    backward = [(target, source) for source, target in forward]
    from_low = lax.ppermute(low_source, "gy", forward)
    from_high = lax.ppermute(high_source, "gy", backward)
    y_low, y_high = from_low[:3], from_high[:3]
    rest = lane_count - LAYERS
    low_lanes = jnp.pad(y_low[:, :, 0], ((0, 0), (0, 0), (0, rest)))
    high_lanes = jnp.pad(y_high[:, :, 0], ((0, 0), (0, 0), (rest, 0)))
    packed, pressure_residual, active, sliding = residual_parts(
        solution, forcing, viscosity, blocks, layer_count, bed_frozen, low_lanes, high_lanes
    )
    residual = pressure_residual[None]
    whole = gather_rows(packed, "gx")
    all_rows = whole.shape[1]
    whole_off = whole[3:4]
    padded_masked = jnp.pad(whole[7:10], ((0, 0), (1, 1), (0, 0)))
    whole_rhs = whole[4:7] + whole_off * (padded_masked[:, :-2] + padded_masked[:, 2:])
    solver = line_solve if all_rows <= 32 else line_solve_scan
    whole_corr = solver(whole[0:3], jnp.broadcast_to(whole_off, whole_rhs.shape), whole_rhs)

    first = lax.axis_index("gx") * row_count
    padded_corr = jnp.pad(whole_corr, ((0, 0), (1, 1), (0, 0)))
    near_corr = lax.dynamic_slice_in_dim(padded_corr, first, row_count + 2, axis=1)
    near_masked = lax.dynamic_slice_in_dim(padded_masked, first, row_count + 2, axis=1)
    correction = near_corr[:, 1:-1]

    pressure_in = residual[0] - (
        matrix[3, 0] * correction[0] + matrix[3, 1] * correction[1] + matrix[3, 2] * correction[2]
    )
    pressure_step = active * pressure_in / viscosity
    full_step = jnp.concatenate([correction, pressure_step[None]], axis=0)
    smoothed = solution + full_step

    smoothed_masked = smoothed * active[None]
    sm_grid = smoothed_masked[:3].reshape(grid)
    edge = (3, 1, y_cells, LAYERS)
    x_low2 = (near_masked[:, :1] + near_corr[:, :1]).reshape(edge)
    x_high2 = (near_masked[:, -1:] + near_corr[:, -1:]).reshape(edge)
    no_cols = jnp.zeros((3, row_count, 1, LAYERS), jnp.float32)
    in_cell2 = in_cell_terms(smoothed_masked, matrix)
    moving2 = in_cell2[:3] + neighbour_terms(sm_grid, x_low2, x_high2, no_cols, no_cols, viscosity, sliding)
    post = active[None] * (forcing - jnp.concatenate([moving2, in_cell2[3:]], axis=0))
    column_local = jnp.sum(post.reshape(4, row_count, y_cells, LAYERS), axis=-1)

    to_low = jnp.sum(from_low[3:4, :, 0] * sm_grid[:, :, 0], axis=-1)
    to_high = jnp.sum(from_high[3:4, :, 0] * sm_grid[:, :, -1], axis=-1)
    edge_terms = jnp.zeros((3, row_count, y_cells), jnp.float32)
    count = lax.axis_size("gy")
    if count != 4:
        forward = [(i, i + 1) for i in range(count - 1)]
        backward = [(target, source) for source, target in forward]
        for_last = lax.ppermute(to_low, "gy", backward)
        for_first = lax.ppermute(to_high, "gy", forward)
        edge_terms = edge_terms.at[:, :, 0].set(for_first).at[:, :, -1].set(for_last)
        column_residual = column_local + jnp.pad(edge_terms, ((0, 1), (0, 0), (0, 0)))
    basin_count = lax.axis_size("gx") // 2 * lax.axis_size("gy")
    basin_ids = jnp.arange(basin_count, dtype=jnp.int32)
    member = basin_map.reshape(-1)[:, None] == basin_ids[None, :]
    partial_sums = jnp.sum(jnp.where(member[None], column_local.reshape(4, -1)[:, :, None], 0.0), axis=1)
    beside_ids = jnp.concatenate([from_low[4, :, 0, 0], from_high[4, :, 0, 0]]).astype(jnp.int32)
    beside_member = beside_ids[:, None] == basin_ids[None, :]
    beside_terms = jnp.concatenate([to_low, to_high], axis=1)
    beside_sums = jnp.sum(jnp.where(beside_member[None], beside_terms[:, :, None], 0.0), axis=1)
    partial_sums = partial_sums + jnp.pad(beside_sums, ((0, 1), (0, 0)))
    basin_sums = partial_sums
    if count != 4:
        basin_residual = tree_sum(tree_sum(basin_sums, "gx"), "gy")
    else:
        even = lax.axis_index("gy") % 2 == 0
        first_out = jnp.pad(jnp.where(even, to_high, to_low), ((0, 1), (0, 0)))
        second_out = jnp.pad(jnp.where(even, to_low, to_high), ((0, 1), (0, 0)))
        received = []
        for edge_out, pairs in (
            (first_out, [(0, 1), (1, 0), (2, 3), (3, 2)]),
            (second_out, [(1, 2), (2, 1), (3, 0), (0, 3)]),
        ):
            got = lax.ppermute(jnp.concatenate([basin_sums, edge_out], axis=1), "gy", pairs)
            basin_sums = basin_sums + got[:, :basin_count]
            received.append(got[:, basin_count:])
        basin_residual = tree_sum(basin_sums, "gx")
        first_term = jnp.where(even, received[1], received[0])
        last_term = jnp.where(even, received[0], received[1])
        middle = jnp.zeros((4, row_count, y_cells - 2), jnp.float32)
        column_residual = column_local + jnp.concatenate(
            [first_term[:, :, None], middle, last_term[:, :, None]], axis=2
        )
    return (smoothed, column_residual, basin_residual)


def solution(mesh):
    return jax.shard_map(
        local,
        mesh=mesh,
        in_specs=(
            P(None, "gx", "gy"),
            P(None, "gx", "gy"),
            P("gx", "gy"),
            P(None, "gx", "gy"),
            P("gx", "gy"),
            P("gx", "gy"),
            P("gx", "gy"),
        ),
        out_specs=(P(None, "gx", "gy"), P(None, "gx", "gy"), P()),
        check_vma=False,
    )
```

```python
import jax
import jax.numpy as jnp
from jax import lax
from jax.experimental import pallas as pl
from jax.experimental.pallas import tpu as pltpu
from jax.sharding import PartitionSpec as P

LAYERS = 80


coupling = 0.25


def neighbour_shift(block, axis, dim, width):
    count = lax.axis_size(axis)
    forward = [(i, i + 1) for i in range(count - 1)]
    backward = [(target, source) for source, target in forward]
    low = lax.ppermute(lax.slice_in_dim(block, block.shape[dim] - width, None, axis=dim), axis, forward)
    high = lax.ppermute(lax.slice_in_dim(block, 0, width, axis=dim), axis, backward)
    return low, high


def payload_kernel(sol_ref, count_ref, visc_ref, basin_ref, low_ref, high_ref):
    rows = sol_ref.shape[1]
    lanes = sol_ref.shape[2]
    layer = lax.broadcasted_iota(jnp.int32, (rows, LAYERS), 1)
    for out_ref, column in ((low_ref, lanes // LAYERS - 1), (high_ref, 0)):
        start = column * LAYERS
        active = (layer < count_ref[:, column : column + 1]).astype(jnp.float32)
        for k in range(3):
            out_ref[k] = sol_ref[k, :, start : start + LAYERS] * active
        out_ref[3] = coupling * visc_ref[:, start : start + LAYERS] * active
        out_ref[4] = jnp.broadcast_to(basin_ref[:, column : column + 1].astype(jnp.float32), (rows, LAYERS))


def edge_payloads(solution, layer_count, viscosity, basin_map):
    rows = solution.shape[1]
    shape = jax.ShapeDtypeStruct((5, rows, LAYERS), jnp.float32)
    low, high = pl.pallas_call(payload_kernel, out_shape=(shape, shape))(
        solution, layer_count, viscosity, basin_map
    )
    return low.reshape(5, rows, 1, LAYERS), high.reshape(5, rows, 1, LAYERS)


def residual_kernel(
    sol_ref, force_ref, visc_ref, block_ref, count_ref, frozen_ref, low_ref, high_ref,
    packed_ref, pressure_ref, active_ref, sliding_ref,
):
    rows, lanes = visc_ref.shape
    lane = lax.broadcasted_iota(jnp.int32, (rows, lanes), 1)
    count_lanes = jnp.broadcast_to(count_ref[:, 0:1], (rows, lanes))
    frozen_lanes = jnp.broadcast_to(frozen_ref[:, 0:1], (rows, lanes))
    base = jnp.zeros((rows, lanes), jnp.int32)
    for column in range(1, lanes // LAYERS):
        later = lane >= column * LAYERS
        count_lanes = jnp.where(later, count_ref[:, column : column + 1], count_lanes)
        frozen_lanes = jnp.where(later, frozen_ref[:, column : column + 1], frozen_lanes)
        base = jnp.where(later, column * LAYERS, base)
    layer = lane - base
    active = (layer < count_lanes).astype(jnp.float32)
    sliding = 1.0 - frozen_lanes.astype(jnp.float32)
    viscosity = visc_ref[...]
    masked = [sol_ref[j] * active for j in range(4)]
    off = viscosity * active
    for k in range(4):
        in_cell = block_ref[4 * k] * masked[0]
        for j in range(1, 4):
            in_cell = in_cell + block_ref[4 * k + j] * masked[j]
        if k == 3:
            pressure_ref[...] = active * (force_ref[3] - in_cell)
            continue
        v = masked[k]
        zeros_rest = jnp.zeros((rows, lanes - LAYERS), jnp.float32)
        low_lanes = jnp.concatenate([low_ref[k, :, 0], zeros_rest], axis=1)
        high_lanes = jnp.concatenate([zeros_rest, high_ref[k, :, 0]], axis=1)
        y_low = jnp.where(lane >= LAYERS, pltpu.roll(v, LAYERS, 1), low_lanes)
        y_high = jnp.where(lane < lanes - LAYERS, pltpu.roll(v, lanes - LAYERS, 1), high_lanes)
        lower = jnp.where(layer == 0, v * sliding, pltpu.roll(v, 1, 1))
        upper = jnp.where(layer == LAYERS - 1, 0.0, pltpu.roll(v, lanes - 1, 1))
        across = y_low + y_high + (lower + upper)
        moving = in_cell + (viscosity * (2.0 * v) - coupling * viscosity * across)
        packed_ref[4 + k] = active * (force_ref[k] - moving)
        packed_ref[k] = jnp.where(active > 0.0, block_ref[5 * k] + 2.0 * viscosity, 1.0)
        packed_ref[7 + k] = v
    packed_ref[3] = off
    active_ref[...] = active
    sliding_ref[...] = 1.0 - frozen_ref[...].astype(jnp.float32)


def residual_parts(solution, forcing, viscosity, blocks, layer_count, bed_frozen, y_low, y_high):
    rows, lanes = viscosity.shape
    shapes = (
        jax.ShapeDtypeStruct((10, rows, lanes), jnp.float32),
        jax.ShapeDtypeStruct((rows, lanes), jnp.float32),
        jax.ShapeDtypeStruct((rows, lanes), jnp.float32),
        jax.ShapeDtypeStruct(layer_count.shape, jnp.float32),
    )
    return pl.pallas_call(residual_kernel, out_shape=shapes)(
        solution, forcing, viscosity, blocks, layer_count, bed_frozen, y_low, y_high
    )


def vertical_pair(grid_view, sliding):
    lower_cells = jnp.concatenate(
        [grid_view[..., :1] * sliding[None, :, :, None], grid_view[..., :-1]], axis=-1
    )
    upper_cells = jnp.concatenate([grid_view[..., 1:], jnp.zeros_like(grid_view[..., :1])], axis=-1)
    return lower_cells + upper_cells


def neighbour_terms(grid_view, x_low, x_high, y_low, y_high, viscosity, sliding):
    shape = grid_view.shape
    y_pad = jnp.concatenate([y_low, grid_view, y_high], axis=2)
    if x_low is None:
        along_line = 2.0 * grid_view
    else:
        x_pad = jnp.concatenate([x_low, grid_view, x_high], axis=1)
        along_line = 2.0 * grid_view - x_pad[:, :-2] - x_pad[:, 2:]
    across_line = y_pad[:, :, :-2] + y_pad[:, :, 2:] + vertical_pair(grid_view, sliding)
    flat = (3, shape[1], shape[2] * shape[3])
    return viscosity * along_line.reshape(flat) - coupling * viscosity * across_line.reshape(flat)


def in_cell_terms(masked, matrix):
    return jnp.sum(matrix * masked[None], axis=1)


def gather_rows(block, axis):
    count, mine = (lax.axis_size(axis), lax.axis_index(axis))
    if count > 8:
        return lax.all_gather(block, axis, axis=1, tiled=True)
    pieces = [block]
    for step in range(1, count):
        pairs = [((i + step) % count, i) for i in range(count)]
        pieces.append(lax.ppermute(block, axis, pairs))
    stacked = jnp.stack(pieces + pieces, axis=0)
    ordered = lax.dynamic_slice_in_dim(stacked, count - mine, count, axis=0)
    ordered = jnp.moveaxis(ordered, 0, 1)
    return ordered.reshape(block.shape[0], count * block.shape[1], *block.shape[2:])


def line_solve(line_lead, line_off, line_rhs):
    rows = line_lead.shape[1]
    gain_prev = jnp.zeros_like(line_rhs[:, 0])
    value_prev = jnp.zeros_like(line_rhs[:, 0])
    gains, values = [], []
    for cell_idx in range(rows):
        off_cell = line_off[:, cell_idx]
        pivot = line_lead[:, cell_idx] - off_cell * gain_prev
        gain_prev = off_cell / pivot
        value_prev = (line_rhs[:, cell_idx] + off_cell * value_prev) / pivot
        gains.append(gain_prev)
        values.append(value_prev)
    next_value = jnp.zeros_like(line_rhs[:, 0])
    corrections = list(values)
    for cell_idx in reversed(range(rows)):
        next_value = values[cell_idx] + gains[cell_idx] * next_value
        corrections[cell_idx] = next_value
    return jnp.stack(corrections, axis=1)


def line_solve_scan(line_lead, line_off, line_rhs):
    def sweep_down(carried, cell_cols):
        gain_prev, value_prev = carried
        lead_cell, off_cell, rhs_cell = cell_cols
        pivot = lead_cell - off_cell * gain_prev
        gain = off_cell / pivot
        value = (rhs_cell + off_cell * value_prev) / pivot
        return (gain, value), (gain, value)

    zeros_line = jnp.zeros_like(line_rhs[:, 0])
    scanned = (jnp.moveaxis(line_lead, 1, 0), jnp.moveaxis(line_off, 1, 0), jnp.moveaxis(line_rhs, 1, 0))
    _, (gains, values) = lax.scan(sweep_down, (zeros_line, zeros_line), scanned)

    def sweep_up(next_value, cell_cols):
        gain, value = cell_cols
        solved = value + gain * next_value
        return solved, solved

    _, corrections = lax.scan(sweep_up, zeros_line, (gains, values), reverse=True)
    return jnp.moveaxis(corrections, 0, 1)


def tree_sum(value, axis):
    count = lax.axis_size(axis)
    if count & (count - 1):
        return lax.psum(value, axis)
    step = 1
    while step < count:
        value = value + lax.ppermute(value, axis, [(i, i ^ step) for i in range(count)])
        step *= 2
    return value


def local(solution, forcing, viscosity, blocks, layer_count, bed_frozen, basin_map):
    row_count = solution.shape[1]
    lane_count = solution.shape[2]
    y_cells = lane_count // LAYERS
    matrix = blocks.reshape(4, 4, row_count, lane_count)
    grid = (3, row_count, y_cells, LAYERS)

    low_source, high_source = edge_payloads(solution, layer_count, viscosity, basin_map)
    count = lax.axis_size("gy")
    forward = [(i, i + 1) for i in range(count - 1)]
    backward = [(target, source) for source, target in forward]
    from_low = lax.ppermute(low_source, "gy", forward)
    from_high = lax.ppermute(high_source, "gy", backward)
    y_low, y_high = from_low[:3], from_high[:3]
    packed, pressure_residual, active, sliding = residual_parts(
        solution, forcing, viscosity, blocks, layer_count, bed_frozen, from_low, from_high
    )
    residual = pressure_residual[None]
    whole = gather_rows(packed, "gx")
    all_rows = whole.shape[1]
    whole_off = whole[3:4]
    padded_masked = jnp.pad(whole[7:10], ((0, 0), (1, 1), (0, 0)))
    whole_rhs = whole[4:7] + whole_off * (padded_masked[:, :-2] + padded_masked[:, 2:])
    solver = line_solve if all_rows <= 32 else line_solve_scan
    whole_corr = solver(whole[0:3], jnp.broadcast_to(whole_off, whole_rhs.shape), whole_rhs)

    first = lax.axis_index("gx") * row_count
    padded_corr = jnp.pad(whole_corr, ((0, 0), (1, 1), (0, 0)))
    near_corr = lax.dynamic_slice_in_dim(padded_corr, first, row_count + 2, axis=1)
    near_masked = lax.dynamic_slice_in_dim(padded_masked, first, row_count + 2, axis=1)
    correction = near_corr[:, 1:-1]

    pressure_in = residual[0] - (
        matrix[3, 0] * correction[0] + matrix[3, 1] * correction[1] + matrix[3, 2] * correction[2]
    )
    pressure_step = active * pressure_in / viscosity
    full_step = jnp.concatenate([correction, pressure_step[None]], axis=0)
    smoothed = solution + full_step

    smoothed_masked = smoothed * active[None]
    sm_grid = smoothed_masked[:3].reshape(grid)
    edge = (3, 1, y_cells, LAYERS)
    x_low2 = (near_masked[:, :1] + near_corr[:, :1]).reshape(edge)
    x_high2 = (near_masked[:, -1:] + near_corr[:, -1:]).reshape(edge)
    no_cols = jnp.zeros((3, row_count, 1, LAYERS), jnp.float32)
    in_cell2 = in_cell_terms(smoothed_masked, matrix)
    moving2 = in_cell2[:3] + neighbour_terms(sm_grid, x_low2, x_high2, no_cols, no_cols, viscosity, sliding)
    post = active[None] * (forcing - jnp.concatenate([moving2, in_cell2[3:]], axis=0))
    column_local = jnp.sum(post.reshape(4, row_count, y_cells, LAYERS), axis=-1)

    to_low = jnp.sum(from_low[3:4, :, 0] * sm_grid[:, :, 0], axis=-1)
    to_high = jnp.sum(from_high[3:4, :, 0] * sm_grid[:, :, -1], axis=-1)
    edge_terms = jnp.zeros((3, row_count, y_cells), jnp.float32)
    count = lax.axis_size("gy")
    if count != 4:
        forward = [(i, i + 1) for i in range(count - 1)]
        backward = [(target, source) for source, target in forward]
        for_last = lax.ppermute(to_low, "gy", backward)
        for_first = lax.ppermute(to_high, "gy", forward)
        edge_terms = edge_terms.at[:, :, 0].set(for_first).at[:, :, -1].set(for_last)
        column_residual = column_local + jnp.pad(edge_terms, ((0, 1), (0, 0), (0, 0)))
    basin_count = lax.axis_size("gx") // 2 * lax.axis_size("gy")
    basin_ids = jnp.arange(basin_count, dtype=jnp.int32)
    member = basin_map.reshape(-1)[:, None] == basin_ids[None, :]
    partial_sums = jnp.sum(jnp.where(member[None], column_local.reshape(4, -1)[:, :, None], 0.0), axis=1)
    beside_ids = jnp.concatenate([from_low[4, :, 0, 0], from_high[4, :, 0, 0]]).astype(jnp.int32)
    beside_member = beside_ids[:, None] == basin_ids[None, :]
    beside_terms = jnp.concatenate([to_low, to_high], axis=1)
    beside_sums = jnp.sum(jnp.where(beside_member[None], beside_terms[:, :, None], 0.0), axis=1)
    partial_sums = partial_sums + jnp.pad(beside_sums, ((0, 1), (0, 0)))
    basin_sums = partial_sums
    if count != 4:
        basin_residual = tree_sum(tree_sum(basin_sums, "gx"), "gy")
    else:
        even = lax.axis_index("gy") % 2 == 0
        first_out = jnp.pad(jnp.where(even, to_high, to_low), ((0, 1), (0, 0)))
        second_out = jnp.pad(jnp.where(even, to_low, to_high), ((0, 1), (0, 0)))
        received = []
        for edge_out, pairs in (
            (first_out, [(0, 1), (1, 0), (2, 3), (3, 2)]),
            (second_out, [(1, 2), (2, 1), (3, 0), (0, 3)]),
        ):
            got = lax.ppermute(jnp.concatenate([basin_sums, edge_out], axis=1), "gy", pairs)
            basin_sums = basin_sums + got[:, :basin_count]
            received.append(got[:, basin_count:])
        basin_residual = tree_sum(basin_sums, "gx")
        first_term = jnp.where(even, received[1], received[0])
        last_term = jnp.where(even, received[0], received[1])
        middle = jnp.zeros((4, row_count, y_cells - 2), jnp.float32)
        column_residual = column_local + jnp.concatenate(
            [first_term[:, :, None], middle, last_term[:, :, None]], axis=2
        )
    return (smoothed, column_residual, basin_residual)


def solution(mesh):
    return jax.shard_map(
        local,
        mesh=mesh,
        in_specs=(
            P(None, "gx", "gy"),
            P(None, "gx", "gy"),
            P("gx", "gy"),
            P(None, "gx", "gy"),
            P("gx", "gy"),
            P("gx", "gy"),
            P("gx", "gy"),
        ),
        out_specs=(P(None, "gx", "gy"), P(None, "gx", "gy"), P()),
        check_vma=False,
    )
```

```python
import jax
import jax.numpy as jnp
from jax import lax
from jax.sharding import PartitionSpec as P

LAYERS = 80


coupling = 0.25


def neighbour_shift(block, axis, dim, width):
    count = lax.axis_size(axis)
    forward = [(i, i + 1) for i in range(count - 1)]
    backward = [(target, source) for source, target in forward]
    low = lax.ppermute(lax.slice_in_dim(block, block.shape[dim] - width, None, axis=dim), axis, forward)
    high = lax.ppermute(lax.slice_in_dim(block, 0, width, axis=dim), axis, backward)
    return low, high


def vertical_pair(grid_view, frozen):
    lower_cells = jnp.concatenate(
        [grid_view[..., :1] * (1.0 - frozen)[None, :, :, None], grid_view[..., :-1]], axis=-1
    )
    upper_cells = jnp.concatenate([grid_view[..., 1:], jnp.zeros_like(grid_view[..., :1])], axis=-1)
    return lower_cells + upper_cells


def neighbour_terms(grid_view, x_low, x_high, y_low, y_high, viscosity, frozen):
    shape = grid_view.shape
    y_pad = jnp.concatenate([y_low, grid_view, y_high], axis=2)
    if x_low is None:
        along_line = 2.0 * grid_view
    else:
        x_pad = jnp.concatenate([x_low, grid_view, x_high], axis=1)
        along_line = 2.0 * grid_view - x_pad[:, :-2] - x_pad[:, 2:]
    across_line = y_pad[:, :, :-2] + y_pad[:, :, 2:] + vertical_pair(grid_view, frozen)
    flat = (3, shape[1], shape[2] * shape[3])
    return viscosity * along_line.reshape(flat) - coupling * viscosity * across_line.reshape(flat)


def in_cell_terms(masked, matrix):
    return jnp.sum(matrix * masked[None], axis=1)


def gather_rows(block, axis):
    count, mine = (lax.axis_size(axis), lax.axis_index(axis))
    if count > 8:
        return lax.all_gather(block, axis, axis=1, tiled=True)
    pieces = [block]
    for step in range(1, count):
        pairs = [((i + step) % count, i) for i in range(count)]
        pieces.append(lax.ppermute(block, axis, pairs))
    stacked = jnp.stack(pieces + pieces, axis=0)
    ordered = lax.dynamic_slice_in_dim(stacked, count - mine, count, axis=0)
    ordered = jnp.moveaxis(ordered, 0, 1)
    return ordered.reshape(block.shape[0], count * block.shape[1], *block.shape[2:])


def line_solve(line_lead, line_off, line_rhs):
    rows = line_lead.shape[1]
    gain_prev = jnp.zeros_like(line_rhs[:, 0])
    value_prev = jnp.zeros_like(line_rhs[:, 0])
    gains, values = [], []
    for cell_idx in range(rows):
        off_cell = line_off[:, cell_idx]
        pivot = line_lead[:, cell_idx] - off_cell * gain_prev
        gain_prev = off_cell / pivot
        value_prev = (line_rhs[:, cell_idx] + off_cell * value_prev) / pivot
        gains.append(gain_prev)
        values.append(value_prev)
    next_value = jnp.zeros_like(line_rhs[:, 0])
    corrections = list(values)
    for cell_idx in reversed(range(rows)):
        next_value = values[cell_idx] + gains[cell_idx] * next_value
        corrections[cell_idx] = next_value
    return jnp.stack(corrections, axis=1)


def line_solve_scan(line_lead, line_off, line_rhs):
    def sweep_down(carried, cell_cols):
        gain_prev, value_prev = carried
        lead_cell, off_cell, rhs_cell = cell_cols
        pivot = lead_cell - off_cell * gain_prev
        gain = off_cell / pivot
        value = (rhs_cell + off_cell * value_prev) / pivot
        return (gain, value), (gain, value)

    zeros_line = jnp.zeros_like(line_rhs[:, 0])
    scanned = (jnp.moveaxis(line_lead, 1, 0), jnp.moveaxis(line_off, 1, 0), jnp.moveaxis(line_rhs, 1, 0))
    _, (gains, values) = lax.scan(sweep_down, (zeros_line, zeros_line), scanned)

    def sweep_up(next_value, cell_cols):
        gain, value = cell_cols
        solved = value + gain * next_value
        return solved, solved

    _, corrections = lax.scan(sweep_up, zeros_line, (gains, values), reverse=True)
    return jnp.moveaxis(corrections, 0, 1)


def tree_sum(value, axis):
    count = lax.axis_size(axis)
    if count & (count - 1):
        return lax.psum(value, axis)
    step = count // 2
    while step >= 1:
        value = value + lax.ppermute(value, axis, [(i, i ^ step) for i in range(count)])
        step //= 2
    return value


def local(solution, forcing, viscosity, blocks, layer_count, bed_frozen, basin_map):
    row_count = solution.shape[1]
    lane_count = solution.shape[2]
    y_cells = lane_count // LAYERS
    layer_idx = jnp.arange(LAYERS, dtype=jnp.int32)
    active = (
        (layer_idx[None, None, :] < layer_count[:, :, None])
        .astype(jnp.float32)
        .reshape(row_count, lane_count)
    )
    frozen = bed_frozen.astype(jnp.float32)
    matrix = blocks.reshape(4, 4, row_count, lane_count)
    grid = (3, row_count, y_cells, LAYERS)

    masked = solution * active[None]
    masked_grid = masked[:3].reshape(grid)
    weight_grid = (coupling * viscosity * active).reshape(1, row_count, y_cells, LAYERS)
    basin_grid = jnp.broadcast_to(
        basin_map.astype(jnp.float32)[None, :, :, None], (1, row_count, y_cells, LAYERS)
    )
    halo_source = jnp.concatenate([masked_grid, weight_grid, basin_grid], axis=0)
    from_low, from_high = neighbour_shift(halo_source, "gy", 2, 1)
    y_low, y_high = from_low[:3], from_high[:3]
    in_cell = in_cell_terms(masked, matrix)
    moving = in_cell[:3] + neighbour_terms(masked_grid, None, None, y_low, y_high, viscosity, frozen)
    residual = active[None] * (forcing - jnp.concatenate([moving, in_cell[3:]], axis=0))

    diagonal = jnp.stack([matrix[0, 0], matrix[1, 1], matrix[2, 2]])
    line_lead = jnp.where(active[None] > 0.0, diagonal + 2.0 * viscosity[None], 1.0)
    line_off = (viscosity * active)[None]
    packed = jnp.concatenate([line_lead, line_off, residual[:3], masked[:3]], axis=0)
    whole = gather_rows(packed, "gx")
    all_rows = whole.shape[1]
    whole_off = whole[3:4]
    padded_masked = jnp.pad(whole[7:10], ((0, 0), (1, 1), (0, 0)))
    whole_rhs = whole[4:7] + whole_off * (padded_masked[:, :-2] + padded_masked[:, 2:])
    solver = line_solve if all_rows <= 32 else line_solve_scan
    whole_corr = solver(whole[0:3], jnp.broadcast_to(whole_off, whole_rhs.shape), whole_rhs)

    first = lax.axis_index("gx") * row_count
    padded_corr = jnp.pad(whole_corr, ((0, 0), (1, 1), (0, 0)))
    near_corr = lax.dynamic_slice_in_dim(padded_corr, first, row_count + 2, axis=1)
    near_masked = lax.dynamic_slice_in_dim(padded_masked, first, row_count + 2, axis=1)
    correction = near_corr[:, 1:-1]

    pressure_in = residual[3] - (
        matrix[3, 0] * correction[0] + matrix[3, 1] * correction[1] + matrix[3, 2] * correction[2]
    )
    pressure_step = active * pressure_in / viscosity
    full_step = jnp.concatenate([correction, pressure_step[None]], axis=0)
    smoothed = solution + full_step

    smoothed_masked = smoothed * active[None]
    sm_grid = smoothed_masked[:3].reshape(grid)
    edge = (3, 1, y_cells, LAYERS)
    x_low2 = (near_masked[:, :1] + near_corr[:, :1]).reshape(edge)
    x_high2 = (near_masked[:, -1:] + near_corr[:, -1:]).reshape(edge)
    no_cols = jnp.zeros((3, row_count, 1, LAYERS), jnp.float32)
    in_cell2 = in_cell_terms(smoothed_masked, matrix)
    moving2 = in_cell2[:3] + neighbour_terms(sm_grid, x_low2, x_high2, no_cols, no_cols, viscosity, frozen)
    post = active[None] * (forcing - jnp.concatenate([moving2, in_cell2[3:]], axis=0))
    column_local = jnp.sum(post.reshape(4, row_count, y_cells, LAYERS), axis=-1)

    to_low = jnp.sum(from_low[3:4, :, 0] * sm_grid[:, :, 0], axis=-1)
    to_high = jnp.sum(from_high[3:4, :, 0] * sm_grid[:, :, -1], axis=-1)
    edge_terms = jnp.zeros((3, row_count, y_cells), jnp.float32)
    count = lax.axis_size("gy")
    if count != 4:
        forward = [(i, i + 1) for i in range(count - 1)]
        backward = [(target, source) for source, target in forward]
        for_last = lax.ppermute(to_low, "gy", backward)
        for_first = lax.ppermute(to_high, "gy", forward)
        edge_terms = edge_terms.at[:, :, 0].set(for_first).at[:, :, -1].set(for_last)
        column_residual = column_local + jnp.pad(edge_terms, ((0, 1), (0, 0), (0, 0)))
    basin_count = lax.axis_size("gx") // 2 * lax.axis_size("gy")
    basin_ids = jnp.arange(basin_count, dtype=jnp.int32)
    member = basin_map.reshape(-1)[:, None] == basin_ids[None, :]
    partial_sums = jnp.sum(jnp.where(member[None], column_local.reshape(4, -1)[:, :, None], 0.0), axis=1)
    beside_ids = jnp.concatenate([from_low[4, :, 0, 0], from_high[4, :, 0, 0]]).astype(jnp.int32)
    beside_member = beside_ids[:, None] == basin_ids[None, :]
    beside_terms = jnp.concatenate([to_low, to_high], axis=1)
    beside_sums = jnp.sum(jnp.where(beside_member[None], beside_terms[:, :, None], 0.0), axis=1)
    partial_sums = partial_sums + jnp.pad(beside_sums, ((0, 1), (0, 0)))
    basin_sums = partial_sums
    if count != 4:
        basin_residual = tree_sum(tree_sum(basin_sums, "gx"), "gy")
    else:
        even = lax.axis_index("gy") % 2 == 0
        first_out = jnp.pad(jnp.where(even, to_high, to_low), ((0, 1), (0, 0)))
        second_out = jnp.pad(jnp.where(even, to_low, to_high), ((0, 1), (0, 0)))
        received = []
        for edge_out, pairs in (
            (first_out, [(0, 1), (1, 0), (2, 3), (3, 2)]),
            (second_out, [(1, 2), (2, 1), (3, 0), (0, 3)]),
        ):
            got = lax.ppermute(jnp.concatenate([basin_sums, edge_out], axis=1), "gy", pairs)
            basin_sums = basin_sums + got[:, :basin_count]
            received.append(got[:, basin_count:])
        basin_residual = tree_sum(basin_sums, "gx")
        first_term = jnp.where(even, received[1], received[0])
        last_term = jnp.where(even, received[0], received[1])
        middle = jnp.zeros((4, row_count, y_cells - 2), jnp.float32)
        column_residual = column_local + jnp.concatenate(
            [first_term[:, :, None], middle, last_term[:, :, None]], axis=2
        )
    return (smoothed, column_residual, basin_residual)


def solution(mesh):
    return jax.shard_map(
        local,
        mesh=mesh,
        in_specs=(
            P(None, "gx", "gy"),
            P(None, "gx", "gy"),
            P("gx", "gy"),
            P(None, "gx", "gy"),
            P("gx", "gy"),
            P("gx", "gy"),
            P("gx", "gy"),
        ),
        out_specs=(P(None, "gx", "gy"), P(None, "gx", "gy"), P()),
        check_vma=False,
    )
```

```python
import jax
import jax.numpy as jnp
from jax import lax
from jax.sharding import PartitionSpec as P

LAYERS = 80


coupling = 0.25


def neighbour_shift(block, axis, dim, width):
    count = lax.axis_size(axis)
    forward = [(i, i + 1) for i in range(count - 1)]
    backward = [(target, source) for source, target in forward]
    low = lax.ppermute(lax.slice_in_dim(block, block.shape[dim] - width, None, axis=dim), axis, forward)
    high = lax.ppermute(lax.slice_in_dim(block, 0, width, axis=dim), axis, backward)
    return low, high


def vertical_pair(grid_view, frozen):
    lower_cells = jnp.concatenate(
        [grid_view[..., :1] * (1.0 - frozen)[None, :, :, None], grid_view[..., :-1]], axis=-1
    )
    upper_cells = jnp.concatenate([grid_view[..., 1:], jnp.zeros_like(grid_view[..., :1])], axis=-1)
    return lower_cells + upper_cells


def neighbour_terms(grid_view, x_low, x_high, y_low, y_high, viscosity, frozen):
    shape = grid_view.shape
    y_pad = jnp.concatenate([y_low, grid_view, y_high], axis=2)
    if x_low is None:
        along_line = 2.0 * grid_view
    else:
        x_pad = jnp.concatenate([x_low, grid_view, x_high], axis=1)
        along_line = 2.0 * grid_view - x_pad[:, :-2] - x_pad[:, 2:]
    across_line = y_pad[:, :, :-2] + y_pad[:, :, 2:] + vertical_pair(grid_view, frozen)
    flat = (3, shape[1], shape[2] * shape[3])
    return viscosity * along_line.reshape(flat) - coupling * viscosity * across_line.reshape(flat)


def in_cell_terms(masked, matrix):
    return jnp.sum(matrix * masked[None], axis=1)


def gather_rows(block, axis):
    count, mine = (lax.axis_size(axis), lax.axis_index(axis))
    if count > 8:
        return lax.all_gather(block, axis, axis=1, tiled=True)
    pieces = [block]
    for step in range(1, count):
        pairs = [((i + step) % count, i) for i in range(count)]
        pieces.append(lax.ppermute(block, axis, pairs))
    stacked = jnp.stack(pieces + pieces, axis=0)
    ordered = lax.dynamic_slice_in_dim(stacked, count - mine, count, axis=0)
    ordered = jnp.moveaxis(ordered, 0, 1)
    return ordered.reshape(block.shape[0], count * block.shape[1], *block.shape[2:])


def line_solve(line_lead, line_off, line_rhs):
    rows = line_lead.shape[1]
    gain_prev = jnp.zeros_like(line_rhs[:, 0])
    value_prev = jnp.zeros_like(line_rhs[:, 0])
    gains, values = [], []
    for cell_idx in range(rows):
        off_cell = line_off[:, cell_idx]
        pivot = line_lead[:, cell_idx] - off_cell * gain_prev
        gain_prev = off_cell / pivot
        value_prev = (line_rhs[:, cell_idx] + off_cell * value_prev) / pivot
        gains.append(gain_prev)
        values.append(value_prev)
    next_value = jnp.zeros_like(line_rhs[:, 0])
    corrections = list(values)
    for cell_idx in reversed(range(rows)):
        next_value = values[cell_idx] + gains[cell_idx] * next_value
        corrections[cell_idx] = next_value
    return jnp.stack(corrections, axis=1)


def line_solve_scan(line_lead, line_off, line_rhs):
    def sweep_down(carried, cell_cols):
        gain_prev, value_prev = carried
        lead_cell, off_cell, rhs_cell = cell_cols
        pivot = lead_cell - off_cell * gain_prev
        gain = off_cell / pivot
        value = (rhs_cell + off_cell * value_prev) / pivot
        return (gain, value), (gain, value)

    zeros_line = jnp.zeros_like(line_rhs[:, 0])
    scanned = (jnp.moveaxis(line_lead, 1, 0), jnp.moveaxis(line_off, 1, 0), jnp.moveaxis(line_rhs, 1, 0))
    _, (gains, values) = lax.scan(sweep_down, (zeros_line, zeros_line), scanned)

    def sweep_up(next_value, cell_cols):
        gain, value = cell_cols
        solved = value + gain * next_value
        return solved, solved

    _, corrections = lax.scan(sweep_up, zeros_line, (gains, values), reverse=True)
    return jnp.moveaxis(corrections, 0, 1)


def tree_sum(value, axis):
    count = lax.axis_size(axis)
    if count & (count - 1):
        return lax.psum(value, axis)
    step = 1
    while step < count:
        value = value + lax.ppermute(value, axis, [(i, i ^ step) for i in range(count)])
        step *= 2
    return value


def local(solution, forcing, viscosity, blocks, layer_count, bed_frozen, basin_map):
    row_count = solution.shape[1]
    lane_count = solution.shape[2]
    y_cells = lane_count // LAYERS
    layer_idx = jnp.arange(LAYERS, dtype=jnp.int32)
    active = (
        (layer_idx[None, None, :] < layer_count[:, :, None])
        .astype(jnp.float32)
        .reshape(row_count, lane_count)
    )
    frozen = bed_frozen.astype(jnp.float32)
    matrix = blocks.reshape(4, 4, row_count, lane_count)
    grid = (3, row_count, y_cells, LAYERS)

    masked = solution * active[None]
    masked_grid = masked[:3].reshape(grid)
    weight_grid = (coupling * viscosity * active).reshape(1, row_count, y_cells, LAYERS)
    basin_grid = jnp.broadcast_to(
        basin_map.astype(jnp.float32)[None, :, :, None], (1, row_count, y_cells, LAYERS)
    )
    halo_source = jnp.concatenate([masked_grid, weight_grid, basin_grid], axis=0)
    from_low, from_high = neighbour_shift(halo_source, "gy", 2, 1)
    y_low, y_high = from_low[:3], from_high[:3]
    in_cell = in_cell_terms(masked, matrix)
    moving = in_cell[:3] + neighbour_terms(masked_grid, None, None, y_low, y_high, viscosity, frozen)
    residual = active[None] * (forcing - jnp.concatenate([moving, in_cell[3:]], axis=0))

    diagonal = jnp.stack([matrix[0, 0], matrix[1, 1], matrix[2, 2]])
    line_lead = jnp.where(active[None] > 0.0, diagonal + 2.0 * viscosity[None], 1.0)
    line_off = (viscosity * active)[None]
    packed = jnp.concatenate([line_lead, line_off, residual[:3], masked[:3]], axis=0)
    whole = gather_rows(packed, "gx")
    all_rows = whole.shape[1]
    whole_off = whole[3:4]
    padded_masked = jnp.pad(whole[7:10], ((0, 0), (1, 1), (0, 0)))
    whole_rhs = whole[4:7] + whole_off * (padded_masked[:, :-2] + padded_masked[:, 2:])
    solver = line_solve if all_rows <= 32 else line_solve_scan
    whole_corr = solver(whole[0:3], jnp.broadcast_to(whole_off, whole_rhs.shape), whole_rhs)

    first = lax.axis_index("gx") * row_count
    padded_corr = jnp.pad(whole_corr, ((0, 0), (1, 1), (0, 0)))
    near_corr = lax.dynamic_slice_in_dim(padded_corr, first, row_count + 2, axis=1)
    near_masked = lax.dynamic_slice_in_dim(padded_masked, first, row_count + 2, axis=1)
    correction = near_corr[:, 1:-1]

    pressure_in = residual[3] - (
        matrix[3, 0] * correction[0] + matrix[3, 1] * correction[1] + matrix[3, 2] * correction[2]
    )
    pressure_step = active * pressure_in / viscosity
    full_step = jnp.concatenate([correction, pressure_step[None]], axis=0)
    smoothed = solution + full_step

    smoothed_masked = smoothed * active[None]
    sm_grid = smoothed_masked[:3].reshape(grid)
    edge = (3, 1, y_cells, LAYERS)
    x_low2 = (near_masked[:, :1] + near_corr[:, :1]).reshape(edge)
    x_high2 = (near_masked[:, -1:] + near_corr[:, -1:]).reshape(edge)
    no_cols = jnp.zeros((3, row_count, 1, LAYERS), jnp.float32)
    in_cell2 = in_cell_terms(smoothed_masked, matrix)
    moving2 = in_cell2[:3] + neighbour_terms(sm_grid, x_low2, x_high2, no_cols, no_cols, viscosity, frozen)
    post = active[None] * (forcing - jnp.concatenate([moving2, in_cell2[3:]], axis=0))
    column_local = jnp.sum(post.reshape(4, row_count, y_cells, LAYERS), axis=-1)

    to_low = jnp.sum(from_low[3:4, :, 0] * sm_grid[:, :, 0], axis=-1)
    to_high = jnp.sum(from_high[3:4, :, 0] * sm_grid[:, :, -1], axis=-1)
    edge_terms = jnp.zeros((3, row_count, y_cells), jnp.float32)
    count = lax.axis_size("gy")
    if count != 4:
        forward = [(i, i + 1) for i in range(count - 1)]
        backward = [(target, source) for source, target in forward]
        for_last = lax.ppermute(to_low, "gy", backward)
        for_first = lax.ppermute(to_high, "gy", forward)
        edge_terms = edge_terms.at[:, :, 0].set(for_first).at[:, :, -1].set(for_last)
        column_residual = column_local + jnp.pad(edge_terms, ((0, 1), (0, 0), (0, 0)))
    basin_count = lax.axis_size("gx") // 2 * lax.axis_size("gy")
    basin_ids = jnp.arange(basin_count, dtype=jnp.int32)
    basin_float = basin_grid[0, :, :, 0].reshape(-1)
    member = basin_float[:, None] == basin_ids.astype(jnp.float32)[None, :]
    partial_sums = jnp.sum(jnp.where(member[None], column_local.reshape(4, -1)[:, :, None], 0.0), axis=1)
    beside_ids = jnp.concatenate([from_low[4, :, 0, 0], from_high[4, :, 0, 0]]).astype(jnp.int32)
    beside_member = beside_ids[:, None] == basin_ids[None, :]
    beside_terms = jnp.concatenate([to_low, to_high], axis=1)
    beside_sums = jnp.sum(jnp.where(beside_member[None], beside_terms[:, :, None], 0.0), axis=1)
    partial_sums = partial_sums + jnp.pad(beside_sums, ((0, 1), (0, 0)))
    basin_sums = partial_sums
    if count != 4:
        basin_residual = tree_sum(tree_sum(basin_sums, "gx"), "gy")
    else:
        even = lax.axis_index("gy") % 2 == 0
        first_out = jnp.pad(jnp.where(even, to_high, to_low), ((0, 1), (0, 0)))
        second_out = jnp.pad(jnp.where(even, to_low, to_high), ((0, 1), (0, 0)))
        received = []
        for edge_out, pairs in (
            (first_out, [(0, 1), (1, 0), (2, 3), (3, 2)]),
            (second_out, [(1, 2), (2, 1), (3, 0), (0, 3)]),
        ):
            got = lax.ppermute(jnp.concatenate([basin_sums, edge_out], axis=1), "gy", pairs)
            basin_sums = basin_sums + got[:, :basin_count]
            received.append(got[:, basin_count:])
        basin_residual = tree_sum(basin_sums, "gx")
        first_term = jnp.where(even, received[1], received[0])
        last_term = jnp.where(even, received[0], received[1])
        middle = jnp.zeros((4, row_count, y_cells - 2), jnp.float32)
        column_residual = column_local + jnp.concatenate(
            [first_term[:, :, None], middle, last_term[:, :, None]], axis=2
        )
    return (smoothed, column_residual, basin_residual)


def solution(mesh):
    return jax.shard_map(
        local,
        mesh=mesh,
        in_specs=(
            P(None, "gx", "gy"),
            P(None, "gx", "gy"),
            P("gx", "gy"),
            P(None, "gx", "gy"),
            P("gx", "gy"),
            P("gx", "gy"),
            P("gx", "gy"),
        ),
        out_specs=(P(None, "gx", "gy"), P(None, "gx", "gy"), P()),
        check_vma=False,
    )
```
